32 devices in a mesh: req: 8 (over z, x), tp: 4 (over y, core).
Axes of the slice: x: 2, y: 2, z: 4, core: 2. Of those that a mesh axis runs over, the one named last changes fastest.
Arguments:
- hidden_in: bfloat16 [8, 1024, 1024], P('req', 'tp'), may hold values from -6 to 6
- short_cache: bfloat16 [8, 1536, 2, 1024], P('req', None, None, 'tp')
- long_cache: bfloat16 [3, 4096, 2, 1024], P(None, 'req', None, 'tp')
- short_len: int32 [8], P('req'), may hold values from 512 to 1536, as said below
- long_owner: int32 [3], replicated, may hold values from 0 to 7, as said below
- w_qkv: bfloat16 [3, 1024, 1024], P(None, None, 'tp'), may hold values from -0.1875 to 0.1875
- b_qkv: float32 [3, 1024], P(None, 'tp'), may hold values from -3 to 3
- w_out: bfloat16 [1024, 1024], P('tp'), may hold values from -0.1875 to 0.1875
- b_out: float32 [1024], replicated, may hold values from -3 to 3
- w_in: bfloat16 [1024, 4096], P(None, 'tp'), may hold values from -0.1875 to 0.1875
- b_in: float32 [4096], P('tp'), may hold values from -3 to 3
- w_down: bfloat16 [4096, 1024], P('tp'), may hold values from -0.09375 to 0.09375
- b_down: float32 [1024], replicated, may hold values from -3 to 3
- norm_gain: float32 [2, 1024], replicated, may hold values from 0.1 to 1.9
- norm_offset: float32 [2, 1024], replicated, may hold values from -2 to 2
Outputs:
- hidden_out: bfloat16 [8, 1024, 1024], P('req', 'tp')
- new_kv: bfloat16 [8, 1024, 2, 1024], P('req', None, None, 'tp')
The draws below stay inside these ranges and needn't reach their ends.
Inputs may be any that keep to these rules, and one draw needn't show every extreme that they name: `short_len`: some request uses all 1536 positions. `long_owner`: 3 different requests.
All inputs are finite; a program needn't handle non-finite values.
Results may differ from the reference program's by a relative error of at most 0.025.
The reference program's roundings to bfloat16 on the way count: a program that leaves them out, or rounds other values in their place, can miss the bound.
Values may be sent and summed in bfloat16 or wider, within the bound.
No kernel may reach another device: no remote copies, remote signals or barrier semaphores. Data moves between devices by JAX's collectives and lax.ppermute only.
A program may use at most 192 MiB of HBM per device.

```python
import jax
import jax.numpy as jnp
from jax import lax

D = 1024
HEADS = 16
HEAD_DIM = 64
FF = 4096
SPAN = 1024
SHORT_MAX = 1536
NLONG = 3
REQS = 8
LONG_LEN = 4096


def cache_values(key, shape):
    subkeys = jax.random.split(key, 1)
    is_key = (jnp.arange(2) == 0)[:, None]
    base = jax.random.normal(subkeys[0], shape, jnp.float32) * jnp.where(is_key, 2.5, 2.0)
    return base.astype(jnp.bfloat16)


def draw_short_cache(key, part):
    return cache_values(jax.random.fold_in(key, 11), (REQS, SHORT_MAX, 2, D))


def draw_long_cache(key, part):
    return cache_values(jax.random.fold_in(key, 23), (NLONG, LONG_LEN, 2, D))


def draw_short_len(key, part):
    first_key, second_key = jax.random.split(jax.random.fold_in(key, 37))
    lengths = jax.random.randint(first_key, (REQS,), SHORT_MAX // 3, SHORT_MAX + 1)
    chosen = jax.random.randint(second_key, (), 0, REQS)
    return jnp.where(jnp.arange(REQS) == chosen, SHORT_MAX, lengths).astype(jnp.int32)


def draw_long_owner(key, part):
    first_key, second_key = jax.random.split(jax.random.fold_in(key, 41))
    middle = jax.random.randint(first_key, (), 1, REQS - 1).astype(jnp.int32)
    owners = jnp.stack([jnp.zeros((), jnp.int32), jnp.full((), REQS - 1, jnp.int32), middle])
    order = jax.random.permutation(second_key, NLONG)
    return owners[order].astype(jnp.int32)


def shard_levels(key, dims, shards, smallest, largest):
    level, own = 1.0, jax.random.fold_in(key, 6)
    for axis_at, parts in shards:
        heights = jnp.exp(jax.random.uniform(jax.random.fold_in(own, axis_at), (parts,), jnp.float32, smallest / len(shards), largest / len(shards)))
        level = level * jnp.repeat(heights, dims[axis_at] // parts).reshape([-1 if axis == axis_at else 1 for axis in range(len(dims))])
    return level


def gaussian(key, dims, width, most, shards=(), kind=jnp.bfloat16):
    values = jax.random.normal(key, dims, jnp.float32) * width
    if len(shards) > 0:
        values = shard_levels(key, dims, shards, -0.22, 0.18) * values
    return jnp.clip(values, min=-most, max=most).astype(kind)


def setup_inputs(seed: int = 0) -> dict:
    keys = jax.random.split(jax.random.key(seed), 16)
    hidden_in = gaussian(keys[0], (REQS, SPAN, D), 1.0, 6.0, ((0, 8), (1, 4)))
    short_cache = draw_short_cache(jax.random.fold_in(keys[15], 71), 0)
    long_cache = draw_long_cache(jax.random.fold_in(keys[15], 71), 0)
    short_len = draw_short_len(jax.random.fold_in(keys[15], 71), 0)
    long_owner = draw_long_owner(jax.random.fold_in(keys[15], 71), 0)
    w_qkv = gaussian(keys[5], (3, D, D), D ** -0.5, 0.1875, ((2, 4),))
    b_qkv = gaussian(keys[6], (3, D), 0.5, 3.0, ((1, 4),), jnp.float32)
    w_out = gaussian(keys[7], (D, D), D ** -0.5, 0.1875, ((0, 4),))
    b_out = gaussian(keys[8], (D,), 0.5, 3.0, (), jnp.float32)
    w_in = gaussian(keys[9], (D, FF), D ** -0.5, 0.1875, ((1, 4),))
    b_in = gaussian(keys[10], (FF,), 0.5, 3.0, ((0, 4),), jnp.float32)
    w_down = gaussian(keys[11], (FF, D), FF ** -0.5, 0.09375, ((0, 4),))
    b_down = gaussian(keys[12], (D,), 0.5, 3.0, (), jnp.float32)
    norm_gain = jnp.clip(1.0 + 0.18 * jax.random.normal(keys[13], (2, D), jnp.float32), 0.1, 1.9)
    norm_offset = gaussian(keys[14], (2, D), 0.3, 2.0, (), jnp.float32)
    return dict(hidden_in=hidden_in, short_cache=short_cache, long_cache=long_cache, short_len=short_len, long_owner=long_owner, w_qkv=w_qkv, b_qkv=b_qkv, w_out=w_out, b_out=b_out, w_in=w_in, b_in=b_in, w_down=w_down, b_down=b_down, norm_gain=norm_gain, norm_offset=norm_offset)


masked_score = -1e+30

def layer_norm(rows_in, gain, shift):
    center = rows_in - lax.optimization_barrier(jnp.mean(rows_in, axis=-1, keepdims=True))
    spread = lax.optimization_barrier(jnp.mean(center * center, axis=-1, keepdims=True))
    return center * lax.rsqrt(spread + 1e-05) * gain + shift

def attend_head(query, key_matrix, value_matrix, allowed):
    logit_scores = jnp.dot(query, key_matrix.T, preferred_element_type=jnp.float32)
    logit_scores = jnp.where(allowed, logit_scores, masked_score)
    row_peak = lax.optimization_barrier(jnp.max(logit_scores, axis=1, keepdims=True))
    softmax_weights = jnp.where(allowed, jnp.exp(logit_scores - row_peak), 0.0)
    row_total = lax.optimization_barrier(jnp.sum(softmax_weights, axis=1, keepdims=True))
    summed = jnp.dot(softmax_weights.astype(jnp.bfloat16), value_matrix, preferred_element_type=jnp.float32)
    return summed / row_total

def split_heads(matrix):
    return matrix.reshape(matrix.shape[0], HEADS, HEAD_DIM).transpose(1, 0, 2)

def reference(hidden_in, short_cache, long_cache, short_len, long_owner, w_qkv, b_qkv, w_out, b_out, w_in, b_in, w_down, b_down, norm_gain, norm_offset):

    def one_request(request):
        rows_in = hidden_in[request]
        query = ((jnp.dot(rows_in, w_qkv[0], preferred_element_type=jnp.float32) + b_qkv[0]) * 0.125).astype(jnp.bfloat16)
        new_keys = (jnp.dot(rows_in, w_qkv[1], preferred_element_type=jnp.float32) + b_qkv[1]).astype(jnp.bfloat16)
        new_values = (jnp.dot(rows_in, w_qkv[2], preferred_element_type=jnp.float32) + b_qkv[2]).astype(jnp.bfloat16)
        limit = short_len[request]
        owned = long_owner == request
        has_long = jnp.any(owned)
        which_long = jnp.sum(jnp.where(owned, jnp.arange(NLONG, dtype=jnp.int32), 0)).astype(jnp.int32)
        short_rows = short_cache[request]
        causal = jnp.arange(SPAN)[None, :] <= jnp.arange(SPAN)[:, None]
        cache_mask = jnp.broadcast_to((jnp.arange(SHORT_MAX) < limit)[None, :], (SPAN, SHORT_MAX))
        base_mask = jnp.concatenate([cache_mask, causal], axis=1)
        query_heads = split_heads(query)
        base_keys = jnp.concatenate([split_heads(short_rows[:, 0]), split_heads(new_keys)], axis=1)
        base_values = jnp.concatenate([split_heads(short_rows[:, 1]), split_heads(new_values)], axis=1)

        def without_long(unused):
            return lax.map(lambda group: attend_head(group[0], group[1], group[2], base_mask), (query_heads, base_keys, base_values))

        def with_long(unused):
            long_rows = long_cache[which_long]
            all_keys = jnp.concatenate([split_heads(long_rows[:, 0]), base_keys], axis=1)
            all_values = jnp.concatenate([split_heads(long_rows[:, 1]), base_values], axis=1)
            full_mask = jnp.concatenate([jnp.ones((SPAN, LONG_LEN), bool), base_mask], axis=1)
            return lax.map(lambda group: attend_head(group[0], group[1], group[2], full_mask), (query_heads, all_keys, all_values))
        context_heads = lax.cond(has_long, with_long, without_long, 0)
        context = context_heads.transpose(1, 0, 2).reshape(SPAN, D).astype(jnp.bfloat16)
        attended = jnp.dot(context, w_out, preferred_element_type=jnp.float32) + b_out
        normed = layer_norm(rows_in.astype(jnp.float32) + attended, norm_gain[0], norm_offset[0]).astype(jnp.bfloat16)
        units = jax.nn.gelu(jnp.dot(normed, w_in, preferred_element_type=jnp.float32) + b_in, approximate=False).astype(jnp.bfloat16)
        mixed = jnp.dot(units, w_down, preferred_element_type=jnp.float32) + b_down
        hidden_out = layer_norm(normed.astype(jnp.float32) + mixed, norm_gain[1], norm_offset[1]).astype(jnp.bfloat16)
        return (hidden_out, jnp.stack([new_keys, new_values], axis=1))
    results = lax.map(one_request, jnp.arange(REQS, dtype=jnp.int32))
    return (results[0], results[1])
```

```python
import functools

import jax
import jax.numpy as jnp
from jax import lax
from jax.experimental import pallas as pl
from jax.experimental.pallas import tpu as pltpu
from jax.sharding import PartitionSpec as P

HEAD_DIM = 64
masked_score = -1e30
TQ = 512
TK = 512


def layer_norm(rows_in, gain, shift):
    center = rows_in - jnp.mean(rows_in, axis=-1, keepdims=True)
    spread = jnp.mean(center * center, axis=-1, keepdims=True)
    return center * lax.rsqrt(spread + 1e-05) * gain + shift


def _attend_block(q_ref, k_ref, v_ref, m_sc, l_sc, acc_sc, valid):
    width = q_ref.shape[1]
    col = lax.broadcasted_iota(jnp.int32, (q_ref.shape[0], 128), 1)
    low = col < HEAD_DIM
    for pair in range(width // 128):
        cols = slice(pair * 128, (pair + 1) * 128)
        q2 = q_ref[:, cols]
        k2 = k_ref[:, cols]
        v2 = v_ref[:, cols]
        alphas = []
        pvs = []
        for half in range(2):
            h = pair * 2 + half
            qh = jnp.where(low if half == 0 else jnp.logical_not(low), q2, jnp.zeros_like(q2))
            s = lax.dot_general(
                qh, k2, (((1,), (1,)), ((), ())), preferred_element_type=jnp.float32
            )
            if valid is not None:
                s = jnp.where(valid, s, masked_score)
            m_prev = m_sc[h]
            m_new = jnp.maximum(m_prev, jnp.max(s, axis=1, keepdims=True))
            alpha = jnp.exp(m_prev - m_new)
            p = jnp.exp(s - m_new[:, 0:1])
            l_sc[h] = alpha * l_sc[h] + jnp.sum(p, axis=1, keepdims=True)
            m_sc[h] = m_new
            pvs.append(jnp.dot(p.astype(jnp.bfloat16), v2, preferred_element_type=jnp.float32))
            alphas.append(alpha)
        alpha2 = jnp.where(low, alphas[0], alphas[1])
        acc_sc[:, cols] = alpha2 * acc_sc[:, cols] + jnp.where(low, pvs[0], pvs[1])


def _local_kernel(sref, q_ref, k_ref, v_ref, m_out, l_out, acc_out, m_sc, l_sc, acc_sc, *, n_short, nk):
    i = pl.program_id(0)
    j = pl.program_id(1)
    short_len = sref[0]

    @pl.when(j == 0)
    def _():
        m_sc[...] = jnp.full(m_sc.shape, masked_score, jnp.float32)
        l_sc[...] = jnp.zeros(l_sc.shape, jnp.float32)
        acc_sc[...] = jnp.zeros(acc_sc.shape, jnp.float32)

    is_short = j < n_short
    c = j - n_short
    first_row = i * TQ
    full = jnp.where(is_short, (j + 1) * TK <= short_len, c * TK + TK - 1 <= first_row)
    some = jnp.where(is_short, j * TK < short_len, c * TK <= first_row + TQ - 1)

    @pl.when(full)
    def _():
        _attend_block(q_ref, k_ref, v_ref, m_sc, l_sc, acc_sc, None)

    @pl.when(jnp.logical_and(some, jnp.logical_not(full)))
    def _():
        rows = lax.broadcasted_iota(jnp.int32, (TQ, TK), 0) + first_row
        keys = lax.broadcasted_iota(jnp.int32, (TQ, TK), 1)
        bound = jnp.where(is_short, short_len - j * TK, rows - c * TK + 1)
        valid = keys < bound
        _attend_block(q_ref, k_ref, v_ref, m_sc, l_sc, acc_sc, valid)

    @pl.when(j == nk - 1)
    def _():
        m_out[...] = m_sc[...]
        l_out[...] = l_sc[...]
        acc_out[...] = acc_sc[...]


def _long_kernel(sref, q_ref, k_ref, v_ref, m_in, l_in, acc_in, o_ref, m_sc, l_sc, acc_sc, *, nk):
    j = pl.program_id(1)

    @pl.when(j == 0)
    def _():
        m_sc[...] = m_in[...]
        l_sc[...] = l_in[...]
        acc_sc[...] = acc_in[...]

    @pl.when(sref[1] > 0)
    def _():
        _attend_block(q_ref, k_ref, v_ref, m_sc, l_sc, acc_sc, None)

    @pl.when(j == nk - 1)
    def _():
        width = o_ref.shape[1]
        col = lax.broadcasted_iota(jnp.int32, (TQ, 128), 1)
        for pair in range(width // 128):
            cols = slice(pair * 128, (pair + 1) * 128)
            total = jnp.where(col < HEAD_DIM, l_sc[2 * pair], l_sc[2 * pair + 1])
            o_ref[:, cols] = (acc_sc[:, cols] / total).astype(o_ref.dtype)


def local_attention(scalars, q, kv, n_short):
    span, width = q.shape
    heads = width // HEAD_DIM
    nq = span // TQ
    nk = kv.shape[0] // TK

    def kv_block(i, j, s):
        last_short = (s[0] - 1) // TK
        last_new = (i * TQ + TQ - 1) // TK
        return jnp.where(
            j < n_short, jnp.minimum(j, last_short), n_short + jnp.minimum(j - n_short, last_new)
        )

    stat_spec = pl.BlockSpec((heads, TQ, 128), lambda i, j, s: (0, i, 0))
    grid_spec = pltpu.PrefetchScalarGridSpec(
        num_scalar_prefetch=1,
        grid=(nq, nk),
        in_specs=[
            pl.BlockSpec((TQ, width), lambda i, j, s: (i, 0)),
            pl.BlockSpec((TK, width), lambda i, j, s: (kv_block(i, j, s), 0)),
            pl.BlockSpec((TK, width), lambda i, j, s: (kv_block(i, j, s), 1)),
        ],
        out_specs=[stat_spec, stat_spec, pl.BlockSpec((TQ, width), lambda i, j, s: (i, 0))],
        scratch_shapes=[
            pltpu.VMEM((heads, TQ, 128), jnp.float32),
            pltpu.VMEM((heads, TQ, 128), jnp.float32),
            pltpu.VMEM((TQ, width), jnp.float32),
        ],
    )
    return pl.pallas_call(
        functools.partial(_local_kernel, n_short=n_short, nk=nk),
        grid_spec=grid_spec,
        out_shape=[
            jax.ShapeDtypeStruct((heads, span, 128), jnp.float32),
            jax.ShapeDtypeStruct((heads, span, 128), jnp.float32),
            jax.ShapeDtypeStruct((span, width), jnp.float32),
        ],
        compiler_params=pltpu.CompilerParams(dimension_semantics=("arbitrary", "arbitrary")),
    )(scalars, q, kv, kv)


def long_attention(scalars, q, kv, m, l, acc):
    span, width = q.shape
    heads = width // HEAD_DIM
    nq = span // TQ
    nk = kv.shape[0] // TK
    stat_spec = pl.BlockSpec((heads, TQ, 128), lambda i, j, s: (0, i, 0))
    row_spec = pl.BlockSpec((TQ, width), lambda i, j, s: (i, 0))
    grid_spec = pltpu.PrefetchScalarGridSpec(
        num_scalar_prefetch=1,
        grid=(nq, nk),
        in_specs=[
            row_spec,
            pl.BlockSpec((TK, width), lambda i, j, s: (j * s[1], 0)),
            pl.BlockSpec((TK, width), lambda i, j, s: (j * s[1], 1)),
            stat_spec,
            stat_spec,
            row_spec,
        ],
        out_specs=row_spec,
        scratch_shapes=[
            pltpu.VMEM((heads, TQ, 128), jnp.float32),
            pltpu.VMEM((heads, TQ, 128), jnp.float32),
            pltpu.VMEM((TQ, width), jnp.float32),
        ],
    )
    return pl.pallas_call(
        functools.partial(_long_kernel, nk=nk),
        grid_spec=grid_spec,
        out_shape=jax.ShapeDtypeStruct((span, width), jnp.bfloat16),
        compiler_params=pltpu.CompilerParams(dimension_semantics=("arbitrary", "arbitrary")),
    )(scalars, q, kv, kv, m, l, acc)


def solution(mesh):
    n_req = mesh.shape["req"]

    def body(
        hidden_in,
        short_cache,
        long_cache,
        short_len,
        long_owner,
        w_qkv,
        b_qkv,
        w_out,
        b_out,
        w_in,
        b_in,
        w_down,
        b_down,
        norm_gain,
        norm_offset,
    ):
        n_long = long_cache.shape[0]
        long_ids = jnp.arange(n_long, dtype=jnp.int32)

        def which_long(request):
            owned = long_owner == request
            return jnp.sum(jnp.where(owned, long_ids, 0)), jnp.any(owned)

        me = lax.axis_index("req")
        my_long, has_long = which_long(me)
        stripes = [lax.dynamic_index_in_dim(long_cache, my_long, 0, keepdims=False)]
        for shift in range(1, n_req):
            dest_long, unused = which_long((me + shift) % n_req)
            chunk = lax.dynamic_index_in_dim(long_cache, dest_long, 0, keepdims=False)
            stripes.append(
                lax.ppermute(chunk, "req", [(k, (k + shift) % n_req) for k in range(n_req)])
            )
        long_kv = jnp.concatenate(stripes, axis=0)
        long_kv = long_kv.reshape(long_kv.shape[0], -1)

        w_out_full = lax.all_gather(w_out, "tp", axis=0, tiled=True)

        local_rows = hidden_in[0]
        factors = jnp.array([0.125, 1.0, 1.0], jnp.float32)[None, :, None]
        mixed = jnp.einsum(
            "nd,cdk->nck",
            lax.all_gather(local_rows, "tp", axis=0, tiled=True),
            w_qkv,
            preferred_element_type=jnp.float32,
        )
        projected = ((mixed + b_qkv[None]) * factors).astype(jnp.bfloat16)
        span_len = projected.shape[0]
        queries = projected[:, 0]
        new_kv = projected[None, :, 1:3]
        short_rows = short_cache[0]
        cache_len = short_rows.shape[0]
        local_kv = jnp.concatenate(
            [short_rows.reshape(cache_len, -1), projected[:, 1:3].reshape(span_len, -1)], axis=0
        )
        scalars = jnp.stack([short_len[0], has_long.astype(jnp.int32)])
        m, l, acc = local_attention(scalars, queries, local_kv, cache_len // TK)
        context = long_attention(scalars, queries, long_kv, m, l, acc)

        context_rows = lax.all_to_all(context, "tp", 0, 1, tiled=True)
        attended = jnp.dot(context_rows, w_out_full, preferred_element_type=jnp.float32) + b_out
        normed = layer_norm(
            local_rows.astype(jnp.float32) + attended, norm_gain[0], norm_offset[0]
        ).astype(jnp.bfloat16)
        units = jax.nn.gelu(
            jnp.dot(
                lax.all_gather(normed, "tp", axis=0, tiled=True),
                w_in,
                preferred_element_type=jnp.float32,
            )
            + b_in,
            approximate=False,
        ).astype(jnp.bfloat16)
        mixed = (
            lax.psum_scatter(
                jnp.dot(units, w_down, preferred_element_type=jnp.float32),
                "tp",
                scatter_dimension=0,
                tiled=True,
            )
            + b_down
        )
        hidden_out = layer_norm(
            normed.astype(jnp.float32) + mixed, norm_gain[1], norm_offset[1]
        ).astype(jnp.bfloat16)
        return (hidden_out[None], new_kv)

    return jax.shard_map(
        body,
        mesh=mesh,
        in_specs=(
            P("req", "tp", None),
            P("req", None, None, "tp"),
            P(None, "req", None, "tp"),
            P("req"),
            P(),
            P(None, None, "tp"),
            P(None, "tp"),
            P("tp", None),
            P(),
            P(None, "tp"),
            P("tp"),
            P("tp", None),
            P(),
            P(),
            P(),
        ),
        out_specs=(P("req", "tp", None), P("req", None, None, "tp")),
        check_vma=False,
    )
```

```python
import functools

import jax
import jax.numpy as jnp
from jax import lax
from jax.experimental import pallas as pl
from jax.experimental.pallas import tpu as pltpu
from jax.sharding import PartitionSpec as P

HEAD_DIM = 64
masked_score = -1e30
TQ = 512
TK = 512


def layer_norm(rows_in, gain, shift):
    center = rows_in - jnp.mean(rows_in, axis=-1, keepdims=True)
    spread = jnp.mean(center * center, axis=-1, keepdims=True)
    return center * lax.rsqrt(spread + 1e-05) * gain + shift


def _attend_block(q_ref, k_ref, v_ref, m_sc, l_sc, acc_sc, valid):
    width = q_ref.shape[1]
    col = lax.broadcasted_iota(jnp.int32, (q_ref.shape[0], 128), 1)
    low = col < HEAD_DIM
    for pair in range(width // 128):
        cols = slice(pair * 128, (pair + 1) * 128)
        q2 = q_ref[:, cols]
        k2 = k_ref[:, cols]
        v2 = v_ref[:, cols]
        alphas = []
        pvs = []
        for half in range(2):
            h = pair * 2 + half
            qh = jnp.where(low if half == 0 else jnp.logical_not(low), q2, jnp.zeros_like(q2))
            s = lax.dot_general(
                qh, k2, (((1,), (1,)), ((), ())), preferred_element_type=jnp.float32
            )
            if valid is not None:
                s = jnp.where(valid, s, masked_score)
            m_prev = m_sc[h]
            m_new = jnp.maximum(m_prev, jnp.max(s, axis=1, keepdims=True))
            alpha = jnp.exp(m_prev - m_new)
            p = jnp.exp(s - m_new[:, 0:1])
            l_sc[h] = alpha * l_sc[h] + jnp.sum(p, axis=1, keepdims=True)
            m_sc[h] = m_new
            pvs.append(jnp.dot(p.astype(jnp.bfloat16), v2, preferred_element_type=jnp.float32))
            alphas.append(alpha)
        alpha2 = jnp.where(low, alphas[0], alphas[1])
        acc_sc[:, cols] = alpha2 * acc_sc[:, cols] + jnp.where(low, pvs[0], pvs[1])


def _local_kernel(sref, q_ref, k_ref, v_ref, m_out, l_out, acc_out, m_sc, l_sc, acc_sc, *, n_short, nk):
    i = pl.program_id(0)
    j = pl.program_id(1)
    short_len = sref[0]

    @pl.when(j == 0)
    def _():
        m_sc[...] = jnp.full(m_sc.shape, masked_score, jnp.float32)
        l_sc[...] = jnp.zeros(l_sc.shape, jnp.float32)
        acc_sc[...] = jnp.zeros(acc_sc.shape, jnp.float32)

    is_short = j < n_short
    c = j - n_short
    first_row = i * TQ
    full = jnp.where(is_short, (j + 1) * TK <= short_len, c * TK + TK - 1 <= first_row)
    some = jnp.where(is_short, j * TK < short_len, c * TK <= first_row + TQ - 1)

    @pl.when(full)
    def _():
        _attend_block(q_ref, k_ref, v_ref, m_sc, l_sc, acc_sc, None)

    @pl.when(jnp.logical_and(some, jnp.logical_not(full)))
    def _():
        rows = lax.broadcasted_iota(jnp.int32, (TQ, TK), 0) + first_row
        keys = lax.broadcasted_iota(jnp.int32, (TQ, TK), 1)
        bound = jnp.where(is_short, short_len - j * TK, rows - c * TK + 1)
        valid = keys < bound
        _attend_block(q_ref, k_ref, v_ref, m_sc, l_sc, acc_sc, valid)

    @pl.when(j == nk - 1)
    def _():
        m_out[...] = m_sc[...]
        l_out[...] = l_sc[...]
        acc_out[...] = acc_sc[...]


def _long_kernel(sref, q_ref, k_ref, v_ref, m_in, l_in, acc_in, o_ref, m_sc, l_sc, acc_sc, *, nk):
    j = pl.program_id(1)

    @pl.when(j == 0)
    def _():
        m_sc[...] = m_in[...]
        l_sc[...] = l_in[...]
        acc_sc[...] = acc_in[...]

    @pl.when(sref[1] > 0)
    def _():
        _attend_block(q_ref, k_ref, v_ref, m_sc, l_sc, acc_sc, None)

    @pl.when(j == nk - 1)
    def _():
        width = o_ref.shape[1]
        col = lax.broadcasted_iota(jnp.int32, (TQ, 128), 1)
        for pair in range(width // 128):
            cols = slice(pair * 128, (pair + 1) * 128)
            total = jnp.where(col < HEAD_DIM, l_sc[2 * pair], l_sc[2 * pair + 1])
            o_ref[:, cols] = (acc_sc[:, cols] / total).astype(o_ref.dtype)


def _cost(span, keys, width):
    heads = width // HEAD_DIM
    return pl.CostEstimate(
        flops=8 * span * keys * width,
        transcendentals=span * keys * heads,
        bytes_accessed=2 * keys * width * 2 * (span // TQ) + 16 * span * width,
    )


def local_attention(scalars, q, kv, n_short):
    span, width = q.shape
    heads = width // HEAD_DIM
    nq = span // TQ
    nk = kv.shape[0] // TK

    def kv_block(i, j, s):
        last_short = (s[0] - 1) // TK
        last_new = (i * TQ + TQ - 1) // TK
        return jnp.where(
            j < n_short, jnp.minimum(j, last_short), n_short + jnp.minimum(j - n_short, last_new)
        )

    stat_spec = pl.BlockSpec((heads, TQ, 128), lambda i, j, s: (0, i, 0))
    grid_spec = pltpu.PrefetchScalarGridSpec(
        num_scalar_prefetch=1,
        grid=(nq, nk),
        in_specs=[
            pl.BlockSpec((TQ, width), lambda i, j, s: (i, 0)),
            pl.BlockSpec((TK, width), lambda i, j, s: (kv_block(i, j, s), 0)),
            pl.BlockSpec((TK, width), lambda i, j, s: (kv_block(i, j, s), 1)),
        ],
        out_specs=[stat_spec, stat_spec, pl.BlockSpec((TQ, width), lambda i, j, s: (i, 0))],
        scratch_shapes=[
            pltpu.VMEM((heads, TQ, 128), jnp.float32),
            pltpu.VMEM((heads, TQ, 128), jnp.float32),
            pltpu.VMEM((TQ, width), jnp.float32),
        ],
    )
    return pl.pallas_call(
        functools.partial(_local_kernel, n_short=n_short, nk=nk),
        grid_spec=grid_spec,
        out_shape=[
            jax.ShapeDtypeStruct((heads, span, 128), jnp.float32),
            jax.ShapeDtypeStruct((heads, span, 128), jnp.float32),
            jax.ShapeDtypeStruct((span, width), jnp.float32),
        ],
        compiler_params=pltpu.CompilerParams(dimension_semantics=("arbitrary", "arbitrary")),
        cost_estimate=_cost(span, kv.shape[0], width),
    )(scalars, q, kv, kv)


def long_attention(scalars, q, kv, m, l, acc):
    span, width = q.shape
    heads = width // HEAD_DIM
    nq = span // TQ
    nk = kv.shape[0] // TK
    stat_spec = pl.BlockSpec((heads, TQ, 128), lambda i, j, s: (0, i, 0))
    row_spec = pl.BlockSpec((TQ, width), lambda i, j, s: (i, 0))
    grid_spec = pltpu.PrefetchScalarGridSpec(
        num_scalar_prefetch=1,
        grid=(nq, nk),
        in_specs=[
            row_spec,
            pl.BlockSpec((TK, width), lambda i, j, s: (j * s[1], 0)),
            pl.BlockSpec((TK, width), lambda i, j, s: (j * s[1], 1)),
            stat_spec,
            stat_spec,
            row_spec,
        ],
        out_specs=row_spec,
        scratch_shapes=[
            pltpu.VMEM((heads, TQ, 128), jnp.float32),
            pltpu.VMEM((heads, TQ, 128), jnp.float32),
            pltpu.VMEM((TQ, width), jnp.float32),
        ],
    )
    return pl.pallas_call(
        functools.partial(_long_kernel, nk=nk),
        grid_spec=grid_spec,
        out_shape=jax.ShapeDtypeStruct((span, width), jnp.bfloat16),
        compiler_params=pltpu.CompilerParams(dimension_semantics=("arbitrary", "arbitrary")),
        cost_estimate=_cost(span, kv.shape[0], width),
    )(scalars, q, kv, kv, m, l, acc)


def solution(mesh):
    n_req = mesh.shape["req"]

    def body(
        hidden_in,
        short_cache,
        long_cache,
        short_len,
        long_owner,
        w_qkv,
        b_qkv,
        w_out,
        b_out,
        w_in,
        b_in,
        w_down,
        b_down,
        norm_gain,
        norm_offset,
    ):
        n_long = long_cache.shape[0]
        long_ids = jnp.arange(n_long, dtype=jnp.int32)

        def which_long(request):
            owned = long_owner == request
            return jnp.sum(jnp.where(owned, long_ids, 0)), jnp.any(owned)

        me = lax.axis_index("req")
        my_long, has_long = which_long(me)
        outgoing = jnp.stack(
            [
                lax.dynamic_index_in_dim(long_cache, which_long(r)[0], 0, keepdims=False)
                for r in range(n_req)
            ]
        )
        long_kv = lax.all_to_all(outgoing, "req", 0, 0, tiled=True)
        long_kv = long_kv.reshape(-1, long_kv.shape[-2] * long_kv.shape[-1])

        w_out_full = lax.all_gather(w_out, "tp", axis=0, tiled=True)

        local_rows = hidden_in[0]
        factors = jnp.array([0.125, 1.0, 1.0], jnp.float32)[None, :, None]
        mixed = jnp.einsum(
            "nd,cdk->nck",
            lax.all_gather(local_rows, "tp", axis=0, tiled=True),
            w_qkv,
            preferred_element_type=jnp.float32,
        )
        projected = ((mixed + b_qkv[None]) * factors).astype(jnp.bfloat16)
        span_len = projected.shape[0]
        queries = projected[:, 0]
        new_kv = projected[None, :, 1:3]
        short_rows = short_cache[0]
        cache_len = short_rows.shape[0]
        local_kv = jnp.concatenate(
            [short_rows.reshape(cache_len, -1), projected[:, 1:3].reshape(span_len, -1)], axis=0
        )
        scalars = jnp.stack([short_len[0], has_long.astype(jnp.int32)])
        m, l, acc = local_attention(scalars, queries, local_kv, cache_len // TK)
        context = long_attention(scalars, queries, long_kv, m, l, acc)

        context_rows = lax.all_to_all(context, "tp", 0, 1, tiled=True)
        attended = jnp.dot(context_rows, w_out_full, preferred_element_type=jnp.float32) + b_out
        normed = layer_norm(
            local_rows.astype(jnp.float32) + attended, norm_gain[0], norm_offset[0]
        ).astype(jnp.bfloat16)
        units = jax.nn.gelu(
            jnp.dot(
                lax.all_gather(normed, "tp", axis=0, tiled=True),
                w_in,
                preferred_element_type=jnp.float32,
            )
            + b_in,
            approximate=False,
        ).astype(jnp.bfloat16)
        mixed = (
            lax.psum_scatter(
                jnp.dot(units, w_down, preferred_element_type=jnp.float32),
                "tp",
                scatter_dimension=0,
                tiled=True,
            )
            + b_down
        )
        hidden_out = layer_norm(
            normed.astype(jnp.float32) + mixed, norm_gain[1], norm_offset[1]
        ).astype(jnp.bfloat16)
        return (hidden_out[None], new_kv)

    return jax.shard_map(
        body,
        mesh=mesh,
        in_specs=(
            P("req", "tp", None),
            P("req", None, None, "tp"),
            P(None, "req", None, "tp"),
            P("req"),
            P(),
            P(None, None, "tp"),
            P(None, "tp"),
            P("tp", None),
            P(),
            P(None, "tp"),
            P("tp"),
            P("tp", None),
            P(),
            P(),
            P(),
        ),
        out_specs=(P("req", "tp", None), P("req", None, None, "tp")),
        check_vma=False,
    )
```

```python
import functools

import jax
import jax.numpy as jnp
from jax import lax
from jax.experimental import pallas as pl
from jax.experimental.pallas import tpu as pltpu
from jax.sharding import PartitionSpec as P

HEAD_DIM = 64
masked_score = -1e30
TQ = 512
TK = 512


def layer_norm(rows_in, gain, shift):
    center = rows_in - jnp.mean(rows_in, axis=-1, keepdims=True)
    spread = jnp.mean(center * center, axis=-1, keepdims=True)
    return center * lax.rsqrt(spread + 1e-05) * gain + shift


def _attend_block(q_ref, k_ref, v_ref, m_sc, l_sc, acc_sc, valid):
    width = q_ref.shape[1]
    col = lax.broadcasted_iota(jnp.int32, (q_ref.shape[0], 128), 1)
    low = col < HEAD_DIM
    for pair in range(width // 128):
        cols = slice(pair * 128, (pair + 1) * 128)
        q2 = q_ref[:, cols]
        k2 = k_ref[:, cols]
        v2 = v_ref[:, cols]
        alphas = []
        pvs = []
        for half in range(2):
            h = pair * 2 + half
            qh = jnp.where(low if half == 0 else jnp.logical_not(low), q2, jnp.zeros_like(q2))
            s = lax.dot_general(
                qh, k2, (((1,), (1,)), ((), ())), preferred_element_type=jnp.float32
            )
            if valid is not None:
                s = jnp.where(valid, s, masked_score)
            m_prev = m_sc[h]
            m_new = jnp.maximum(m_prev, jnp.max(s, axis=1, keepdims=True))
            alpha = jnp.exp(m_prev - m_new)
            p = jnp.exp(s - m_new[:, 0:1])
            l_sc[h] = alpha * l_sc[h] + jnp.sum(p, axis=1, keepdims=True)
            m_sc[h] = m_new
            pvs.append(jnp.dot(p.astype(jnp.bfloat16), v2, preferred_element_type=jnp.float32))
            alphas.append(alpha)
        alpha2 = jnp.where(low, alphas[0], alphas[1])
        acc_sc[:, cols] = alpha2 * acc_sc[:, cols] + jnp.where(low, pvs[0], pvs[1])


def _local_kernel(sref, q_ref, k_ref, v_ref, m_out, l_out, acc_out, m_sc, l_sc, acc_sc, *, n_short, nk):
    i = pl.program_id(0)
    j = pl.program_id(1)
    short_len = sref[0]

    @pl.when(j == 0)
    def _():
        m_sc[...] = jnp.full(m_sc.shape, masked_score, jnp.float32)
        l_sc[...] = jnp.zeros(l_sc.shape, jnp.float32)
        acc_sc[...] = jnp.zeros(acc_sc.shape, jnp.float32)

    is_short = j < n_short
    c = j - n_short
    first_row = i * TQ
    full = jnp.where(is_short, (j + 1) * TK <= short_len, c * TK + TK - 1 <= first_row)
    some = jnp.where(is_short, j * TK < short_len, c * TK <= first_row + TQ - 1)

    @pl.when(full)
    def _():
        _attend_block(q_ref, k_ref, v_ref, m_sc, l_sc, acc_sc, None)

    @pl.when(jnp.logical_and(some, jnp.logical_not(full)))
    def _():
        rows = lax.broadcasted_iota(jnp.int32, (TQ, TK), 0) + first_row
        keys = lax.broadcasted_iota(jnp.int32, (TQ, TK), 1)
        bound = jnp.where(is_short, short_len - j * TK, rows - c * TK + 1)
        valid = keys < bound
        _attend_block(q_ref, k_ref, v_ref, m_sc, l_sc, acc_sc, valid)

    @pl.when(j == nk - 1)
    def _():
        m_out[...] = m_sc[...]
        l_out[...] = l_sc[...]
        acc_out[...] = acc_sc[...]


def _long_kernel(sref, q_ref, k_ref, v_ref, m_in, l_in, acc_in, o_ref, m_sc, l_sc, acc_sc, *, nk):
    j = pl.program_id(1)

    @pl.when(j == 0)
    def _():
        m_sc[...] = m_in[...]
        l_sc[...] = l_in[...]
        acc_sc[...] = acc_in[...]

    @pl.when(sref[1] > 0)
    def _():
        _attend_block(q_ref, k_ref, v_ref, m_sc, l_sc, acc_sc, None)

    @pl.when(j == nk - 1)
    def _():
        width = o_ref.shape[1]
        col = lax.broadcasted_iota(jnp.int32, (TQ, 128), 1)
        for pair in range(width // 128):
            cols = slice(pair * 128, (pair + 1) * 128)
            total = jnp.where(col < HEAD_DIM, l_sc[2 * pair], l_sc[2 * pair + 1])
            o_ref[:, cols] = (acc_sc[:, cols] / total).astype(o_ref.dtype)


def _cost(span, keys, width):
    heads = width // HEAD_DIM
    return pl.CostEstimate(
        flops=8 * span * keys * width,
        transcendentals=span * keys * heads,
        bytes_accessed=2 * keys * width * 2 * (span // TQ) + 16 * span * width,
    )


def local_attention(scalars, q, kv, n_short):
    span, width = q.shape
    heads = width // HEAD_DIM
    nq = span // TQ
    nk = kv.shape[0] // TK

    def kv_block(i, j, s):
        last_short = (s[0] - 1) // TK
        last_new = (i * TQ + TQ - 1) // TK
        return jnp.where(
            j < n_short, jnp.minimum(j, last_short), n_short + jnp.minimum(j - n_short, last_new)
        )

    stat_spec = pl.BlockSpec((heads, TQ, 128), lambda i, j, s: (0, i, 0))
    grid_spec = pltpu.PrefetchScalarGridSpec(
        num_scalar_prefetch=1,
        grid=(nq, nk),
        in_specs=[
            pl.BlockSpec((TQ, width), lambda i, j, s: (i, 0)),
            pl.BlockSpec((TK, width), lambda i, j, s: (kv_block(i, j, s), 0)),
            pl.BlockSpec((TK, width), lambda i, j, s: (kv_block(i, j, s), 1)),
        ],
        out_specs=[stat_spec, stat_spec, pl.BlockSpec((TQ, width), lambda i, j, s: (i, 0))],
        scratch_shapes=[
            pltpu.VMEM((heads, TQ, 128), jnp.float32),
            pltpu.VMEM((heads, TQ, 128), jnp.float32),
            pltpu.VMEM((TQ, width), jnp.float32),
        ],
    )
    return pl.pallas_call(
        functools.partial(_local_kernel, n_short=n_short, nk=nk),
        grid_spec=grid_spec,
        out_shape=[
            jax.ShapeDtypeStruct((heads, span, 128), jnp.float32),
            jax.ShapeDtypeStruct((heads, span, 128), jnp.float32),
            jax.ShapeDtypeStruct((span, width), jnp.float32),
        ],
        compiler_params=pltpu.CompilerParams(dimension_semantics=("arbitrary", "arbitrary")),
        cost_estimate=_cost(span, kv.shape[0], width),
    )(scalars, q, kv, kv)


def long_attention(scalars, q, kv, m, l, acc):
    span, width = q.shape
    heads = width // HEAD_DIM
    nq = span // TQ
    nk = kv.shape[0] // TK
    stat_spec = pl.BlockSpec((heads, TQ, 128), lambda i, j, s: (0, i, 0))
    row_spec = pl.BlockSpec((TQ, width), lambda i, j, s: (i, 0))
    grid_spec = pltpu.PrefetchScalarGridSpec(
        num_scalar_prefetch=1,
        grid=(nq, nk),
        in_specs=[
            row_spec,
            pl.BlockSpec((TK, width), lambda i, j, s: (j * s[1], 0)),
            pl.BlockSpec((TK, width), lambda i, j, s: (j * s[1], 1)),
            stat_spec,
            stat_spec,
            row_spec,
        ],
        out_specs=row_spec,
        scratch_shapes=[
            pltpu.VMEM((heads, TQ, 128), jnp.float32),
            pltpu.VMEM((heads, TQ, 128), jnp.float32),
            pltpu.VMEM((TQ, width), jnp.float32),
        ],
    )
    return pl.pallas_call(
        functools.partial(_long_kernel, nk=nk),
        grid_spec=grid_spec,
        out_shape=jax.ShapeDtypeStruct((span, width), jnp.bfloat16),
        compiler_params=pltpu.CompilerParams(dimension_semantics=("arbitrary", "arbitrary")),
        cost_estimate=_cost(span, kv.shape[0], width),
    )(scalars, q, kv, kv, m, l, acc)


def solution(mesh):
    n_req = mesh.shape["req"]

    def body(
        hidden_in,
        short_cache,
        long_cache,
        short_len,
        long_owner,
        w_qkv,
        b_qkv,
        w_out,
        b_out,
        w_in,
        b_in,
        w_down,
        b_down,
        norm_gain,
        norm_offset,
    ):
        n_long = long_cache.shape[0]
        long_ids = jnp.arange(n_long, dtype=jnp.int32)

        def which_long(request):
            owned = long_owner == request
            return jnp.sum(jnp.where(owned, long_ids, 0)), jnp.any(owned)

        me = lax.axis_index("req")
        my_long, has_long = which_long(me)
        dest_long = jnp.stack([which_long(r)[0] for r in range(n_req)])
        pick = dest_long[:, None, None, None, None] == long_ids[None, :, None, None, None]
        outgoing = jnp.max(
            jnp.where(pick, long_cache[None], jnp.finfo(long_cache.dtype).min), axis=1
        )
        long_kv = lax.all_to_all(outgoing, "req", 0, 0, tiled=True)
        long_kv = long_kv.reshape(-1, long_kv.shape[-2] * long_kv.shape[-1])

        w_out_full = lax.all_gather(w_out, "tp", axis=0, tiled=True)

        local_rows = hidden_in[0]
        factors = jnp.array([0.125, 1.0, 1.0], jnp.float32)[None, :, None]
        mixed = jnp.einsum(
            "nd,cdk->nck",
            lax.all_gather(local_rows, "tp", axis=0, tiled=True),
            w_qkv,
            preferred_element_type=jnp.float32,
        )
        projected = ((mixed + b_qkv[None]) * factors).astype(jnp.bfloat16)
        span_len = projected.shape[0]
        queries = projected[:, 0]
        new_kv = projected[None, :, 1:3]
        short_rows = short_cache[0]
        cache_len = short_rows.shape[0]
        local_kv = jnp.concatenate(
            [short_rows.reshape(cache_len, -1), projected[:, 1:3].reshape(span_len, -1)], axis=0
        )
        scalars = jnp.stack([short_len[0], has_long.astype(jnp.int32)])
        m, l, acc = local_attention(scalars, queries, local_kv, cache_len // TK)
        context = long_attention(scalars, queries, long_kv, m, l, acc)

        context_rows = lax.all_to_all(context, "tp", 0, 1, tiled=True)
        attended = jnp.dot(context_rows, w_out_full, preferred_element_type=jnp.float32) + b_out
        normed = layer_norm(
            local_rows.astype(jnp.float32) + attended, norm_gain[0], norm_offset[0]
        ).astype(jnp.bfloat16)
        units = jax.nn.gelu(
            jnp.dot(
                lax.all_gather(normed, "tp", axis=0, tiled=True),
                w_in,
                preferred_element_type=jnp.float32,
            )
            + b_in,
            approximate=False,
        ).astype(jnp.bfloat16)
        mixed = (
            lax.psum_scatter(
                jnp.dot(units, w_down, preferred_element_type=jnp.float32).astype(jnp.bfloat16),
                "tp",
                scatter_dimension=0,
                tiled=True,
            ).astype(jnp.float32)
            + b_down
        )
        hidden_out = layer_norm(
            normed.astype(jnp.float32) + mixed, norm_gain[1], norm_offset[1]
        ).astype(jnp.bfloat16)
        return (hidden_out[None], new_kv)

    return jax.shard_map(
        body,
        mesh=mesh,
        in_specs=(
            P("req", "tp", None),
            P("req", None, None, "tp"),
            P(None, "req", None, "tp"),
            P("req"),
            P(),
            P(None, None, "tp"),
            P(None, "tp"),
            P("tp", None),
            P(),
            P(None, "tp"),
            P("tp"),
            P("tp", None),
            P(),
            P(),
            P(),
        ),
        out_specs=(P("req", "tp", None), P("req", None, None, "tp")),
        check_vma=False,
    )
```

```python
import functools

import jax
import jax.numpy as jnp
from jax import lax
from jax.experimental import pallas as pl
from jax.experimental.pallas import tpu as pltpu
from jax.sharding import PartitionSpec as P

HEAD_DIM = 64
masked_score = -1e30
TQ = 512
TK = 512


def layer_norm(rows_in, gain, shift):
    center = rows_in - jnp.mean(rows_in, axis=-1, keepdims=True)
    spread = jnp.mean(center * center, axis=-1, keepdims=True)
    return center * lax.rsqrt(spread + 1e-05) * gain + shift


def _attend_block(q_ref, k_ref, v_ref, m_sc, l_sc, acc_sc, valid):
    width = q_ref.shape[1]
    col = lax.broadcasted_iota(jnp.int32, (q_ref.shape[0], 128), 1)
    low = col < HEAD_DIM
    for pair in range(width // 128):
        cols = slice(pair * 128, (pair + 1) * 128)
        q2 = q_ref[:, cols]
        k2 = k_ref[..., cols].reshape(-1, 128)
        v2 = v_ref[..., cols].reshape(-1, 128)
        alphas = []
        pvs = []
        for half in range(2):
            h = pair * 2 + half
            qh = jnp.where(low if half == 0 else jnp.logical_not(low), q2, jnp.zeros_like(q2))
            s = lax.dot_general(
                qh, k2, (((1,), (1,)), ((), ())), preferred_element_type=jnp.float32
            )
            if valid is not None:
                s = jnp.where(valid, s, masked_score)
            m_prev = m_sc[h]
            m_new = jnp.maximum(m_prev, jnp.max(s, axis=1, keepdims=True))
            alpha = jnp.exp(m_prev - m_new)
            p = jnp.exp(s - m_new[:, 0:1])
            l_sc[h] = alpha * l_sc[h] + jnp.sum(p, axis=1, keepdims=True)
            m_sc[h] = m_new
            pvs.append(jnp.dot(p.astype(jnp.bfloat16), v2, preferred_element_type=jnp.float32))
            alphas.append(alpha)
        alpha2 = jnp.where(low, alphas[0], alphas[1])
        acc_sc[:, cols] = alpha2 * acc_sc[:, cols] + jnp.where(low, pvs[0], pvs[1])


def _local_kernel(sref, q_ref, k_ref, v_ref, m_out, l_out, acc_out, m_sc, l_sc, acc_sc, *, n_short, nk):
    i = pl.program_id(0)
    j = pl.program_id(1)
    short_len = sref[0]

    @pl.when(j == 0)
    def _():
        m_sc[...] = jnp.full(m_sc.shape, masked_score, jnp.float32)
        l_sc[...] = jnp.zeros(l_sc.shape, jnp.float32)
        acc_sc[...] = jnp.zeros(acc_sc.shape, jnp.float32)

    is_short = j < n_short
    c = j - n_short
    first_row = i * TQ
    full = jnp.where(is_short, (j + 1) * TK <= short_len, c * TK + TK - 1 <= first_row)
    some = jnp.where(is_short, j * TK < short_len, c * TK <= first_row + TQ - 1)

    @pl.when(full)
    def _():
        _attend_block(q_ref, k_ref, v_ref, m_sc, l_sc, acc_sc, None)

    @pl.when(jnp.logical_and(some, jnp.logical_not(full)))
    def _():
        rows = lax.broadcasted_iota(jnp.int32, (TQ, TK), 0) + first_row
        keys = lax.broadcasted_iota(jnp.int32, (TQ, TK), 1)
        bound = jnp.where(is_short, short_len - j * TK, rows - c * TK + 1)
        valid = keys < bound
        _attend_block(q_ref, k_ref, v_ref, m_sc, l_sc, acc_sc, valid)

    @pl.when(j == nk - 1)
    def _():
        m_out[...] = m_sc[...]
        l_out[...] = l_sc[...]
        acc_out[...] = acc_sc[...]


def _long_kernel(sref, q_ref, k_ref, v_ref, m_in, l_in, acc_in, *rest, nk, finalize):
    j = pl.program_id(1)
    if finalize:
        o_ref, m_sc, l_sc, acc_sc = rest
    else:
        m_out, l_out, acc_out, m_sc, l_sc, acc_sc = rest

    @pl.when(j == 0)
    def _():
        m_sc[...] = m_in[...]
        l_sc[...] = l_in[...]
        acc_sc[...] = acc_in[...]

    @pl.when(sref[1] > 0)
    def _():
        _attend_block(q_ref, k_ref, v_ref, m_sc, l_sc, acc_sc, None)

    @pl.when(j == nk - 1)
    def _():
        if finalize:
            width = o_ref.shape[1]
            col = lax.broadcasted_iota(jnp.int32, (TQ, 128), 1)
            for pair in range(width // 128):
                cols = slice(pair * 128, (pair + 1) * 128)
                total = jnp.where(col < HEAD_DIM, l_sc[2 * pair], l_sc[2 * pair + 1])
                o_ref[:, cols] = (acc_sc[:, cols] / total).astype(o_ref.dtype)
        else:
            m_out[...] = m_sc[...]
            l_out[...] = l_sc[...]
            acc_out[...] = acc_sc[...]


def _cost(span, keys, width):
    heads = width // HEAD_DIM
    return pl.CostEstimate(
        flops=8 * span * keys * width,
        transcendentals=span * keys * heads,
        bytes_accessed=2 * keys * width * 2 * (span // TQ) + 16 * span * width,
    )


def local_attention(scalars, q, kv, n_short):
    span, width = q.shape
    heads = width // HEAD_DIM
    nq = span // TQ
    nk = kv.shape[0] // TK

    def kv_block(i, j, s):
        last_short = (s[0] - 1) // TK
        last_new = (i * TQ + TQ - 1) // TK
        return jnp.where(
            j < n_short, jnp.minimum(j, last_short), n_short + jnp.minimum(j - n_short, last_new)
        )

    stat_spec = pl.BlockSpec((heads, TQ, 128), lambda i, j, s: (0, i, 0))
    grid_spec = pltpu.PrefetchScalarGridSpec(
        num_scalar_prefetch=1,
        grid=(nq, nk),
        in_specs=[
            pl.BlockSpec((TQ, width), lambda i, j, s: (i, 0)),
            pl.BlockSpec((TK, width), lambda i, j, s: (kv_block(i, j, s), 0)),
            pl.BlockSpec((TK, width), lambda i, j, s: (kv_block(i, j, s), 1)),
        ],
        out_specs=[stat_spec, stat_spec, pl.BlockSpec((TQ, width), lambda i, j, s: (i, 0))],
        scratch_shapes=[
            pltpu.VMEM((heads, TQ, 128), jnp.float32),
            pltpu.VMEM((heads, TQ, 128), jnp.float32),
            pltpu.VMEM((TQ, width), jnp.float32),
        ],
    )
    return pl.pallas_call(
        functools.partial(_local_kernel, n_short=n_short, nk=nk),
        grid_spec=grid_spec,
        out_shape=[
            jax.ShapeDtypeStruct((heads, span, 128), jnp.float32),
            jax.ShapeDtypeStruct((heads, span, 128), jnp.float32),
            jax.ShapeDtypeStruct((span, width), jnp.float32),
        ],
        compiler_params=pltpu.CompilerParams(dimension_semantics=("arbitrary", "arbitrary")),
        cost_estimate=_cost(span, kv.shape[0], width),
    )(scalars, q, kv, kv)


def long_attention(scalars, q, kv, m, l, acc, finalize):
    span, width = q.shape
    heads = width // HEAD_DIM
    nq = span // TQ
    group = max(1, TK // kv.shape[2])
    nk = kv.shape[0] // group
    stat_spec = pl.BlockSpec((heads, TQ, 128), lambda i, j, s: (0, i, 0))
    row_spec = pl.BlockSpec((TQ, width), lambda i, j, s: (i, 0))
    kv_shape = (group, None, kv.shape[2], width)
    if finalize:
        out_specs = row_spec
        out_shape = jax.ShapeDtypeStruct((span, width), jnp.bfloat16)
    else:
        out_specs = [stat_spec, stat_spec, row_spec]
        out_shape = [
            jax.ShapeDtypeStruct((heads, span, 128), jnp.float32),
            jax.ShapeDtypeStruct((heads, span, 128), jnp.float32),
            jax.ShapeDtypeStruct((span, width), jnp.float32),
        ]
    grid_spec = pltpu.PrefetchScalarGridSpec(
        num_scalar_prefetch=1,
        grid=(nq, nk),
        in_specs=[
            row_spec,
            pl.BlockSpec(kv_shape, lambda i, j, s: (j * s[1], 0, 0, 0)),
            pl.BlockSpec(kv_shape, lambda i, j, s: (j * s[1], 1, 0, 0)),
            stat_spec,
            stat_spec,
            row_spec,
        ],
        out_specs=out_specs,
        scratch_shapes=[
            pltpu.VMEM((heads, TQ, 128), jnp.float32),
            pltpu.VMEM((heads, TQ, 128), jnp.float32),
            pltpu.VMEM((TQ, width), jnp.float32),
        ],
    )
    return pl.pallas_call(
        functools.partial(_long_kernel, nk=nk, finalize=finalize),
        grid_spec=grid_spec,
        out_shape=out_shape,
        compiler_params=pltpu.CompilerParams(dimension_semantics=("arbitrary", "arbitrary")),
        cost_estimate=_cost(span, kv.shape[0] * kv.shape[2], width),
    )(scalars, q, kv, kv, m, l, acc)


def solution(mesh):
    n_req = mesh.shape["req"]

    def body(
        hidden_in,
        short_cache,
        long_cache,
        short_len,
        long_owner,
        w_qkv,
        b_qkv,
        w_out,
        b_out,
        w_in,
        b_in,
        w_down,
        b_down,
        norm_gain,
        norm_offset,
    ):
        n_long = long_cache.shape[0]
        long_ids = jnp.arange(n_long, dtype=jnp.int32)

        def which_long(request):
            owned = long_owner == request
            return jnp.sum(jnp.where(owned, long_ids, 0)), jnp.any(owned)

        me = lax.axis_index("req")
        my_long, has_long = which_long(me)
        requests = jnp.arange(n_req, dtype=jnp.int32)
        pick = long_owner[None, :] == requests[:, None]
        dest_long = jnp.sum(jnp.where(pick, long_ids[None, :], 0), axis=1)
        chosen = dest_long[:, None, None, None, None] == long_ids[None, :, None, None, None]
        by_kind = jnp.swapaxes(long_cache, 1, 2)[None]
        outgoing = jnp.max(jnp.where(chosen, by_kind, jnp.finfo(long_cache.dtype).min), axis=1)
        split = outgoing.shape[2] * 3 // 4
        first_part = lax.all_to_all(outgoing[:, :, :split], "req", 0, 0, tiled=True)

        w_out_full = lax.all_gather(w_out, "tp", axis=0, tiled=True)

        local_rows = hidden_in[0]
        factors = jnp.array([0.125, 1.0, 1.0], jnp.float32)[None, :, None]
        mixed = jnp.einsum(
            "nd,cdk->nck",
            lax.all_gather(local_rows, "tp", axis=0, tiled=True),
            w_qkv,
            preferred_element_type=jnp.float32,
        )
        projected = ((mixed + b_qkv[None]) * factors).astype(jnp.bfloat16)
        span_len = projected.shape[0]
        queries = projected[:, 0]
        new_kv = projected[None, :, 1:3]
        short_rows = short_cache[0]
        cache_len = short_rows.shape[0]
        local_kv = jnp.concatenate(
            [short_rows.reshape(cache_len, -1), projected[:, 1:3].reshape(span_len, -1)], axis=0
        )
        scalars = jnp.stack([short_len[0], has_long.astype(jnp.int32)])
        m, l, acc = local_attention(scalars, queries, local_kv, cache_len // TK)
        rest, m = lax.optimization_barrier((outgoing[:, :, split:], m))
        second_part = lax.all_to_all(rest, "req", 0, 0, tiled=True)
        m, l, acc = long_attention(scalars, queries, first_part, m, l, acc, False)
        context = long_attention(scalars, queries, second_part, m, l, acc, True)

        context_rows = lax.all_to_all(context, "tp", 0, 1, tiled=True)
        attended = jnp.dot(context_rows, w_out_full, preferred_element_type=jnp.float32) + b_out
        normed = layer_norm(
            local_rows.astype(jnp.float32) + attended, norm_gain[0], norm_offset[0]
        ).astype(jnp.bfloat16)
        units = jax.nn.gelu(
            jnp.dot(
                lax.all_gather(normed, "tp", axis=0, tiled=True),
                w_in,
                preferred_element_type=jnp.float32,
            )
            + b_in,
            approximate=False,
        ).astype(jnp.bfloat16)
        mixed = (
            lax.psum_scatter(
                jnp.dot(units, w_down, preferred_element_type=jnp.float32).astype(jnp.bfloat16),
                "tp",
                scatter_dimension=0,
                tiled=True,
            ).astype(jnp.float32)
            + b_down
        )
        hidden_out = layer_norm(
            normed.astype(jnp.float32) + mixed, norm_gain[1], norm_offset[1]
        ).astype(jnp.bfloat16)
        return (hidden_out[None], new_kv)

    return jax.shard_map(
        body,
        mesh=mesh,
        in_specs=(
            P("req", "tp", None),
            P("req", None, None, "tp"),
            P(None, "req", None, "tp"),
            P("req"),
            P(),
            P(None, None, "tp"),
            P(None, "tp"),
            P("tp", None),
            P(),
            P(None, "tp"),
            P("tp"),
            P("tp", None),
            P(),
            P(),
            P(),
        ),
        out_specs=(P("req", "tp", None), P("req", None, None, "tp")),
        check_vma=False,
    )
```

```python
import functools

import jax
import jax.numpy as jnp
from jax import lax
from jax.experimental import pallas as pl
from jax.experimental.pallas import tpu as pltpu
from jax.sharding import PartitionSpec as P

HEAD_DIM = 64
masked_score = -1e30
TQ = 512
TK = 512


def layer_norm(rows_in, gain, shift):
    center = rows_in - jnp.mean(rows_in, axis=-1, keepdims=True)
    spread = jnp.mean(center * center, axis=-1, keepdims=True)
    return center * lax.rsqrt(spread + 1e-05) * gain + shift


def _attend_block(q_ref, k_ref, v_ref, m_sc, l_sc, acc_sc, valid):
    width = q_ref.shape[1]
    col = lax.broadcasted_iota(jnp.int32, (q_ref.shape[0], 128), 1)
    low = col < HEAD_DIM
    for pair in range(width // 128):
        cols = slice(pair * 128, (pair + 1) * 128)
        q2 = q_ref[:, cols]
        k2 = k_ref[..., cols].reshape(-1, 128)
        v2 = v_ref[..., cols].reshape(-1, 128)
        alphas = []
        pvs = []
        for half in range(2):
            h = pair * 2 + half
            qh = jnp.where(low if half == 0 else jnp.logical_not(low), q2, jnp.zeros_like(q2))
            s = lax.dot_general(
                qh, k2, (((1,), (1,)), ((), ())), preferred_element_type=jnp.float32
            )
            if valid is not None:
                s = jnp.where(valid, s, masked_score)
            m_prev = m_sc[h]
            m_new = jnp.maximum(m_prev, jnp.max(s, axis=1, keepdims=True))
            alpha = jnp.exp(m_prev - m_new)
            p = jnp.exp(s - m_new[:, 0:1])
            l_sc[h] = alpha * l_sc[h] + jnp.sum(p, axis=1, keepdims=True)
            m_sc[h] = m_new
            pvs.append(jnp.dot(p.astype(jnp.bfloat16), v2, preferred_element_type=jnp.float32))
            alphas.append(alpha)
        alpha2 = jnp.where(low, alphas[0], alphas[1])
        acc_sc[:, cols] = alpha2 * acc_sc[:, cols] + jnp.where(low, pvs[0], pvs[1])


def _local_kernel(sref, q_ref, k_ref, v_ref, m_out, l_out, acc_out, m_sc, l_sc, acc_sc, *, n_short, nk):
    i = pl.program_id(0)
    j = pl.program_id(1)
    short_len = sref[0]

    @pl.when(j == 0)
    def _():
        m_sc[...] = jnp.full(m_sc.shape, masked_score, jnp.float32)
        l_sc[...] = jnp.zeros(l_sc.shape, jnp.float32)
        acc_sc[...] = jnp.zeros(acc_sc.shape, jnp.float32)

    is_short = j < n_short
    c = j - n_short
    first_row = i * TQ
    full = jnp.where(is_short, (j + 1) * TK <= short_len, c * TK + TK - 1 <= first_row)
    some = jnp.where(is_short, j * TK < short_len, c * TK <= first_row + TQ - 1)

    @pl.when(full)
    def _():
        _attend_block(q_ref, k_ref, v_ref, m_sc, l_sc, acc_sc, None)

    @pl.when(jnp.logical_and(some, jnp.logical_not(full)))
    def _():
        rows = lax.broadcasted_iota(jnp.int32, (TQ, TK), 0) + first_row
        keys = lax.broadcasted_iota(jnp.int32, (TQ, TK), 1)
        bound = jnp.where(is_short, short_len - j * TK, rows - c * TK + 1)
        valid = keys < bound
        _attend_block(q_ref, k_ref, v_ref, m_sc, l_sc, acc_sc, valid)

    @pl.when(j == nk - 1)
    def _():
        m_out[...] = m_sc[...]
        l_out[...] = l_sc[...]
        acc_out[...] = acc_sc[...]


def _long_kernel(sref, q_ref, k_ref, v_ref, m_in, l_in, acc_in, *rest, nk, finalize):
    j = pl.program_id(1)
    if finalize:
        o_ref, m_sc, l_sc, acc_sc = rest
    else:
        m_out, l_out, acc_out, m_sc, l_sc, acc_sc = rest

    @pl.when(j == 0)
    def _():
        m_sc[...] = m_in[...]
        l_sc[...] = l_in[...]
        acc_sc[...] = acc_in[...]

    @pl.when(sref[1] > 0)
    def _():
        _attend_block(q_ref, k_ref, v_ref, m_sc, l_sc, acc_sc, None)

    @pl.when(j == nk - 1)
    def _():
        if finalize:
            width = o_ref.shape[1]
            col = lax.broadcasted_iota(jnp.int32, (TQ, 128), 1)
            for pair in range(width // 128):
                cols = slice(pair * 128, (pair + 1) * 128)
                total = jnp.where(col < HEAD_DIM, l_sc[2 * pair], l_sc[2 * pair + 1])
                o_ref[:, cols] = (acc_sc[:, cols] / total).astype(o_ref.dtype)
        else:
            m_out[...] = m_sc[...]
            l_out[...] = l_sc[...]
            acc_out[...] = acc_sc[...]


def _cost(span, keys, width):
    heads = width // HEAD_DIM
    return pl.CostEstimate(
        flops=8 * span * keys * width,
        transcendentals=span * keys * heads,
        bytes_accessed=2 * keys * width * 2 * (span // TQ) + 16 * span * width,
    )


def local_attention(scalars, q, kv, n_short):
    span, width = q.shape
    heads = width // HEAD_DIM
    nq = span // TQ
    nk = kv.shape[0] // TK

    def kv_block(i, j, s):
        last_short = (s[0] - 1) // TK
        last_new = (i * TQ + TQ - 1) // TK
        return jnp.where(
            j < n_short, jnp.minimum(j, last_short), n_short + jnp.minimum(j - n_short, last_new)
        )

    stat_spec = pl.BlockSpec((heads, TQ, 128), lambda i, j, s: (0, i, 0))
    grid_spec = pltpu.PrefetchScalarGridSpec(
        num_scalar_prefetch=1,
        grid=(nq, nk),
        in_specs=[
            pl.BlockSpec((TQ, width), lambda i, j, s: (i, 0)),
            pl.BlockSpec((TK, width), lambda i, j, s: (kv_block(i, j, s), 0)),
            pl.BlockSpec((TK, width), lambda i, j, s: (kv_block(i, j, s), 1)),
        ],
        out_specs=[stat_spec, stat_spec, pl.BlockSpec((TQ, width), lambda i, j, s: (i, 0))],
        scratch_shapes=[
            pltpu.VMEM((heads, TQ, 128), jnp.float32),
            pltpu.VMEM((heads, TQ, 128), jnp.float32),
            pltpu.VMEM((TQ, width), jnp.float32),
        ],
    )
    return pl.pallas_call(
        functools.partial(_local_kernel, n_short=n_short, nk=nk),
        grid_spec=grid_spec,
        out_shape=[
            jax.ShapeDtypeStruct((heads, span, 128), jnp.float32),
            jax.ShapeDtypeStruct((heads, span, 128), jnp.float32),
            jax.ShapeDtypeStruct((span, width), jnp.float32),
        ],
        compiler_params=pltpu.CompilerParams(dimension_semantics=("arbitrary", "arbitrary")),
        cost_estimate=_cost(span, kv.shape[0], width),
    )(scalars, q, kv, kv)


def long_attention(scalars, q, kv, m, l, acc, finalize):
    span, width = q.shape
    heads = width // HEAD_DIM
    nq = span // TQ
    group = max(1, TK // kv.shape[2])
    nk = kv.shape[0] // group
    stat_spec = pl.BlockSpec((heads, TQ, 128), lambda i, j, s: (0, i, 0))
    row_spec = pl.BlockSpec((TQ, width), lambda i, j, s: (i, 0))
    kv_shape = (group, None, kv.shape[2], width)
    if finalize:
        out_specs = row_spec
        out_shape = jax.ShapeDtypeStruct((span, width), jnp.bfloat16)
    else:
        out_specs = [stat_spec, stat_spec, row_spec]
        out_shape = [
            jax.ShapeDtypeStruct((heads, span, 128), jnp.float32),
            jax.ShapeDtypeStruct((heads, span, 128), jnp.float32),
            jax.ShapeDtypeStruct((span, width), jnp.float32),
        ]
    grid_spec = pltpu.PrefetchScalarGridSpec(
        num_scalar_prefetch=1,
        grid=(nq, nk),
        in_specs=[
            row_spec,
            pl.BlockSpec(kv_shape, lambda i, j, s: (j * s[1], 0, 0, 0)),
            pl.BlockSpec(kv_shape, lambda i, j, s: (j * s[1], 1, 0, 0)),
            stat_spec,
            stat_spec,
            row_spec,
        ],
        out_specs=out_specs,
        scratch_shapes=[
            pltpu.VMEM((heads, TQ, 128), jnp.float32),
            pltpu.VMEM((heads, TQ, 128), jnp.float32),
            pltpu.VMEM((TQ, width), jnp.float32),
        ],
    )
    return pl.pallas_call(
        functools.partial(_long_kernel, nk=nk, finalize=finalize),
        grid_spec=grid_spec,
        out_shape=out_shape,
        compiler_params=pltpu.CompilerParams(dimension_semantics=("arbitrary", "arbitrary")),
        cost_estimate=_cost(span, kv.shape[0] * kv.shape[2], width),
    )(scalars, q, kv, kv, m, l, acc)


def solution(mesh):
    n_req = mesh.shape["req"]

    def body(
        hidden_in,
        short_cache,
        long_cache,
        short_len,
        long_owner,
        w_qkv,
        b_qkv,
        w_out,
        b_out,
        w_in,
        b_in,
        w_down,
        b_down,
        norm_gain,
        norm_offset,
    ):
        n_long = long_cache.shape[0]
        long_ids = jnp.arange(n_long, dtype=jnp.int32)

        def which_long(request):
            owned = long_owner == request
            return jnp.sum(jnp.where(owned, long_ids, 0)), jnp.any(owned)

        me = lax.axis_index("req")
        my_long, has_long = which_long(me)
        requests = jnp.arange(n_req, dtype=jnp.int32)
        pick = long_owner[None, :] == requests[:, None]
        dest_long = jnp.sum(jnp.where(pick, long_ids[None, :], 0), axis=1)
        chosen = dest_long[:, None, None, None, None] == long_ids[None, :, None, None, None]
        by_kind = jnp.swapaxes(long_cache, 1, 2)[None]
        outgoing = jnp.max(jnp.where(chosen, by_kind, jnp.finfo(long_cache.dtype).min), axis=1)
        split = outgoing.shape[2] * 3 // 4
        first_part = lax.all_to_all(outgoing[:, :, :split], "req", 0, 0, tiled=True)

        w_out_full = lax.all_gather(w_out, "tp", axis=0, tiled=True)

        local_rows = hidden_in[0]
        factors = jnp.array([0.125, 1.0, 1.0], jnp.float32)[None, :, None]
        mixed = jnp.einsum(
            "nd,cdk->nck",
            lax.all_gather(local_rows, "tp", axis=0, tiled=True),
            w_qkv,
            preferred_element_type=jnp.float32,
        )
        projected = ((mixed + b_qkv[None]) * factors).astype(jnp.bfloat16)
        span_len = projected.shape[0]
        queries = projected[:, 0]
        new_kv = projected[None, :, 1:3]
        short_rows = short_cache[0]
        cache_len = short_rows.shape[0]
        local_kv = jnp.concatenate(
            [short_rows.reshape(cache_len, -1), projected[:, 1:3].reshape(span_len, -1)], axis=0
        )
        scalars = jnp.stack([short_len[0], has_long.astype(jnp.int32)])
        m, l, acc = local_attention(scalars, queries, local_kv, cache_len // TK)
        rest, m = lax.optimization_barrier((outgoing[:, :, split:], m))
        second_part = lax.all_to_all(rest, "req", 0, 0, tiled=True)
        m, l, acc = long_attention(scalars, queries, first_part, m, l, acc, False)
        context = long_attention(scalars, queries, second_part, m, l, acc, True)

        context_rows = lax.all_to_all(context, "tp", 0, 1, tiled=True)
        attended = jnp.dot(context_rows, w_out_full, preferred_element_type=jnp.float32) + b_out
        normed = layer_norm(
            local_rows.astype(jnp.float32) + attended, norm_gain[0], norm_offset[0]
        ).astype(jnp.bfloat16)
        n_tp = mesh.shape["tp"]
        sibling = [(k, k ^ 1) for k in range(n_tp)]
        halves_in = (w_in, lax.ppermute(w_in, "tp", sibling))
        halves_b = (b_in, lax.ppermute(b_in, "tp", sibling))
        halves_down = (w_down, lax.ppermute(w_down, "tp", sibling))

        def ffn_part(rows):
            total = None
            for w_a, b_a, w_b in zip(halves_in, halves_b, halves_down):
                units = jax.nn.gelu(
                    jnp.dot(rows, w_a, preferred_element_type=jnp.float32) + b_a,
                    approximate=False,
                ).astype(jnp.bfloat16)
                part = jnp.dot(units, w_b, preferred_element_type=jnp.float32)
                total = part if total is None else total + part
            return total

        own_rows = normed
        returned = []
        for step in range(1, n_tp // 2):
            ahead = [(k, (k + 2 * step) % n_tp) for k in range(n_tp)]
            behind = [(b, a) for a, b in ahead]
            peer_part = ffn_part(lax.ppermute(normed, "tp", ahead))
            own_rows, peer_part = lax.optimization_barrier((own_rows, peer_part))
            returned.append(lax.ppermute(peer_part, "tp", behind))
        mixed = ffn_part(own_rows)
        for part in returned:
            mixed = mixed + part
        mixed = mixed + b_down
        hidden_out = layer_norm(
            normed.astype(jnp.float32) + mixed, norm_gain[1], norm_offset[1]
        ).astype(jnp.bfloat16)
        return (hidden_out[None], new_kv)

    return jax.shard_map(
        body,
        mesh=mesh,
        in_specs=(
            P("req", "tp", None),
            P("req", None, None, "tp"),
            P(None, "req", None, "tp"),
            P("req"),
            P(),
            P(None, None, "tp"),
            P(None, "tp"),
            P("tp", None),
            P(),
            P(None, "tp"),
            P("tp"),
            P("tp", None),
            P(),
            P(),
            P(),
        ),
        out_specs=(P("req", "tp", None), P("req", None, None, "tp")),
        check_vma=False,
    )
```

```python
import functools

import jax
import jax.numpy as jnp
from jax import lax
from jax.experimental import pallas as pl
from jax.experimental.pallas import tpu as pltpu
from jax.sharding import PartitionSpec as P

HEAD_DIM = 64
masked_score = -1e30
TQ = 512
TK = 512


def layer_norm(rows_in, gain, shift):
    center = rows_in - jnp.mean(rows_in, axis=-1, keepdims=True)
    spread = jnp.mean(center * center, axis=-1, keepdims=True)
    return center * lax.rsqrt(spread + 1e-05) * gain + shift


def _attend_block(q_ref, k_ref, v_ref, m_sc, l_sc, acc_sc, valid):
    width = q_ref.shape[1]
    col = lax.broadcasted_iota(jnp.int32, (q_ref.shape[0], 128), 1)
    low = col < HEAD_DIM
    for pair in range(width // 128):
        cols = slice(pair * 128, (pair + 1) * 128)
        q2 = q_ref[:, cols]
        k2 = k_ref[..., cols].reshape(-1, 128)
        v2 = v_ref[..., cols].reshape(-1, 128)
        alphas = []
        pvs = []
        for half in range(2):
            h = pair * 2 + half
            qh = jnp.where(low if half == 0 else jnp.logical_not(low), q2, jnp.zeros_like(q2))
            s = lax.dot_general(
                qh, k2, (((1,), (1,)), ((), ())), preferred_element_type=jnp.float32
            )
            if valid is not None:
                s = jnp.where(valid, s, masked_score)
            m_prev = m_sc[h]
            m_new = jnp.maximum(m_prev, jnp.max(s, axis=1, keepdims=True))
            alpha = jnp.exp(m_prev - m_new)
            p = jnp.exp(s - m_new[:, 0:1])
            l_sc[h] = alpha * l_sc[h] + jnp.sum(p, axis=1, keepdims=True)
            m_sc[h] = m_new
            pvs.append(jnp.dot(p.astype(jnp.bfloat16), v2, preferred_element_type=jnp.float32))
            alphas.append(alpha)
        alpha2 = jnp.where(low, alphas[0], alphas[1])
        acc_sc[:, cols] = alpha2 * acc_sc[:, cols] + jnp.where(low, pvs[0], pvs[1])


def _local_kernel(sref, q_ref, k_ref, v_ref, m_out, l_out, acc_out, m_sc, l_sc, acc_sc, *, n_short, nk):
    i = pl.program_id(0)
    j = pl.program_id(1)
    short_len = sref[0]

    @pl.when(j == 0)
    def _():
        m_sc[...] = jnp.full(m_sc.shape, masked_score, jnp.float32)
        l_sc[...] = jnp.zeros(l_sc.shape, jnp.float32)
        acc_sc[...] = jnp.zeros(acc_sc.shape, jnp.float32)

    is_short = j < n_short
    c = j - n_short
    first_row = i * TQ
    full = jnp.where(is_short, (j + 1) * TK <= short_len, c * TK + TK - 1 <= first_row)
    some = jnp.where(is_short, j * TK < short_len, c * TK <= first_row + TQ - 1)

    @pl.when(full)
    def _():
        _attend_block(q_ref, k_ref, v_ref, m_sc, l_sc, acc_sc, None)

    @pl.when(jnp.logical_and(some, jnp.logical_not(full)))
    def _():
        rows = lax.broadcasted_iota(jnp.int32, (TQ, TK), 0) + first_row
        keys = lax.broadcasted_iota(jnp.int32, (TQ, TK), 1)
        bound = jnp.where(is_short, short_len - j * TK, rows - c * TK + 1)
        valid = keys < bound
        _attend_block(q_ref, k_ref, v_ref, m_sc, l_sc, acc_sc, valid)

    @pl.when(j == nk - 1)
    def _():
        m_out[...] = m_sc[...]
        l_out[...] = l_sc[...]
        acc_out[...] = acc_sc[...]


def _long_kernel(sref, q_ref, k_ref, v_ref, m_in, l_in, acc_in, *rest, nk, finalize):
    j = pl.program_id(1)
    if finalize:
        o_ref, m_sc, l_sc, acc_sc = rest
    else:
        m_out, l_out, acc_out, m_sc, l_sc, acc_sc = rest

    @pl.when(j == 0)
    def _():
        m_sc[...] = m_in[...]
        l_sc[...] = l_in[...]
        acc_sc[...] = acc_in[...]

    @pl.when(sref[1] > 0)
    def _():
        _attend_block(q_ref, k_ref, v_ref, m_sc, l_sc, acc_sc, None)

    @pl.when(j == nk - 1)
    def _():
        if finalize:
            width = o_ref.shape[1]
            col = lax.broadcasted_iota(jnp.int32, (TQ, 128), 1)
            for pair in range(width // 128):
                cols = slice(pair * 128, (pair + 1) * 128)
                total = jnp.where(col < HEAD_DIM, l_sc[2 * pair], l_sc[2 * pair + 1])
                o_ref[:, cols] = (acc_sc[:, cols] / total).astype(o_ref.dtype)
        else:
            m_out[...] = m_sc[...]
            l_out[...] = l_sc[...]
            acc_out[...] = acc_sc[...]


def _cost(span, keys, width):
    heads = width // HEAD_DIM
    return pl.CostEstimate(
        flops=8 * span * keys * width,
        transcendentals=span * keys * heads,
        bytes_accessed=2 * keys * width * 2 * (span // TQ) + 16 * span * width,
    )


def local_attention(scalars, q, kv, n_short):
    span, width = q.shape
    heads = width // HEAD_DIM
    nq = span // TQ
    nk = kv.shape[0] // TK

    def kv_block(i, j, s):
        last_short = (s[0] - 1) // TK
        last_new = (i * TQ + TQ - 1) // TK
        return jnp.where(
            j < n_short, jnp.minimum(j, last_short), n_short + jnp.minimum(j - n_short, last_new)
        )

    stat_spec = pl.BlockSpec((heads, TQ, 128), lambda i, j, s: (0, i, 0))
    grid_spec = pltpu.PrefetchScalarGridSpec(
        num_scalar_prefetch=1,
        grid=(nq, nk),
        in_specs=[
            pl.BlockSpec((TQ, width), lambda i, j, s: (i, 0)),
            pl.BlockSpec((TK, width), lambda i, j, s: (kv_block(i, j, s), 0)),
            pl.BlockSpec((TK, width), lambda i, j, s: (kv_block(i, j, s), 1)),
        ],
        out_specs=[stat_spec, stat_spec, pl.BlockSpec((TQ, width), lambda i, j, s: (i, 0))],
        scratch_shapes=[
            pltpu.VMEM((heads, TQ, 128), jnp.float32),
            pltpu.VMEM((heads, TQ, 128), jnp.float32),
            pltpu.VMEM((TQ, width), jnp.float32),
        ],
    )
    return pl.pallas_call(
        functools.partial(_local_kernel, n_short=n_short, nk=nk),
        grid_spec=grid_spec,
        out_shape=[
            jax.ShapeDtypeStruct((heads, span, 128), jnp.float32),
            jax.ShapeDtypeStruct((heads, span, 128), jnp.float32),
            jax.ShapeDtypeStruct((span, width), jnp.float32),
        ],
        compiler_params=pltpu.CompilerParams(dimension_semantics=("arbitrary", "arbitrary")),
        cost_estimate=_cost(span, kv.shape[0], width),
    )(scalars, q, kv, kv)


def long_attention(scalars, q, kv, m, l, acc, finalize):
    span, width = q.shape
    heads = width // HEAD_DIM
    nq = span // TQ
    group = -(-TK // kv.shape[2])
    nk = kv.shape[0] // group
    stat_spec = pl.BlockSpec((heads, TQ, 128), lambda i, j, s: (0, i, 0))
    row_spec = pl.BlockSpec((TQ, width), lambda i, j, s: (i, 0))
    kv_shape = (group, None, kv.shape[2], width)
    if finalize:
        out_specs = row_spec
        out_shape = jax.ShapeDtypeStruct((span, width), jnp.bfloat16)
    else:
        out_specs = [stat_spec, stat_spec, row_spec]
        out_shape = [
            jax.ShapeDtypeStruct((heads, span, 128), jnp.float32),
            jax.ShapeDtypeStruct((heads, span, 128), jnp.float32),
            jax.ShapeDtypeStruct((span, width), jnp.float32),
        ]
    grid_spec = pltpu.PrefetchScalarGridSpec(
        num_scalar_prefetch=1,
        grid=(nq, nk),
        in_specs=[
            row_spec,
            pl.BlockSpec(kv_shape, lambda i, j, s: (j * s[1], 0, 0, 0)),
            pl.BlockSpec(kv_shape, lambda i, j, s: (j * s[1], 1, 0, 0)),
            stat_spec,
            stat_spec,
            row_spec,
        ],
        out_specs=out_specs,
        scratch_shapes=[
            pltpu.VMEM((heads, TQ, 128), jnp.float32),
            pltpu.VMEM((heads, TQ, 128), jnp.float32),
            pltpu.VMEM((TQ, width), jnp.float32),
        ],
    )
    return pl.pallas_call(
        functools.partial(_long_kernel, nk=nk, finalize=finalize),
        grid_spec=grid_spec,
        out_shape=out_shape,
        compiler_params=pltpu.CompilerParams(dimension_semantics=("arbitrary", "arbitrary")),
        cost_estimate=_cost(span, kv.shape[0] * kv.shape[2], width),
    )(scalars, q, kv, kv, m, l, acc)


def solution(mesh):
    n_req = mesh.shape["req"]

    def body(
        hidden_in,
        short_cache,
        long_cache,
        short_len,
        long_owner,
        w_qkv,
        b_qkv,
        w_out,
        b_out,
        w_in,
        b_in,
        w_down,
        b_down,
        norm_gain,
        norm_offset,
    ):
        n_long = long_cache.shape[0]
        long_ids = jnp.arange(n_long, dtype=jnp.int32)

        def which_long(request):
            owned = long_owner == request
            return jnp.sum(jnp.where(owned, long_ids, 0)), jnp.any(owned)

        me = lax.axis_index("req")
        my_long, has_long = which_long(me)
        requests = jnp.arange(n_req, dtype=jnp.int32)
        pick = long_owner[None, :] == requests[:, None]
        dest_long = jnp.sum(jnp.where(pick, long_ids[None, :], 0), axis=1)
        chosen = dest_long[:, None, None, None, None] == long_ids[None, :, None, None, None]
        by_kind = jnp.swapaxes(long_cache, 1, 2)[None]
        outgoing = jnp.max(jnp.where(chosen, by_kind, jnp.finfo(long_cache.dtype).min), axis=1)
        split = outgoing.shape[2] * 3 // 4
        first_part = lax.all_to_all(outgoing[:, :, :split], "req", 0, 0, tiled=True)

        w_out_full = lax.all_gather(w_out, "tp", axis=0, tiled=True)

        local_rows = hidden_in[0]
        factors = jnp.array([0.125, 1.0, 1.0], jnp.float32)[None, :, None]
        mixed = jnp.einsum(
            "nd,cdk->nck",
            lax.all_gather(local_rows, "tp", axis=0, tiled=True),
            w_qkv,
            preferred_element_type=jnp.float32,
        )
        projected = ((mixed + b_qkv[None]) * factors).astype(jnp.bfloat16)
        span_len = projected.shape[0]
        queries = projected[:, 0]
        new_kv = projected[None, :, 1:3]
        short_rows = short_cache[0]
        cache_len = short_rows.shape[0]
        local_kv = jnp.concatenate(
            [short_rows.reshape(cache_len, -1), projected[:, 1:3].reshape(span_len, -1)], axis=0
        )
        scalars = jnp.stack([short_len[0], has_long.astype(jnp.int32)])
        m, l, acc = local_attention(scalars, queries, local_kv, cache_len // TK)
        rest, m = lax.optimization_barrier((outgoing[:, :, split:], m))
        second_part = lax.all_to_all(rest, "req", 0, 0, tiled=True)
        m, l, acc = long_attention(scalars, queries, first_part, m, l, acc, False)
        context = long_attention(scalars, queries, second_part, m, l, acc, True)

        context_rows = lax.all_to_all(context, "tp", 0, 1, tiled=True)
        attended = jnp.dot(context_rows, w_out_full, preferred_element_type=jnp.float32) + b_out
        normed = layer_norm(
            local_rows.astype(jnp.float32) + attended, norm_gain[0], norm_offset[0]
        ).astype(jnp.bfloat16)
        n_tp = mesh.shape["tp"]
        sibling = [(k, k ^ 1) for k in range(n_tp)]
        halves_in = (w_in, lax.ppermute(w_in, "tp", sibling))
        halves_b = (b_in, lax.ppermute(b_in, "tp", sibling))
        halves_down = (w_down, lax.ppermute(w_down, "tp", sibling))

        def ffn_part(rows):
            total = None
            for w_a, b_a, w_b in zip(halves_in, halves_b, halves_down):
                units = jax.nn.gelu(
                    jnp.dot(rows, w_a, preferred_element_type=jnp.float32) + b_a,
                    approximate=False,
                ).astype(jnp.bfloat16)
                part = jnp.dot(units, w_b, preferred_element_type=jnp.float32)
                total = part if total is None else total + part
            return total

        own_rows = normed
        returned = []
        for step in range(1, n_tp // 2):
            ahead = [(k, (k + 2 * step) % n_tp) for k in range(n_tp)]
            behind = [(b, a) for a, b in ahead]
            peer_part = ffn_part(lax.ppermute(normed, "tp", ahead))
            own_rows, peer_part = lax.optimization_barrier((own_rows, peer_part))
            returned.append(lax.ppermute(peer_part, "tp", behind))
        mixed = ffn_part(own_rows)
        for part in returned:
            mixed = mixed + part
        mixed = mixed + b_down
        hidden_out = layer_norm(
            normed.astype(jnp.float32) + mixed, norm_gain[1], norm_offset[1]
        ).astype(jnp.bfloat16)
        return (hidden_out[None], new_kv)

    return jax.shard_map(
        body,
        mesh=mesh,
        in_specs=(
            P("req", "tp", None),
            P("req", None, None, "tp"),
            P(None, "req", None, "tp"),
            P("req"),
            P(),
            P(None, None, "tp"),
            P(None, "tp"),
            P("tp", None),
            P(),
            P(None, "tp"),
            P("tp"),
            P("tp", None),
            P(),
            P(),
            P(),
        ),
        out_specs=(P("req", "tp", None), P("req", None, None, "tp")),
        check_vma=False,
    )
```

```python
import functools

import jax
import jax.numpy as jnp
from jax import lax
from jax.experimental import pallas as pl
from jax.experimental.pallas import tpu as pltpu
from jax.sharding import PartitionSpec as P

HEAD_DIM = 64
masked_score = -1e30
TQ = 512
TK = 512


def layer_norm(rows_in, gain, shift):
    center = rows_in - jnp.mean(rows_in, axis=-1, keepdims=True)
    spread = jnp.mean(center * center, axis=-1, keepdims=True)
    return center * lax.rsqrt(spread + 1e-05) * gain + shift


def _attend_block(q_ref, k_ref, v_ref, m_sc, l_sc, acc_sc, valid):
    width = q_ref.shape[1]
    col = lax.broadcasted_iota(jnp.int32, (q_ref.shape[0], 128), 1)
    low = col < HEAD_DIM
    for pair in range(width // 128):
        cols = slice(pair * 128, (pair + 1) * 128)
        q2 = q_ref[:, cols]
        k2 = k_ref[..., cols].reshape(-1, 128)
        v2 = v_ref[..., cols].reshape(-1, 128)
        alphas = []
        pvs = []
        for half in range(2):
            h = pair * 2 + half
            qh = jnp.where(low if half == 0 else jnp.logical_not(low), q2, jnp.zeros_like(q2))
            s = lax.dot_general(
                qh, k2, (((1,), (1,)), ((), ())), preferred_element_type=jnp.float32
            )
            if valid is not None:
                s = jnp.where(valid, s, masked_score)
            m_prev = m_sc[h]
            m_new = jnp.maximum(m_prev, jnp.max(s, axis=1, keepdims=True))
            alpha = jnp.exp(m_prev - m_new)
            p = jnp.exp(s - m_new[:, 0:1])
            l_sc[h] = alpha * l_sc[h] + jnp.sum(p, axis=1, keepdims=True)
            m_sc[h] = m_new
            pvs.append(jnp.dot(p.astype(jnp.bfloat16), v2, preferred_element_type=jnp.float32))
            alphas.append(alpha)
        alpha2 = jnp.where(low, alphas[0], alphas[1])
        acc_sc[:, cols] = alpha2 * acc_sc[:, cols] + jnp.where(low, pvs[0], pvs[1])


def _local_kernel(sref, q_ref, k_ref, v_ref, m_out, l_out, acc_out, m_sc, l_sc, acc_sc, *, n_short, nk):
    i = pl.program_id(0)
    j = pl.program_id(1)
    short_len = sref[0]

    @pl.when(j == 0)
    def _():
        m_sc[...] = jnp.full(m_sc.shape, masked_score, jnp.float32)
        l_sc[...] = jnp.zeros(l_sc.shape, jnp.float32)
        acc_sc[...] = jnp.zeros(acc_sc.shape, jnp.float32)

    is_short = j < n_short
    c = j - n_short
    first_row = i * TQ
    full = jnp.where(is_short, (j + 1) * TK <= short_len, c * TK + TK - 1 <= first_row)
    some = jnp.where(is_short, j * TK < short_len, c * TK <= first_row + TQ - 1)

    @pl.when(full)
    def _():
        _attend_block(q_ref, k_ref, v_ref, m_sc, l_sc, acc_sc, None)

    @pl.when(jnp.logical_and(some, jnp.logical_not(full)))
    def _():
        rows = lax.broadcasted_iota(jnp.int32, (TQ, TK), 0) + first_row
        keys = lax.broadcasted_iota(jnp.int32, (TQ, TK), 1)
        bound = jnp.where(is_short, short_len - j * TK, rows - c * TK + 1)
        valid = keys < bound
        _attend_block(q_ref, k_ref, v_ref, m_sc, l_sc, acc_sc, valid)

    @pl.when(j == nk - 1)
    def _():
        m_out[...] = m_sc[...]
        l_out[...] = l_sc[...]
        acc_out[...] = acc_sc[...]


def _long_kernel(sref, q_ref, k_ref, v_ref, m_in, l_in, acc_in, *rest, nk, finalize):
    j = pl.program_id(1)
    if finalize:
        o_ref, m_sc, l_sc, acc_sc = rest
    else:
        m_out, l_out, acc_out, m_sc, l_sc, acc_sc = rest

    @pl.when(j == 0)
    def _():
        m_sc[...] = m_in[...]
        l_sc[...] = l_in[...]
        acc_sc[...] = acc_in[...]

    @pl.when(sref[1] > 0)
    def _():
        _attend_block(q_ref, k_ref, v_ref, m_sc, l_sc, acc_sc, None)

    @pl.when(j == nk - 1)
    def _():
        if finalize:
            width = o_ref.shape[1]
            col = lax.broadcasted_iota(jnp.int32, (TQ, 128), 1)
            for pair in range(width // 128):
                cols = slice(pair * 128, (pair + 1) * 128)
                total = jnp.where(col < HEAD_DIM, l_sc[2 * pair], l_sc[2 * pair + 1])
                o_ref[:, cols] = (acc_sc[:, cols] / total).astype(o_ref.dtype)
        else:
            m_out[...] = m_sc[...]
            l_out[...] = l_sc[...]
            acc_out[...] = acc_sc[...]


def _cost(span, keys, width):
    heads = width // HEAD_DIM
    return pl.CostEstimate(
        flops=8 * span * keys * width,
        transcendentals=span * keys * heads,
        bytes_accessed=2 * keys * width * 2 * (span // TQ) + 16 * span * width,
    )


def local_attention(scalars, q, kv, n_short):
    span, width = q.shape
    heads = width // HEAD_DIM
    nq = span // TQ
    nk = kv.shape[0] // TK

    def kv_block(i, j, s):
        last_short = (s[0] - 1) // TK
        last_new = (i * TQ + TQ - 1) // TK
        return jnp.where(
            j < n_short, jnp.minimum(j, last_short), n_short + jnp.minimum(j - n_short, last_new)
        )

    stat_spec = pl.BlockSpec((heads, TQ, 128), lambda i, j, s: (0, i, 0))
    grid_spec = pltpu.PrefetchScalarGridSpec(
        num_scalar_prefetch=1,
        grid=(nq, nk),
        in_specs=[
            pl.BlockSpec((TQ, width), lambda i, j, s: (i, 0)),
            pl.BlockSpec((TK, width), lambda i, j, s: (kv_block(i, j, s), 0)),
            pl.BlockSpec((TK, width), lambda i, j, s: (kv_block(i, j, s), 1)),
        ],
        out_specs=[stat_spec, stat_spec, pl.BlockSpec((TQ, width), lambda i, j, s: (i, 0))],
        scratch_shapes=[
            pltpu.VMEM((heads, TQ, 128), jnp.float32),
            pltpu.VMEM((heads, TQ, 128), jnp.float32),
            pltpu.VMEM((TQ, width), jnp.float32),
        ],
    )
    return pl.pallas_call(
        functools.partial(_local_kernel, n_short=n_short, nk=nk),
        grid_spec=grid_spec,
        out_shape=[
            jax.ShapeDtypeStruct((heads, span, 128), jnp.float32),
            jax.ShapeDtypeStruct((heads, span, 128), jnp.float32),
            jax.ShapeDtypeStruct((span, width), jnp.float32),
        ],
        compiler_params=pltpu.CompilerParams(dimension_semantics=("arbitrary", "arbitrary")),
        cost_estimate=_cost(span, kv.shape[0], width),
    )(scalars, q, kv, kv)


def long_attention(scalars, q, kv, m, l, acc, finalize):
    span, width = q.shape
    heads = width // HEAD_DIM
    nq = span // TQ
    group = -(-TK // kv.shape[2])
    nk = kv.shape[0] // group
    stat_spec = pl.BlockSpec((heads, TQ, 128), lambda i, j, s: (0, i, 0))
    row_spec = pl.BlockSpec((TQ, width), lambda i, j, s: (i, 0))
    kv_shape = (group, None, kv.shape[2], width)
    if finalize:
        out_specs = row_spec
        out_shape = jax.ShapeDtypeStruct((span, width), jnp.bfloat16)
    else:
        out_specs = [stat_spec, stat_spec, row_spec]
        out_shape = [
            jax.ShapeDtypeStruct((heads, span, 128), jnp.float32),
            jax.ShapeDtypeStruct((heads, span, 128), jnp.float32),
            jax.ShapeDtypeStruct((span, width), jnp.float32),
        ]
    grid_spec = pltpu.PrefetchScalarGridSpec(
        num_scalar_prefetch=1,
        grid=(nq, nk),
        in_specs=[
            row_spec,
            pl.BlockSpec(kv_shape, lambda i, j, s: (j * s[1], 0, 0, 0)),
            pl.BlockSpec(kv_shape, lambda i, j, s: (j * s[1], 1, 0, 0)),
            stat_spec,
            stat_spec,
            row_spec,
        ],
        out_specs=out_specs,
        scratch_shapes=[
            pltpu.VMEM((heads, TQ, 128), jnp.float32),
            pltpu.VMEM((heads, TQ, 128), jnp.float32),
            pltpu.VMEM((TQ, width), jnp.float32),
        ],
    )
    return pl.pallas_call(
        functools.partial(_long_kernel, nk=nk, finalize=finalize),
        grid_spec=grid_spec,
        out_shape=out_shape,
        compiler_params=pltpu.CompilerParams(dimension_semantics=("arbitrary", "arbitrary")),
        cost_estimate=_cost(span, kv.shape[0] * kv.shape[2], width),
    )(scalars, q, kv, kv, m, l, acc)


def solution(mesh):
    n_req = mesh.shape["req"]

    def body(
        hidden_in,
        short_cache,
        long_cache,
        short_len,
        long_owner,
        w_qkv,
        b_qkv,
        w_out,
        b_out,
        w_in,
        b_in,
        w_down,
        b_down,
        norm_gain,
        norm_offset,
    ):
        n_long = long_cache.shape[0]
        long_ids = jnp.arange(n_long, dtype=jnp.int32)

        def which_long(request):
            owned = long_owner == request
            return jnp.sum(jnp.where(owned, long_ids, 0)), jnp.any(owned)

        me = lax.axis_index("req")
        my_long, has_long = which_long(me)
        requests = jnp.arange(n_req, dtype=jnp.int32)
        pick = long_owner[None, :] == requests[:, None]
        dest_long = jnp.sum(jnp.where(pick, long_ids[None, :], 0), axis=1)
        chosen = dest_long[:, None, None, None, None] == long_ids[None, :, None, None, None]
        by_kind = jnp.swapaxes(long_cache, 1, 2)[None]
        outgoing = jnp.max(jnp.where(chosen, by_kind, jnp.finfo(long_cache.dtype).min), axis=1)
        stripe = outgoing.shape[2]
        cuts = (0, stripe // 2, stripe * 3 // 4, stripe)
        pieces = [outgoing[:, :, cuts[k] : cuts[k + 1]] for k in range(3)]
        first_part = lax.all_to_all(pieces[0], "req", 0, 0, tiled=True)

        w_out_full = lax.all_gather(w_out, "tp", axis=0, tiled=True)

        local_rows = hidden_in[0]
        factors = jnp.array([0.125, 1.0, 1.0], jnp.float32)[None, :, None]
        mixed = jnp.einsum(
            "nd,cdk->nck",
            lax.all_gather(local_rows, "tp", axis=0, tiled=True),
            w_qkv,
            preferred_element_type=jnp.float32,
        )
        projected = ((mixed + b_qkv[None]) * factors).astype(jnp.bfloat16)
        second_src, projected = lax.optimization_barrier((pieces[1], projected))
        second_part = lax.all_to_all(second_src, "req", 0, 0, tiled=True)
        span_len = projected.shape[0]
        queries = projected[:, 0]
        new_kv = projected[None, :, 1:3]
        short_rows = short_cache[0]
        cache_len = short_rows.shape[0]
        local_kv = jnp.concatenate(
            [short_rows.reshape(cache_len, -1), projected[:, 1:3].reshape(span_len, -1)], axis=0
        )
        scalars = jnp.stack([short_len[0], has_long.astype(jnp.int32)])
        m, l, acc = local_attention(scalars, queries, local_kv, cache_len // TK)
        third_src, m = lax.optimization_barrier((pieces[2], m))
        third_part = lax.all_to_all(third_src, "req", 0, 0, tiled=True)
        m, l, acc = long_attention(scalars, queries, first_part, m, l, acc, False)
        m, l, acc = long_attention(scalars, queries, second_part, m, l, acc, False)
        context = long_attention(scalars, queries, third_part, m, l, acc, True)

        context_rows = lax.all_to_all(context, "tp", 0, 1, tiled=True)
        attended = jnp.dot(context_rows, w_out_full, preferred_element_type=jnp.float32) + b_out
        normed = layer_norm(
            local_rows.astype(jnp.float32) + attended, norm_gain[0], norm_offset[0]
        ).astype(jnp.bfloat16)
        n_tp = mesh.shape["tp"]
        sibling = [(k, k ^ 1) for k in range(n_tp)]
        halves_in = (w_in, lax.ppermute(w_in, "tp", sibling))
        halves_b = (b_in, lax.ppermute(b_in, "tp", sibling))
        halves_down = (w_down, lax.ppermute(w_down, "tp", sibling))

        def ffn_part(rows):
            total = None
            for w_a, b_a, w_b in zip(halves_in, halves_b, halves_down):
                units = jax.nn.gelu(
                    jnp.dot(rows, w_a, preferred_element_type=jnp.float32) + b_a,
                    approximate=False,
                ).astype(jnp.bfloat16)
                part = jnp.dot(units, w_b, preferred_element_type=jnp.float32)
                total = part if total is None else total + part
            return total

        own_rows = normed
        returned = []
        for step in range(1, n_tp // 2):
            ahead = [(k, (k + 2 * step) % n_tp) for k in range(n_tp)]
            behind = [(b, a) for a, b in ahead]
            peer_part = ffn_part(lax.ppermute(normed, "tp", ahead))
            own_rows, peer_part = lax.optimization_barrier((own_rows, peer_part))
            returned.append(lax.ppermute(peer_part, "tp", behind))
        mixed = ffn_part(own_rows)
        for part in returned:
            mixed = mixed + part
        mixed = mixed + b_down
        hidden_out = layer_norm(
            normed.astype(jnp.float32) + mixed, norm_gain[1], norm_offset[1]
        ).astype(jnp.bfloat16)
        return (hidden_out[None], new_kv)

    return jax.shard_map(
        body,
        mesh=mesh,
        in_specs=(
            P("req", "tp", None),
            P("req", None, None, "tp"),
            P(None, "req", None, "tp"),
            P("req"),
            P(),
            P(None, None, "tp"),
            P(None, "tp"),
            P("tp", None),
            P(),
            P(None, "tp"),
            P("tp"),
            P("tp", None),
            P(),
            P(),
            P(),
        ),
        out_specs=(P("req", "tp", None), P("req", None, None, "tp")),
        check_vma=False,
    )
```

```python
import functools

import jax
import jax.numpy as jnp
from jax import lax
from jax.experimental import pallas as pl
from jax.experimental.pallas import tpu as pltpu
from jax.sharding import PartitionSpec as P

HEAD_DIM = 64
masked_score = -1e30
TQ = 512
TK = 512


def layer_norm(rows_in, gain, shift):
    center = rows_in - jnp.mean(rows_in, axis=-1, keepdims=True)
    spread = jnp.mean(center * center, axis=-1, keepdims=True)
    return center * lax.rsqrt(spread + 1e-05) * gain + shift


def _attend_block(q_ref, k_ref, v_ref, m_sc, l_sc, acc_sc, valid):
    width = q_ref.shape[1]
    col = lax.broadcasted_iota(jnp.int32, (q_ref.shape[0], 128), 1)
    low = col < HEAD_DIM
    for pair in range(width // 128):
        cols = slice(pair * 128, (pair + 1) * 128)
        q2 = q_ref[:, cols]
        k2 = k_ref[..., cols].reshape(-1, 128)
        v2 = v_ref[..., cols].reshape(-1, 128)
        alphas = []
        pvs = []
        for half in range(2):
            h = pair * 2 + half
            qh = jnp.where(low if half == 0 else jnp.logical_not(low), q2, jnp.zeros_like(q2))
            s = lax.dot_general(
                qh, k2, (((1,), (1,)), ((), ())), preferred_element_type=jnp.float32
            )
            if valid is not None:
                s = jnp.where(valid, s, masked_score)
            m_prev = m_sc[h]
            m_new = jnp.maximum(m_prev, jnp.max(s, axis=1, keepdims=True))
            alpha = jnp.exp(m_prev - m_new)
            p = jnp.exp(s - m_new[:, 0:1])
            l_sc[h] = alpha * l_sc[h] + jnp.sum(p, axis=1, keepdims=True)
            m_sc[h] = m_new
            pvs.append(jnp.dot(p.astype(jnp.bfloat16), v2, preferred_element_type=jnp.float32))
            alphas.append(alpha)
        alpha2 = jnp.where(low, alphas[0], alphas[1])
        acc_sc[:, cols] = alpha2 * acc_sc[:, cols] + jnp.where(low, pvs[0], pvs[1])


def _local_kernel(sref, q_ref, k_ref, v_ref, m_out, l_out, acc_out, m_sc, l_sc, acc_sc, *, n_short, nk):
    i = pl.program_id(0)
    j = pl.program_id(1)
    short_len = sref[0]

    @pl.when(j == 0)
    def _():
        m_sc[...] = jnp.full(m_sc.shape, masked_score, jnp.float32)
        l_sc[...] = jnp.zeros(l_sc.shape, jnp.float32)
        acc_sc[...] = jnp.zeros(acc_sc.shape, jnp.float32)

    is_short = j < n_short
    c = j - n_short
    first_row = i * TQ
    full = jnp.where(is_short, (j + 1) * TK <= short_len, c * TK + TK - 1 <= first_row)
    some = jnp.where(is_short, j * TK < short_len, c * TK <= first_row + TQ - 1)

    @pl.when(full)
    def _():
        _attend_block(q_ref, k_ref, v_ref, m_sc, l_sc, acc_sc, None)

    @pl.when(jnp.logical_and(some, jnp.logical_not(full)))
    def _():
        rows = lax.broadcasted_iota(jnp.int32, (TQ, TK), 0) + first_row
        keys = lax.broadcasted_iota(jnp.int32, (TQ, TK), 1)
        bound = jnp.where(is_short, short_len - j * TK, rows - c * TK + 1)
        valid = keys < bound
        _attend_block(q_ref, k_ref, v_ref, m_sc, l_sc, acc_sc, valid)

    @pl.when(j == nk - 1)
    def _():
        m_out[...] = m_sc[...]
        l_out[...] = l_sc[...]
        acc_out[...] = acc_sc[...]


def _long_kernel(sref, q_ref, k_ref, v_ref, m_in, l_in, acc_in, *rest, nk, finalize):
    j = pl.program_id(1)
    if finalize:
        o_ref, m_sc, l_sc, acc_sc = rest
    else:
        m_out, l_out, acc_out, m_sc, l_sc, acc_sc = rest

    @pl.when(j == 0)
    def _():
        m_sc[...] = m_in[...]
        l_sc[...] = l_in[...]
        acc_sc[...] = acc_in[...]

    @pl.when(sref[1] > 0)
    def _():
        _attend_block(q_ref, k_ref, v_ref, m_sc, l_sc, acc_sc, None)

    @pl.when(j == nk - 1)
    def _():
        if finalize:
            width = o_ref.shape[1]
            col = lax.broadcasted_iota(jnp.int32, (TQ, 128), 1)
            for pair in range(width // 128):
                cols = slice(pair * 128, (pair + 1) * 128)
                total = jnp.where(col < HEAD_DIM, l_sc[2 * pair], l_sc[2 * pair + 1])
                o_ref[:, cols] = (acc_sc[:, cols] / total).astype(o_ref.dtype)
        else:
            m_out[...] = m_sc[...]
            l_out[...] = l_sc[...]
            acc_out[...] = acc_sc[...]


def _cost(span, keys, width):
    heads = width // HEAD_DIM
    return pl.CostEstimate(
        flops=8 * span * keys * width,
        transcendentals=span * keys * heads,
        bytes_accessed=2 * keys * width * 2 * (span // TQ) + 16 * span * width,
    )


def local_attention(scalars, q, kv, n_short):
    span, width = q.shape
    heads = width // HEAD_DIM
    nq = span // TQ
    nk = kv.shape[0] // TK

    def kv_block(i, j, s):
        last_short = (s[0] - 1) // TK
        last_new = (i * TQ + TQ - 1) // TK
        return jnp.where(
            j < n_short, jnp.minimum(j, last_short), n_short + jnp.minimum(j - n_short, last_new)
        )

    stat_spec = pl.BlockSpec((heads, TQ, 128), lambda i, j, s: (0, i, 0))
    grid_spec = pltpu.PrefetchScalarGridSpec(
        num_scalar_prefetch=1,
        grid=(nq, nk),
        in_specs=[
            pl.BlockSpec((TQ, width), lambda i, j, s: (i, 0)),
            pl.BlockSpec((TK, width), lambda i, j, s: (kv_block(i, j, s), 0)),
            pl.BlockSpec((TK, width), lambda i, j, s: (kv_block(i, j, s), 1)),
        ],
        out_specs=[stat_spec, stat_spec, pl.BlockSpec((TQ, width), lambda i, j, s: (i, 0))],
        scratch_shapes=[
            pltpu.VMEM((heads, TQ, 128), jnp.float32),
            pltpu.VMEM((heads, TQ, 128), jnp.float32),
            pltpu.VMEM((TQ, width), jnp.float32),
        ],
    )
    return pl.pallas_call(
        functools.partial(_local_kernel, n_short=n_short, nk=nk),
        grid_spec=grid_spec,
        out_shape=[
            jax.ShapeDtypeStruct((heads, span, 128), jnp.float32),
            jax.ShapeDtypeStruct((heads, span, 128), jnp.float32),
            jax.ShapeDtypeStruct((span, width), jnp.float32),
        ],
        compiler_params=pltpu.CompilerParams(dimension_semantics=("arbitrary", "arbitrary")),
        cost_estimate=_cost(span, kv.shape[0], width),
    )(scalars, q, kv, kv)


def long_attention(scalars, q, kv, m, l, acc, finalize):
    span, width = q.shape
    heads = width // HEAD_DIM
    nq = span // TQ
    group = -(-TK // kv.shape[2])
    nk = kv.shape[0] // group
    stat_spec = pl.BlockSpec((heads, TQ, 128), lambda i, j, s: (0, i, 0))
    row_spec = pl.BlockSpec((TQ, width), lambda i, j, s: (i, 0))
    kv_shape = (group, None, kv.shape[2], width)
    if finalize:
        out_specs = row_spec
        out_shape = jax.ShapeDtypeStruct((span, width), jnp.bfloat16)
    else:
        out_specs = [stat_spec, stat_spec, row_spec]
        out_shape = [
            jax.ShapeDtypeStruct((heads, span, 128), jnp.float32),
            jax.ShapeDtypeStruct((heads, span, 128), jnp.float32),
            jax.ShapeDtypeStruct((span, width), jnp.float32),
        ]
    grid_spec = pltpu.PrefetchScalarGridSpec(
        num_scalar_prefetch=1,
        grid=(nq, nk),
        in_specs=[
            row_spec,
            pl.BlockSpec(kv_shape, lambda i, j, s: (j * s[1], 0, 0, 0)),
            pl.BlockSpec(kv_shape, lambda i, j, s: (j * s[1], 1, 0, 0)),
            stat_spec,
            stat_spec,
            row_spec,
        ],
        out_specs=out_specs,
        scratch_shapes=[
            pltpu.VMEM((heads, TQ, 128), jnp.float32),
            pltpu.VMEM((heads, TQ, 128), jnp.float32),
            pltpu.VMEM((TQ, width), jnp.float32),
        ],
    )
    return pl.pallas_call(
        functools.partial(_long_kernel, nk=nk, finalize=finalize),
        grid_spec=grid_spec,
        out_shape=out_shape,
        compiler_params=pltpu.CompilerParams(dimension_semantics=("arbitrary", "arbitrary")),
        cost_estimate=_cost(span, kv.shape[0] * kv.shape[2], width),
    )(scalars, q, kv, kv, m, l, acc)


def solution(mesh):
    n_req = mesh.shape["req"]

    def body(
        hidden_in,
        short_cache,
        long_cache,
        short_len,
        long_owner,
        w_qkv,
        b_qkv,
        w_out,
        b_out,
        w_in,
        b_in,
        w_down,
        b_down,
        norm_gain,
        norm_offset,
    ):
        n_long = long_cache.shape[0]
        long_ids = jnp.arange(n_long, dtype=jnp.int32)

        def which_long(request):
            owned = long_owner == request
            return jnp.sum(jnp.where(owned, long_ids, 0)), jnp.any(owned)

        me = lax.axis_index("req")
        my_long, has_long = which_long(me)
        requests = jnp.arange(n_req, dtype=jnp.int32)
        pick = long_owner[None, :] == requests[:, None]
        dest_long = jnp.sum(jnp.where(pick, long_ids[None, :], 0), axis=1)
        chosen = dest_long[:, None, None, None, None] == long_ids[None, :, None, None, None]
        by_kind = jnp.swapaxes(long_cache, 1, 2)[None]
        outgoing = jnp.max(jnp.where(chosen, by_kind, jnp.finfo(long_cache.dtype).min), axis=1)
        split = outgoing.shape[2] * 3 // 4
        first_part = lax.all_to_all(outgoing[:, :, :split], "req", 0, 0, tiled=True)

        w_out_full = lax.all_gather(w_out, "tp", axis=0, tiled=True)

        local_rows = hidden_in[0]
        factors = jnp.array([0.125, 1.0, 1.0], jnp.float32)[None, :, None]
        rows_all = lax.all_gather(local_rows, "tp", axis=0, tiled=True)
        mixed = jnp.einsum(
            "nd,cdk->nck",
            rows_all,
            w_qkv,
            preferred_element_type=jnp.float32,
        )
        projected = ((mixed + b_qkv[None]) * factors).astype(jnp.bfloat16)
        span_len = projected.shape[0]
        queries = projected[:, 0]
        new_kv = projected[None, :, 1:3]
        short_rows = short_cache[0]
        cache_len = short_rows.shape[0]
        local_kv = jnp.concatenate(
            [short_rows.reshape(cache_len, -1), projected[:, 1:3].reshape(span_len, -1)], axis=0
        )
        scalars = jnp.stack([short_len[0], has_long.astype(jnp.int32)])
        m, l, acc = local_attention(scalars, queries, local_kv, cache_len // TK)
        rest, m = lax.optimization_barrier((outgoing[:, :, split:], m))
        second_part = lax.all_to_all(rest, "req", 0, 0, tiled=True)
        m, l, acc = long_attention(scalars, queries, first_part, m, l, acc, False)
        context = long_attention(scalars, queries, second_part, m, l, acc, True)

        n_tp = mesh.shape["tp"]
        n_y = n_tp // 2
        block = span_len // n_tp
        core = lax.axis_index("tp") % 2
        chip = lax.axis_index("tp") // 2
        by_core = jnp.swapaxes(context.reshape(n_y, 2, block, context.shape[1]), 0, 1)
        outgoing_ctx = jnp.broadcast_to(by_core[None], (n_y,) + by_core.shape).reshape(
            (n_tp, n_y, block, context.shape[1])
        )
        got = lax.all_to_all(outgoing_ctx, "tp", 0, 0, tiled=True)
        class_ctx = jnp.transpose(got, (1, 2, 0, 3)).reshape(n_y * block, -1)
        class_rows = lax.dynamic_index_in_dim(
            rows_all.reshape(n_y, 2, block, rows_all.shape[1]), core, 1, keepdims=False
        ).reshape(n_y * block, -1)
        attended = jnp.dot(class_ctx, w_out_full, preferred_element_type=jnp.float32) + b_out
        class_normed = layer_norm(
            class_rows.astype(jnp.float32) + attended, norm_gain[0], norm_offset[0]
        ).astype(jnp.bfloat16).reshape(n_y, block, -1)
        normed = lax.dynamic_index_in_dim(class_normed, chip, 0, keepdims=False)
        sibling = [(k, k ^ 1) for k in range(n_tp)]
        halves_in = (w_in, lax.ppermute(w_in, "tp", sibling))
        halves_b = (b_in, lax.ppermute(b_in, "tp", sibling))
        halves_down = (w_down, lax.ppermute(w_down, "tp", sibling))

        def ffn_part(rows):
            total = None
            for w_a, b_a, w_b in zip(halves_in, halves_b, halves_down):
                units = jax.nn.gelu(
                    jnp.dot(rows, w_a, preferred_element_type=jnp.float32) + b_a,
                    approximate=False,
                ).astype(jnp.bfloat16)
                part = jnp.dot(units, w_b, preferred_element_type=jnp.float32)
                total = part if total is None else total + part
            return total

        own_rows = normed
        returned = []
        for step in range(1, n_y):
            ahead = [(k, (k + 2 * step) % n_tp) for k in range(n_tp)]
            behind = [(b, a) for a, b in ahead]
            peer_rows = lax.dynamic_index_in_dim(
                class_normed, (chip + n_y - step) % n_y, 0, keepdims=False
            )
            peer_part = ffn_part(peer_rows)
            own_rows, peer_part = lax.optimization_barrier((own_rows, peer_part))
            returned.append(lax.ppermute(peer_part, "tp", behind))
        mixed = ffn_part(own_rows)
        for part in returned:
            mixed = mixed + part
        mixed = mixed + b_down
        hidden_out = layer_norm(
            normed.astype(jnp.float32) + mixed, norm_gain[1], norm_offset[1]
        ).astype(jnp.bfloat16)
        return (hidden_out[None], new_kv)

    return jax.shard_map(
        body,
        mesh=mesh,
        in_specs=(
            P("req", "tp", None),
            P("req", None, None, "tp"),
            P(None, "req", None, "tp"),
            P("req"),
            P(),
            P(None, None, "tp"),
            P(None, "tp"),
            P("tp", None),
            P(),
            P(None, "tp"),
            P("tp"),
            P("tp", None),
            P(),
            P(),
            P(),
        ),
        out_specs=(P("req", "tp", None), P("req", None, None, "tp")),
        check_vma=False,
    )
```

```python
import functools

import jax
import jax.numpy as jnp
from jax import lax
from jax.experimental import pallas as pl
from jax.experimental.pallas import tpu as pltpu
from jax.sharding import PartitionSpec as P

HEAD_DIM = 64
masked_score = -1e30
TQ = 512
TK = 512


def layer_norm(rows_in, gain, shift):
    center = rows_in - jnp.mean(rows_in, axis=-1, keepdims=True)
    spread = jnp.mean(center * center, axis=-1, keepdims=True)
    return center * lax.rsqrt(spread + 1e-05) * gain + shift


def _attend_block(q_ref, k_ref, v_ref, m_sc, l_sc, acc_sc, valid):
    width = q_ref.shape[1]
    col = lax.broadcasted_iota(jnp.int32, (q_ref.shape[0], 128), 1)
    low = col < HEAD_DIM
    for pair in range(width // 128):
        cols = slice(pair * 128, (pair + 1) * 128)
        q2 = q_ref[:, cols]
        k2 = k_ref[..., cols].reshape(-1, 128)
        v2 = v_ref[..., cols].reshape(-1, 128)
        alphas = []
        pvs = []
        for half in range(2):
            h = pair * 2 + half
            qh = jnp.where(low if half == 0 else jnp.logical_not(low), q2, jnp.zeros_like(q2))
            s = lax.dot_general(
                qh, k2, (((1,), (1,)), ((), ())), preferred_element_type=jnp.float32
            )
            if valid is not None:
                s = jnp.where(valid, s, masked_score)
            m_prev = m_sc[h]
            m_new = jnp.maximum(m_prev, jnp.max(s, axis=1, keepdims=True))
            alpha = jnp.exp(m_prev - m_new)
            p = jnp.exp(s - m_new[:, 0:1])
            l_sc[h] = alpha * l_sc[h] + jnp.sum(p, axis=1, keepdims=True)
            m_sc[h] = m_new
            pvs.append(jnp.dot(p.astype(jnp.bfloat16), v2, preferred_element_type=jnp.float32))
            alphas.append(alpha)
        alpha2 = jnp.where(low, alphas[0], alphas[1])
        acc_sc[:, cols] = alpha2 * acc_sc[:, cols] + jnp.where(low, pvs[0], pvs[1])


def _local_kernel(sref, q_ref, k_ref, v_ref, m_out, l_out, acc_out, m_sc, l_sc, acc_sc, *, n_short, nk):
    i = pl.program_id(0)
    j = pl.program_id(1)
    short_len = sref[0]

    @pl.when(j == 0)
    def _():
        m_sc[...] = jnp.full(m_sc.shape, masked_score, jnp.float32)
        l_sc[...] = jnp.zeros(l_sc.shape, jnp.float32)
        acc_sc[...] = jnp.zeros(acc_sc.shape, jnp.float32)

    is_short = j < n_short
    c = j - n_short
    first_row = i * TQ
    full = jnp.where(is_short, (j + 1) * TK <= short_len, c * TK + TK - 1 <= first_row)
    some = jnp.where(is_short, j * TK < short_len, c * TK <= first_row + TQ - 1)

    @pl.when(full)
    def _():
        _attend_block(q_ref, k_ref, v_ref, m_sc, l_sc, acc_sc, None)

    @pl.when(jnp.logical_and(some, jnp.logical_not(full)))
    def _():
        rows = lax.broadcasted_iota(jnp.int32, (TQ, TK), 0) + first_row
        keys = lax.broadcasted_iota(jnp.int32, (TQ, TK), 1)
        bound = jnp.where(is_short, short_len - j * TK, rows - c * TK + 1)
        valid = keys < bound
        _attend_block(q_ref, k_ref, v_ref, m_sc, l_sc, acc_sc, valid)

    @pl.when(j == nk - 1)
    def _():
        m_out[...] = m_sc[...]
        l_out[...] = l_sc[...]
        acc_out[...] = acc_sc[...]


def _long_kernel(sref, q_ref, k_ref, v_ref, m_in, l_in, acc_in, *rest, nk, finalize):
    j = pl.program_id(1)
    if finalize:
        o_ref, m_sc, l_sc, acc_sc = rest
    else:
        m_out, l_out, acc_out, m_sc, l_sc, acc_sc = rest

    @pl.when(j == 0)
    def _():
        m_sc[...] = m_in[...]
        l_sc[...] = l_in[...]
        acc_sc[...] = acc_in[...]

    @pl.when(sref[1] > 0)
    def _():
        _attend_block(q_ref, k_ref, v_ref, m_sc, l_sc, acc_sc, None)

    @pl.when(j == nk - 1)
    def _():
        if finalize:
            width = o_ref.shape[1]
            col = lax.broadcasted_iota(jnp.int32, (TQ, 128), 1)
            for pair in range(width // 128):
                cols = slice(pair * 128, (pair + 1) * 128)
                total = jnp.where(col < HEAD_DIM, l_sc[2 * pair], l_sc[2 * pair + 1])
                o_ref[:, cols] = (acc_sc[:, cols] / total).astype(o_ref.dtype)
        else:
            m_out[...] = m_sc[...]
            l_out[...] = l_sc[...]
            acc_out[...] = acc_sc[...]


def _cost(span, keys, width):
    heads = width // HEAD_DIM
    return pl.CostEstimate(
        flops=8 * span * keys * width,
        transcendentals=span * keys * heads,
        bytes_accessed=2 * keys * width * 2 * (span // TQ) + 16 * span * width,
    )


def local_attention(scalars, q, kv, n_short):
    span, width = q.shape
    heads = width // HEAD_DIM
    nq = span // TQ
    nk = kv.shape[0] // TK

    def kv_block(i, j, s):
        last_short = (s[0] - 1) // TK
        last_new = (i * TQ + TQ - 1) // TK
        return jnp.where(
            j < n_short, jnp.minimum(j, last_short), n_short + jnp.minimum(j - n_short, last_new)
        )

    stat_spec = pl.BlockSpec((heads, TQ, 128), lambda i, j, s: (0, i, 0))
    grid_spec = pltpu.PrefetchScalarGridSpec(
        num_scalar_prefetch=1,
        grid=(nq, nk),
        in_specs=[
            pl.BlockSpec((TQ, width), lambda i, j, s: (i, 0)),
            pl.BlockSpec((TK, width), lambda i, j, s: (kv_block(i, j, s), 0)),
            pl.BlockSpec((TK, width), lambda i, j, s: (kv_block(i, j, s), 1)),
        ],
        out_specs=[stat_spec, stat_spec, pl.BlockSpec((TQ, width), lambda i, j, s: (i, 0))],
        scratch_shapes=[
            pltpu.VMEM((heads, TQ, 128), jnp.float32),
            pltpu.VMEM((heads, TQ, 128), jnp.float32),
            pltpu.VMEM((TQ, width), jnp.float32),
        ],
    )
    return pl.pallas_call(
        functools.partial(_local_kernel, n_short=n_short, nk=nk),
        grid_spec=grid_spec,
        out_shape=[
            jax.ShapeDtypeStruct((heads, span, 128), jnp.float32),
            jax.ShapeDtypeStruct((heads, span, 128), jnp.float32),
            jax.ShapeDtypeStruct((span, width), jnp.float32),
        ],
        compiler_params=pltpu.CompilerParams(dimension_semantics=("arbitrary", "arbitrary")),
        cost_estimate=_cost(span, kv.shape[0], width),
    )(scalars, q, kv, kv)


def long_attention(scalars, q, kv, m, l, acc, finalize):
    span, width = q.shape
    heads = width // HEAD_DIM
    nq = span // TQ
    group = -(-TK // kv.shape[2])
    nk = kv.shape[0] // group
    stat_spec = pl.BlockSpec((heads, TQ, 128), lambda i, j, s: (0, i, 0))
    row_spec = pl.BlockSpec((TQ, width), lambda i, j, s: (i, 0))
    kv_shape = (group, None, kv.shape[2], width)
    if finalize:
        out_specs = row_spec
        out_shape = jax.ShapeDtypeStruct((span, width), jnp.bfloat16)
    else:
        out_specs = [stat_spec, stat_spec, row_spec]
        out_shape = [
            jax.ShapeDtypeStruct((heads, span, 128), jnp.float32),
            jax.ShapeDtypeStruct((heads, span, 128), jnp.float32),
            jax.ShapeDtypeStruct((span, width), jnp.float32),
        ]
    grid_spec = pltpu.PrefetchScalarGridSpec(
        num_scalar_prefetch=1,
        grid=(nq, nk),
        in_specs=[
            row_spec,
            pl.BlockSpec(kv_shape, lambda i, j, s: (j * s[1], 0, 0, 0)),
            pl.BlockSpec(kv_shape, lambda i, j, s: (j * s[1], 1, 0, 0)),
            stat_spec,
            stat_spec,
            row_spec,
        ],
        out_specs=out_specs,
        scratch_shapes=[
            pltpu.VMEM((heads, TQ, 128), jnp.float32),
            pltpu.VMEM((heads, TQ, 128), jnp.float32),
            pltpu.VMEM((TQ, width), jnp.float32),
        ],
    )
    return pl.pallas_call(
        functools.partial(_long_kernel, nk=nk, finalize=finalize),
        grid_spec=grid_spec,
        out_shape=out_shape,
        compiler_params=pltpu.CompilerParams(dimension_semantics=("arbitrary", "arbitrary")),
        cost_estimate=_cost(span, kv.shape[0] * kv.shape[2], width),
    )(scalars, q, kv, kv, m, l, acc)


def solution(mesh):
    n_req = mesh.shape["req"]

    def body(
        hidden_in,
        short_cache,
        long_cache,
        short_len,
        long_owner,
        w_qkv,
        b_qkv,
        w_out,
        b_out,
        w_in,
        b_in,
        w_down,
        b_down,
        norm_gain,
        norm_offset,
    ):
        n_long = long_cache.shape[0]
        long_ids = jnp.arange(n_long, dtype=jnp.int32)

        def which_long(request):
            owned = long_owner == request
            return jnp.sum(jnp.where(owned, long_ids, 0)), jnp.any(owned)

        me = lax.axis_index("req")
        my_long, has_long = which_long(me)
        requests = jnp.arange(n_req, dtype=jnp.int32)
        pick = long_owner[None, :] == requests[:, None]
        dest_long = jnp.sum(jnp.where(pick, long_ids[None, :], 0), axis=1)
        chosen = dest_long[:, None, None, None, None] == long_ids[None, :, None, None, None]
        by_kind = jnp.swapaxes(long_cache, 1, 2)[None]
        outgoing = jnp.max(jnp.where(chosen, by_kind, jnp.finfo(long_cache.dtype).min), axis=1)
        split = outgoing.shape[2] * 3 // 4
        first_part = lax.all_to_all(outgoing[:, :, :split], "req", 0, 0, tiled=True)

        w_out_full = lax.all_gather(w_out, "tp", axis=0, tiled=True)

        local_rows = hidden_in[0]
        factors = jnp.array([0.125, 1.0, 1.0], jnp.float32)[None, :, None]
        rows_all = lax.all_gather(local_rows, "tp", axis=0, tiled=True)
        mixed = jnp.einsum(
            "nd,cdk->nck",
            rows_all,
            w_qkv,
            preferred_element_type=jnp.float32,
        )
        projected = ((mixed + b_qkv[None]) * factors).astype(jnp.bfloat16)
        span_len = projected.shape[0]
        queries = projected[:, 0]
        new_kv = projected[None, :, 1:3]
        short_rows = short_cache[0]
        cache_len = short_rows.shape[0]
        local_kv = jnp.concatenate(
            [short_rows.reshape(cache_len, -1), projected[:, 1:3].reshape(span_len, -1)], axis=0
        )
        scalars = jnp.stack([short_len[0], has_long.astype(jnp.int32)])
        m, l, acc = local_attention(scalars, queries, local_kv, cache_len // TK)
        rest, m = lax.optimization_barrier((outgoing[:, :, split:], m))
        second_part = lax.all_to_all(rest, "req", 0, 0, tiled=True)
        m, l, acc = long_attention(scalars, queries, first_part, m, l, acc, False)
        context = long_attention(scalars, queries, second_part, m, l, acc, True)

        n_tp = mesh.shape["tp"]
        n_y = n_tp // 2
        block = span_len // n_tp
        core = lax.axis_index("tp") % 2
        chip = lax.axis_index("tp") // 2
        by_core = jnp.swapaxes(context.reshape(n_y, 2, block, context.shape[1]), 0, 1)
        outgoing_ctx = jnp.broadcast_to(by_core[None], (n_y,) + by_core.shape).reshape(
            (n_tp, n_y, block, context.shape[1])
        )
        got = lax.all_to_all(outgoing_ctx, "tp", 0, 0, tiled=True)
        class_ctx = jnp.transpose(got, (1, 2, 0, 3)).reshape(n_y * block, -1)
        class_rows = lax.dynamic_index_in_dim(
            rows_all.reshape(n_y, 2, block, rows_all.shape[1]), core, 1, keepdims=False
        ).reshape(n_y * block, -1)
        attended = jnp.dot(class_ctx, w_out_full, preferred_element_type=jnp.float32) + b_out
        class_normed = layer_norm(
            class_rows.astype(jnp.float32) + attended, norm_gain[0], norm_offset[0]
        ).astype(jnp.bfloat16).reshape(n_y, block, -1)
        normed = lax.dynamic_index_in_dim(class_normed, chip, 0, keepdims=False)
        sibling = [(k, k ^ 1) for k in range(n_tp)]
        halves_in = (w_in, lax.ppermute(w_in, "tp", sibling))
        halves_b = (b_in, lax.ppermute(b_in, "tp", sibling))
        halves_down = (w_down, lax.ppermute(w_down, "tp", sibling))

        def ffn_part(rows):
            total = None
            for w_a, b_a, w_b in zip(halves_in, halves_b, halves_down):
                units = jax.nn.gelu(
                    jnp.dot(rows, w_a, preferred_element_type=jnp.float32) + b_a,
                    approximate=False,
                ).astype(jnp.bfloat16)
                part = jnp.dot(units, w_b, preferred_element_type=jnp.float32)
                total = part if total is None else total + part
            return total

        own_rows = normed
        returned = []
        for step in range(1, n_y):
            ahead = [(k, (k + 2 * step) % n_tp) for k in range(n_tp)]
            behind = [(b, a) for a, b in ahead]
            peer_rows = lax.dynamic_index_in_dim(
                class_normed, (chip + n_y - step) % n_y, 0, keepdims=False
            )
            peer_part = ffn_part(peer_rows)
            own_rows, peer_part = lax.optimization_barrier((own_rows, peer_part))
            returned.append(lax.ppermute(peer_part, "tp", behind))
        mixed = ffn_part(own_rows)
        mixed, returned = lax.optimization_barrier((mixed, returned))
        for part in returned:
            mixed = mixed + part
        mixed = mixed + b_down
        hidden_out = layer_norm(
            normed.astype(jnp.float32) + mixed, norm_gain[1], norm_offset[1]
        ).astype(jnp.bfloat16)
        return (hidden_out[None], new_kv)

    return jax.shard_map(
        body,
        mesh=mesh,
        in_specs=(
            P("req", "tp", None),
            P("req", None, None, "tp"),
            P(None, "req", None, "tp"),
            P("req"),
            P(),
            P(None, None, "tp"),
            P(None, "tp"),
            P("tp", None),
            P(),
            P(None, "tp"),
            P("tp"),
            P("tp", None),
            P(),
            P(),
            P(),
        ),
        out_specs=(P("req", "tp", None), P("req", None, None, "tp")),
        check_vma=False,
    )
```

```python
import functools

import jax
import jax.numpy as jnp
from jax import lax
from jax.experimental import pallas as pl
from jax.experimental.pallas import tpu as pltpu
from jax.sharding import PartitionSpec as P

HEAD_DIM = 64
masked_score = -1e30
TQ = 512
TK = 512


def layer_norm(rows_in, gain, shift):
    center = rows_in - jnp.mean(rows_in, axis=-1, keepdims=True)
    spread = jnp.mean(center * center, axis=-1, keepdims=True)
    return center * lax.rsqrt(spread + 1e-05) * gain + shift


def _attend_block(q_ref, k_ref, v_ref, m_sc, l_sc, acc_sc, valid):
    width = q_ref.shape[1]
    col = lax.broadcasted_iota(jnp.int32, (q_ref.shape[0], 128), 1)
    low = col < HEAD_DIM
    for pair in range(width // 128):
        cols = slice(pair * 128, (pair + 1) * 128)
        q2 = q_ref[:, cols]
        k2 = k_ref[..., cols].reshape(-1, 128)
        v2 = v_ref[..., cols].reshape(-1, 128)
        alphas = []
        pvs = []
        for half in range(2):
            h = pair * 2 + half
            qh = jnp.where(low if half == 0 else jnp.logical_not(low), q2, jnp.zeros_like(q2))
            s = lax.dot_general(
                qh, k2, (((1,), (1,)), ((), ())), preferred_element_type=jnp.float32
            )
            if valid is not None:
                s = jnp.where(valid, s, masked_score)
            m_prev = m_sc[h]
            m_new = jnp.maximum(m_prev, jnp.max(s, axis=1, keepdims=True))
            alpha = jnp.exp(m_prev - m_new)
            p = jnp.exp(s - m_new[:, 0:1])
            l_sc[h] = alpha * l_sc[h] + jnp.sum(p, axis=1, keepdims=True)
            m_sc[h] = m_new
            pvs.append(jnp.dot(p.astype(jnp.bfloat16), v2, preferred_element_type=jnp.float32))
            alphas.append(alpha)
        alpha2 = jnp.where(low, alphas[0], alphas[1])
        acc_sc[:, cols] = alpha2 * acc_sc[:, cols] + jnp.where(low, pvs[0], pvs[1])


def _local_kernel(sref, q_ref, k_ref, v_ref, m_out, l_out, acc_out, m_sc, l_sc, acc_sc, *, n_short, nk):
    i = pl.program_id(0)
    j = pl.program_id(1)
    short_len = sref[0]

    @pl.when(j == 0)
    def _():
        m_sc[...] = jnp.full(m_sc.shape, masked_score, jnp.float32)
        l_sc[...] = jnp.zeros(l_sc.shape, jnp.float32)
        acc_sc[...] = jnp.zeros(acc_sc.shape, jnp.float32)

    is_short = j < n_short
    c = j - n_short
    first_row = i * TQ
    full = jnp.where(is_short, (j + 1) * TK <= short_len, c * TK + TK - 1 <= first_row)
    some = jnp.where(is_short, j * TK < short_len, c * TK <= first_row + TQ - 1)

    @pl.when(full)
    def _():
        _attend_block(q_ref, k_ref, v_ref, m_sc, l_sc, acc_sc, None)

    @pl.when(jnp.logical_and(some, jnp.logical_not(full)))
    def _():
        rows = lax.broadcasted_iota(jnp.int32, (TQ, TK), 0) + first_row
        keys = lax.broadcasted_iota(jnp.int32, (TQ, TK), 1)
        bound = jnp.where(is_short, short_len - j * TK, rows - c * TK + 1)
        valid = keys < bound
        _attend_block(q_ref, k_ref, v_ref, m_sc, l_sc, acc_sc, valid)

    @pl.when(j == nk - 1)
    def _():
        m_out[...] = m_sc[...]
        l_out[...] = l_sc[...]
        acc_out[...] = acc_sc[...]


def _long_kernel(sref, q_ref, k_ref, v_ref, m_in, l_in, acc_in, *rest, nk, finalize):
    j = pl.program_id(1)
    if finalize:
        o_ref, m_sc, l_sc, acc_sc = rest
    else:
        m_out, l_out, acc_out, m_sc, l_sc, acc_sc = rest

    @pl.when(j == 0)
    def _():
        m_sc[...] = m_in[...]
        l_sc[...] = l_in[...]
        acc_sc[...] = acc_in[...]

    @pl.when(sref[1] > 0)
    def _():
        _attend_block(q_ref, k_ref, v_ref, m_sc, l_sc, acc_sc, None)

    @pl.when(j == nk - 1)
    def _():
        if finalize:
            width = o_ref.shape[1]
            col = lax.broadcasted_iota(jnp.int32, (TQ, 128), 1)
            for pair in range(width // 128):
                cols = slice(pair * 128, (pair + 1) * 128)
                total = jnp.where(col < HEAD_DIM, l_sc[2 * pair], l_sc[2 * pair + 1])
                o_ref[:, cols] = (acc_sc[:, cols] / total).astype(o_ref.dtype)
        else:
            m_out[...] = m_sc[...]
            l_out[...] = l_sc[...]
            acc_out[...] = acc_sc[...]


def _cost(span, keys, width):
    heads = width // HEAD_DIM
    return pl.CostEstimate(
        flops=8 * span * keys * width,
        transcendentals=span * keys * heads,
        bytes_accessed=2 * keys * width * 2 * (span // TQ) + 16 * span * width,
    )


def local_attention(scalars, q, kv, n_short):
    span, width = q.shape
    heads = width // HEAD_DIM
    nq = span // TQ
    nk = kv.shape[0] // TK

    def kv_block(i, j, s):
        last_short = (s[0] - 1) // TK
        last_new = (i * TQ + TQ - 1) // TK
        return jnp.where(
            j < n_short, jnp.minimum(j, last_short), n_short + jnp.minimum(j - n_short, last_new)
        )

    stat_spec = pl.BlockSpec((heads, TQ, 128), lambda i, j, s: (0, i, 0))
    grid_spec = pltpu.PrefetchScalarGridSpec(
        num_scalar_prefetch=1,
        grid=(nq, nk),
        in_specs=[
            pl.BlockSpec((TQ, width), lambda i, j, s: (i, 0)),
            pl.BlockSpec((TK, width), lambda i, j, s: (kv_block(i, j, s), 0)),
            pl.BlockSpec((TK, width), lambda i, j, s: (kv_block(i, j, s), 1)),
        ],
        out_specs=[stat_spec, stat_spec, pl.BlockSpec((TQ, width), lambda i, j, s: (i, 0))],
        scratch_shapes=[
            pltpu.VMEM((heads, TQ, 128), jnp.float32),
            pltpu.VMEM((heads, TQ, 128), jnp.float32),
            pltpu.VMEM((TQ, width), jnp.float32),
        ],
    )
    return pl.pallas_call(
        functools.partial(_local_kernel, n_short=n_short, nk=nk),
        grid_spec=grid_spec,
        out_shape=[
            jax.ShapeDtypeStruct((heads, span, 128), jnp.float32),
            jax.ShapeDtypeStruct((heads, span, 128), jnp.float32),
            jax.ShapeDtypeStruct((span, width), jnp.float32),
        ],
        compiler_params=pltpu.CompilerParams(dimension_semantics=("arbitrary", "arbitrary")),
        cost_estimate=_cost(span, kv.shape[0], width),
    )(scalars, q, kv, kv)


def long_attention(scalars, q, kv, m, l, acc, finalize):
    span, width = q.shape
    heads = width // HEAD_DIM
    nq = span // TQ
    group = -(-TK // kv.shape[2])
    nk = kv.shape[0] // group
    stat_spec = pl.BlockSpec((heads, TQ, 128), lambda i, j, s: (0, i, 0))
    row_spec = pl.BlockSpec((TQ, width), lambda i, j, s: (i, 0))
    kv_shape = (group, None, kv.shape[2], width)
    if finalize:
        out_specs = row_spec
        out_shape = jax.ShapeDtypeStruct((span, width), jnp.bfloat16)
    else:
        out_specs = [stat_spec, stat_spec, row_spec]
        out_shape = [
            jax.ShapeDtypeStruct((heads, span, 128), jnp.float32),
            jax.ShapeDtypeStruct((heads, span, 128), jnp.float32),
            jax.ShapeDtypeStruct((span, width), jnp.float32),
        ]
    grid_spec = pltpu.PrefetchScalarGridSpec(
        num_scalar_prefetch=1,
        grid=(nq, nk),
        in_specs=[
            row_spec,
            pl.BlockSpec(kv_shape, lambda i, j, s: (j * s[1], 0, 0, 0)),
            pl.BlockSpec(kv_shape, lambda i, j, s: (j * s[1], 1, 0, 0)),
            stat_spec,
            stat_spec,
            row_spec,
        ],
        out_specs=out_specs,
        scratch_shapes=[
            pltpu.VMEM((heads, TQ, 128), jnp.float32),
            pltpu.VMEM((heads, TQ, 128), jnp.float32),
            pltpu.VMEM((TQ, width), jnp.float32),
        ],
    )
    return pl.pallas_call(
        functools.partial(_long_kernel, nk=nk, finalize=finalize),
        grid_spec=grid_spec,
        out_shape=out_shape,
        compiler_params=pltpu.CompilerParams(dimension_semantics=("arbitrary", "arbitrary")),
        cost_estimate=_cost(span, kv.shape[0] * kv.shape[2], width),
    )(scalars, q, kv, kv, m, l, acc)


def solution(mesh):
    n_req = mesh.shape["req"]

    def body(
        hidden_in,
        short_cache,
        long_cache,
        short_len,
        long_owner,
        w_qkv,
        b_qkv,
        w_out,
        b_out,
        w_in,
        b_in,
        w_down,
        b_down,
        norm_gain,
        norm_offset,
    ):
        n_long = long_cache.shape[0]
        long_ids = jnp.arange(n_long, dtype=jnp.int32)

        def which_long(request):
            owned = long_owner == request
            return jnp.sum(jnp.where(owned, long_ids, 0)), jnp.any(owned)

        me = lax.axis_index("req")
        my_long, has_long = which_long(me)
        requests = jnp.arange(n_req, dtype=jnp.int32)
        pick = long_owner[None, :] == requests[:, None]
        dest_long = jnp.sum(jnp.where(pick, long_ids[None, :], 0), axis=1)
        chosen = dest_long[:, None, None, None, None] == long_ids[None, :, None, None, None]
        by_kind = jnp.swapaxes(long_cache, 1, 2)[None]
        outgoing = jnp.max(jnp.where(chosen, by_kind, jnp.finfo(long_cache.dtype).min), axis=1)
        split = outgoing.shape[2] * 3 // 4
        first_part = lax.all_to_all(outgoing[:, :, :split], "req", 0, 0, tiled=True)

        w_out_full = lax.all_gather(w_out, "tp", axis=0, tiled=True)

        local_rows = hidden_in[0]
        factors = jnp.array([0.125, 1.0, 1.0], jnp.float32)[None, :, None]
        rows_all = lax.all_gather(local_rows, "tp", axis=0, tiled=True)
        mixed = jnp.einsum(
            "nd,cdk->nck",
            rows_all,
            w_qkv,
            preferred_element_type=jnp.float32,
        )
        projected = ((mixed + b_qkv[None]) * factors).astype(jnp.bfloat16)
        span_len = projected.shape[0]
        queries = projected[:, 0]
        new_kv = projected[None, :, 1:3]
        short_rows = short_cache[0]
        cache_len = short_rows.shape[0]
        local_kv = jnp.concatenate(
            [short_rows.reshape(cache_len, -1), projected[:, 1:3].reshape(span_len, -1)], axis=0
        )
        scalars = jnp.stack([short_len[0], has_long.astype(jnp.int32)])
        m, l, acc = local_attention(scalars, queries, local_kv, cache_len // TK)
        rest, m = lax.optimization_barrier((outgoing[:, :, split:], m))
        second_part = lax.all_to_all(rest, "req", 0, 0, tiled=True)
        m, l, acc = long_attention(scalars, queries, first_part, m, l, acc, False)
        context = long_attention(scalars, queries, second_part, m, l, acc, True)

        n_tp = mesh.shape["tp"]
        n_y = n_tp // 2
        block = span_len // n_tp
        core = lax.axis_index("tp") % 2
        chip = lax.axis_index("tp") // 2
        by_core = jnp.swapaxes(context.reshape(n_y, 2, block, context.shape[1]), 0, 1)
        outgoing_ctx = jnp.broadcast_to(by_core[None], (n_y,) + by_core.shape).reshape(
            (n_tp, n_y, block, context.shape[1])
        )
        got = lax.all_to_all(outgoing_ctx, "tp", 0, 0, tiled=True)
        class_ctx = jnp.transpose(got, (1, 2, 0, 3)).reshape(n_y * block, -1)
        class_rows = lax.dynamic_index_in_dim(
            rows_all.reshape(n_y, 2, block, rows_all.shape[1]), core, 1, keepdims=False
        ).reshape(n_y * block, -1)
        attended = jnp.dot(class_ctx, w_out_full, preferred_element_type=jnp.float32) + b_out
        class_normed = layer_norm(
            class_rows.astype(jnp.float32) + attended, norm_gain[0], norm_offset[0]
        ).astype(jnp.bfloat16).reshape(n_y, block, -1)
        normed = lax.dynamic_index_in_dim(class_normed, chip, 0, keepdims=False)
        sibling = [(k, k ^ 1) for k in range(n_tp)]
        halves_in = (w_in, lax.ppermute(w_in, "tp", sibling))
        halves_b = (b_in, lax.ppermute(b_in, "tp", sibling))
        halves_down = (w_down, lax.ppermute(w_down, "tp", sibling))

        def ffn_part(rows):
            total = None
            for w_a, b_a, w_b in zip(halves_in, halves_b, halves_down):
                units = jax.nn.gelu(
                    jnp.dot(rows, w_a, preferred_element_type=jnp.float32) + b_a,
                    approximate=False,
                ).astype(jnp.bfloat16)
                part = jnp.dot(units, w_b, preferred_element_type=jnp.float32)
                total = part if total is None else total + part
            return total

        own_rows = normed
        returned = []
        for step in range(1, n_y):
            ahead = [(k, (k + 2 * step) % n_tp) for k in range(n_tp)]
            behind = [(b, a) for a, b in ahead]
            peer_rows = lax.dynamic_index_in_dim(
                class_normed, (chip + n_y - step) % n_y, 0, keepdims=False
            )
            peer_part = ffn_part(peer_rows)
            own_rows, peer_part = lax.optimization_barrier((own_rows, peer_part))
            returned.append(lax.ppermute(peer_part.astype(jnp.bfloat16), "tp", behind))
        mixed = ffn_part(own_rows)
        mixed, returned = lax.optimization_barrier((mixed, returned))
        for part in returned:
            mixed = mixed + part.astype(jnp.float32)
        mixed = mixed + b_down
        hidden_out = layer_norm(
            normed.astype(jnp.float32) + mixed, norm_gain[1], norm_offset[1]
        ).astype(jnp.bfloat16)
        return (hidden_out[None], new_kv)

    return jax.shard_map(
        body,
        mesh=mesh,
        in_specs=(
            P("req", "tp", None),
            P("req", None, None, "tp"),
            P(None, "req", None, "tp"),
            P("req"),
            P(),
            P(None, None, "tp"),
            P(None, "tp"),
            P("tp", None),
            P(),
            P(None, "tp"),
            P("tp"),
            P("tp", None),
            P(),
            P(),
            P(),
        ),
        out_specs=(P("req", "tp", None), P("req", None, None, "tp")),
        check_vma=False,
    )
```

```python
import functools

import jax
import jax.numpy as jnp
from jax import lax
from jax.experimental import pallas as pl
from jax.experimental.pallas import tpu as pltpu
from jax.sharding import PartitionSpec as P

HEAD_DIM = 64
masked_score = -1e30
TQ = 512
TK = 512


def layer_norm(rows_in, gain, shift):
    center = rows_in - jnp.mean(rows_in, axis=-1, keepdims=True)
    spread = jnp.mean(center * center, axis=-1, keepdims=True)
    return center * lax.rsqrt(spread + 1e-05) * gain + shift


def _attend_block(q_ref, k_ref, v_ref, m_sc, l_sc, acc_sc, valid):
    width = q_ref.shape[1]
    col = lax.broadcasted_iota(jnp.int32, (q_ref.shape[0], 128), 1)
    low = col < HEAD_DIM
    for pair in range(width // 128):
        cols = slice(pair * 128, (pair + 1) * 128)
        q2 = q_ref[:, cols]
        k2 = k_ref[..., cols].reshape(-1, 128)
        v2 = v_ref[..., cols].reshape(-1, 128)
        alphas = []
        pvs = []
        for half in range(2):
            h = pair * 2 + half
            qh = jnp.where(low if half == 0 else jnp.logical_not(low), q2, jnp.zeros_like(q2))
            s = lax.dot_general(
                qh, k2, (((1,), (1,)), ((), ())), preferred_element_type=jnp.float32
            )
            if valid is not None:
                s = jnp.where(valid, s, masked_score)
            m_prev = m_sc[h]
            m_new = jnp.maximum(m_prev, jnp.max(s, axis=1, keepdims=True))
            alpha = jnp.exp(m_prev - m_new)
            p = jnp.exp(s - m_new[:, 0:1])
            l_sc[h] = alpha * l_sc[h] + jnp.sum(p, axis=1, keepdims=True)
            m_sc[h] = m_new
            pvs.append(jnp.dot(p.astype(jnp.bfloat16), v2, preferred_element_type=jnp.float32))
            alphas.append(alpha)
        alpha2 = jnp.where(low, alphas[0], alphas[1])
        acc_sc[:, cols] = alpha2 * acc_sc[:, cols] + jnp.where(low, pvs[0], pvs[1])


def _local_kernel(sref, q_ref, k_ref, v_ref, m_out, l_out, acc_out, m_sc, l_sc, acc_sc, *, n_short, nk):
    i = pl.program_id(0)
    j = pl.program_id(1)
    short_len = sref[0]

    @pl.when(j == 0)
    def _():
        m_sc[...] = jnp.full(m_sc.shape, masked_score, jnp.float32)
        l_sc[...] = jnp.zeros(l_sc.shape, jnp.float32)
        acc_sc[...] = jnp.zeros(acc_sc.shape, jnp.float32)

    is_short = j < n_short
    c = j - n_short
    first_row = i * TQ
    full = jnp.where(is_short, (j + 1) * TK <= short_len, c * TK + TK - 1 <= first_row)
    some = jnp.where(is_short, j * TK < short_len, c * TK <= first_row + TQ - 1)

    @pl.when(full)
    def _():
        _attend_block(q_ref, k_ref, v_ref, m_sc, l_sc, acc_sc, None)

    @pl.when(jnp.logical_and(some, jnp.logical_not(full)))
    def _():
        rows = lax.broadcasted_iota(jnp.int32, (TQ, TK), 0) + first_row
        keys = lax.broadcasted_iota(jnp.int32, (TQ, TK), 1)
        bound = jnp.where(is_short, short_len - j * TK, rows - c * TK + 1)
        valid = keys < bound
        _attend_block(q_ref, k_ref, v_ref, m_sc, l_sc, acc_sc, valid)

    @pl.when(j == nk - 1)
    def _():
        m_out[...] = m_sc[...]
        l_out[...] = l_sc[...]
        acc_out[...] = acc_sc[...]


def _long_kernel(sref, q_ref, k_ref, v_ref, m_in, l_in, acc_in, *rest, nk, finalize):
    j = pl.program_id(1)
    if finalize:
        o_ref, m_sc, l_sc, acc_sc = rest
    else:
        m_out, l_out, acc_out, m_sc, l_sc, acc_sc = rest

    @pl.when(j == 0)
    def _():
        m_sc[...] = m_in[...]
        l_sc[...] = l_in[...]
        acc_sc[...] = acc_in[...]

    @pl.when(sref[1] > 0)
    def _():
        _attend_block(q_ref, k_ref, v_ref, m_sc, l_sc, acc_sc, None)

    @pl.when(j == nk - 1)
    def _():
        if finalize:
            width = o_ref.shape[1]
            col = lax.broadcasted_iota(jnp.int32, (TQ, 128), 1)
            for pair in range(width // 128):
                cols = slice(pair * 128, (pair + 1) * 128)
                total = jnp.where(col < HEAD_DIM, l_sc[2 * pair], l_sc[2 * pair + 1])
                o_ref[:, cols] = (acc_sc[:, cols] / total).astype(o_ref.dtype)
        else:
            m_out[...] = m_sc[...]
            l_out[...] = l_sc[...]
            acc_out[...] = acc_sc[...]


def _cost(span, keys, width):
    heads = width // HEAD_DIM
    return pl.CostEstimate(
        flops=8 * span * keys * width,
        transcendentals=span * keys * heads,
        bytes_accessed=2 * keys * width * 2 * (span // TQ) + 16 * span * width,
    )


def local_attention(scalars, q, kv, n_short):
    span, width = q.shape
    heads = width // HEAD_DIM
    nq = span // TQ
    nk = kv.shape[0] // TK

    def kv_block(i, j, s):
        last_short = (s[0] - 1) // TK
        last_new = (i * TQ + TQ - 1) // TK
        return jnp.where(
            j < n_short, jnp.minimum(j, last_short), n_short + jnp.minimum(j - n_short, last_new)
        )

    stat_spec = pl.BlockSpec((heads, TQ, 128), lambda i, j, s: (0, i, 0))
    grid_spec = pltpu.PrefetchScalarGridSpec(
        num_scalar_prefetch=1,
        grid=(nq, nk),
        in_specs=[
            pl.BlockSpec((TQ, width), lambda i, j, s: (i, 0)),
            pl.BlockSpec((TK, width), lambda i, j, s: (kv_block(i, j, s), 0)),
            pl.BlockSpec((TK, width), lambda i, j, s: (kv_block(i, j, s), 1)),
        ],
        out_specs=[stat_spec, stat_spec, pl.BlockSpec((TQ, width), lambda i, j, s: (i, 0))],
        scratch_shapes=[
            pltpu.VMEM((heads, TQ, 128), jnp.float32),
            pltpu.VMEM((heads, TQ, 128), jnp.float32),
            pltpu.VMEM((TQ, width), jnp.float32),
        ],
    )
    return pl.pallas_call(
        functools.partial(_local_kernel, n_short=n_short, nk=nk),
        grid_spec=grid_spec,
        out_shape=[
            jax.ShapeDtypeStruct((heads, span, 128), jnp.float32),
            jax.ShapeDtypeStruct((heads, span, 128), jnp.float32),
            jax.ShapeDtypeStruct((span, width), jnp.float32),
        ],
        compiler_params=pltpu.CompilerParams(dimension_semantics=("arbitrary", "arbitrary")),
        cost_estimate=_cost(span, kv.shape[0], width),
    )(scalars, q, kv, kv)


def long_attention(scalars, q, kv, m, l, acc, finalize):
    span, width = q.shape
    heads = width // HEAD_DIM
    nq = span // TQ
    group = -(-TK // kv.shape[2])
    nk = kv.shape[0] // group
    stat_spec = pl.BlockSpec((heads, TQ, 128), lambda i, j, s: (0, i, 0))
    row_spec = pl.BlockSpec((TQ, width), lambda i, j, s: (i, 0))
    kv_shape = (group, None, kv.shape[2], width)
    if finalize:
        out_specs = row_spec
        out_shape = jax.ShapeDtypeStruct((span, width), jnp.bfloat16)
    else:
        out_specs = [stat_spec, stat_spec, row_spec]
        out_shape = [
            jax.ShapeDtypeStruct((heads, span, 128), jnp.float32),
            jax.ShapeDtypeStruct((heads, span, 128), jnp.float32),
            jax.ShapeDtypeStruct((span, width), jnp.float32),
        ]
    grid_spec = pltpu.PrefetchScalarGridSpec(
        num_scalar_prefetch=1,
        grid=(nq, nk),
        in_specs=[
            row_spec,
            pl.BlockSpec(kv_shape, lambda i, j, s: (j * s[1], 0, 0, 0)),
            pl.BlockSpec(kv_shape, lambda i, j, s: (j * s[1], 1, 0, 0)),
            stat_spec,
            stat_spec,
            row_spec,
        ],
        out_specs=out_specs,
        scratch_shapes=[
            pltpu.VMEM((heads, TQ, 128), jnp.float32),
            pltpu.VMEM((heads, TQ, 128), jnp.float32),
            pltpu.VMEM((TQ, width), jnp.float32),
        ],
    )
    return pl.pallas_call(
        functools.partial(_long_kernel, nk=nk, finalize=finalize),
        grid_spec=grid_spec,
        out_shape=out_shape,
        compiler_params=pltpu.CompilerParams(dimension_semantics=("arbitrary", "arbitrary")),
        cost_estimate=_cost(span, kv.shape[0] * kv.shape[2], width),
    )(scalars, q, kv, kv, m, l, acc)


def solution(mesh):
    n_req = mesh.shape["req"]

    def body(
        hidden_in,
        short_cache,
        long_cache,
        short_len,
        long_owner,
        w_qkv,
        b_qkv,
        w_out,
        b_out,
        w_in,
        b_in,
        w_down,
        b_down,
        norm_gain,
        norm_offset,
    ):
        n_long = long_cache.shape[0]
        long_ids = jnp.arange(n_long, dtype=jnp.int32)

        def which_long(request):
            owned = long_owner == request
            return jnp.sum(jnp.where(owned, long_ids, 0)), jnp.any(owned)

        me = lax.axis_index("req")
        my_long, has_long = which_long(me)
        requests = jnp.arange(n_req, dtype=jnp.int32)
        pick = long_owner[None, :] == requests[:, None]
        dest_long = jnp.sum(jnp.where(pick, long_ids[None, :], 0), axis=1)
        chosen = dest_long[:, None, None, None, None] == long_ids[None, :, None, None, None]
        by_kind = jnp.swapaxes(long_cache, 1, 2)[None]
        outgoing = jnp.max(jnp.where(chosen, by_kind, jnp.finfo(long_cache.dtype).min), axis=1)
        split = outgoing.shape[2] * 3 // 4
        first_part = lax.all_to_all(outgoing[:, :, :split], "req", 0, 0, tiled=True)

        n_tp = mesh.shape["tp"]

        def tp_gather(x):
            me_tp = lax.axis_index("tp")
            out = jnp.zeros((n_tp,) + x.shape, x.dtype)
            out = lax.dynamic_update_index_in_dim(out, x, me_tp, 0)
            for shift in range(1, n_tp):
                got = lax.ppermute(x, "tp", [(k, (k + shift) % n_tp) for k in range(n_tp)])
                out = lax.dynamic_update_index_in_dim(out, got, (me_tp + n_tp - shift) % n_tp, 0)
            return out.reshape((-1,) + x.shape[1:])

        w_out_full = tp_gather(w_out)

        local_rows = hidden_in[0]
        factors = jnp.array([0.125, 1.0, 1.0], jnp.float32)[None, :, None]
        rows_all = tp_gather(local_rows)
        mixed = jnp.einsum(
            "nd,cdk->nck",
            rows_all,
            w_qkv,
            preferred_element_type=jnp.float32,
        )
        projected = ((mixed + b_qkv[None]) * factors).astype(jnp.bfloat16)
        span_len = projected.shape[0]
        queries = projected[:, 0]
        new_kv = projected[None, :, 1:3]
        short_rows = short_cache[0]
        cache_len = short_rows.shape[0]
        local_kv = jnp.concatenate(
            [short_rows.reshape(cache_len, -1), projected[:, 1:3].reshape(span_len, -1)], axis=0
        )
        scalars = jnp.stack([short_len[0], has_long.astype(jnp.int32)])
        m, l, acc = local_attention(scalars, queries, local_kv, cache_len // TK)
        rest, m = lax.optimization_barrier((outgoing[:, :, split:], m))
        second_part = lax.all_to_all(rest, "req", 0, 0, tiled=True)
        m, l, acc = long_attention(scalars, queries, first_part, m, l, acc, False)
        context = long_attention(scalars, queries, second_part, m, l, acc, True)

        n_y = n_tp // 2
        block = span_len // n_tp
        core = lax.axis_index("tp") % 2
        chip = lax.axis_index("tp") // 2
        by_core = jnp.swapaxes(context.reshape(n_y, 2, block, context.shape[1]), 0, 1)
        outgoing_ctx = jnp.broadcast_to(by_core[None], (n_y,) + by_core.shape).reshape(
            (n_tp, n_y, block, context.shape[1])
        )
        got = lax.all_to_all(outgoing_ctx, "tp", 0, 0, tiled=True)
        class_ctx = jnp.transpose(got, (1, 2, 0, 3)).reshape(n_y * block, -1)
        class_rows = lax.dynamic_index_in_dim(
            rows_all.reshape(n_y, 2, block, rows_all.shape[1]), core, 1, keepdims=False
        ).reshape(n_y * block, -1)
        attended = jnp.dot(class_ctx, w_out_full, preferred_element_type=jnp.float32) + b_out
        class_normed = layer_norm(
            class_rows.astype(jnp.float32) + attended, norm_gain[0], norm_offset[0]
        ).astype(jnp.bfloat16).reshape(n_y, block, -1)
        normed = lax.dynamic_index_in_dim(class_normed, chip, 0, keepdims=False)
        sibling = [(k, k ^ 1) for k in range(n_tp)]
        halves_in = (w_in, lax.ppermute(w_in, "tp", sibling))
        halves_b = (b_in, lax.ppermute(b_in, "tp", sibling))
        halves_down = (w_down, lax.ppermute(w_down, "tp", sibling))

        def ffn_part(rows):
            total = None
            for w_a, b_a, w_b in zip(halves_in, halves_b, halves_down):
                units = jax.nn.gelu(
                    jnp.dot(rows, w_a, preferred_element_type=jnp.float32) + b_a,
                    approximate=False,
                ).astype(jnp.bfloat16)
                part = jnp.dot(units, w_b, preferred_element_type=jnp.float32)
                total = part if total is None else total + part
            return total

        own_rows = normed
        returned = []
        for step in range(1, n_y):
            ahead = [(k, (k + 2 * step) % n_tp) for k in range(n_tp)]
            behind = [(b, a) for a, b in ahead]
            peer_rows = lax.dynamic_index_in_dim(
                class_normed, (chip + n_y - step) % n_y, 0, keepdims=False
            )
            peer_part = ffn_part(peer_rows)
            own_rows, peer_part = lax.optimization_barrier((own_rows, peer_part))
            returned.append(lax.ppermute(peer_part.astype(jnp.bfloat16), "tp", behind))
        mixed = ffn_part(own_rows)
        mixed, returned = lax.optimization_barrier((mixed, returned))
        for part in returned:
            mixed = mixed + part.astype(jnp.float32)
        mixed = mixed + b_down
        hidden_out = layer_norm(
            normed.astype(jnp.float32) + mixed, norm_gain[1], norm_offset[1]
        ).astype(jnp.bfloat16)
        return (hidden_out[None], new_kv)

    return jax.shard_map(
        body,
        mesh=mesh,
        in_specs=(
            P("req", "tp", None),
            P("req", None, None, "tp"),
            P(None, "req", None, "tp"),
            P("req"),
            P(),
            P(None, None, "tp"),
            P(None, "tp"),
            P("tp", None),
            P(),
            P(None, "tp"),
            P("tp"),
            P("tp", None),
            P(),
            P(),
            P(),
        ),
        out_specs=(P("req", "tp", None), P("req", None, None, "tp")),
        check_vma=False,
    )
```

```python
import functools

import jax
import jax.numpy as jnp
from jax import lax
from jax.experimental import pallas as pl
from jax.experimental.pallas import tpu as pltpu
from jax.sharding import PartitionSpec as P

HEAD_DIM = 64
masked_score = -1e30
TQ = 512
TK = 512


def layer_norm(rows_in, gain, shift):
    center = rows_in - jnp.mean(rows_in, axis=-1, keepdims=True)
    spread = jnp.mean(center * center, axis=-1, keepdims=True)
    return center * lax.rsqrt(spread + 1e-05) * gain + shift


def _attend_block(q_ref, k_ref, v_ref, m_sc, l_sc, acc_sc, valid):
    width = q_ref.shape[1]
    col = lax.broadcasted_iota(jnp.int32, (q_ref.shape[0], 128), 1)
    low = col < HEAD_DIM
    for pair in range(width // 128):
        cols = slice(pair * 128, (pair + 1) * 128)
        q2 = q_ref[:, cols]
        k2 = k_ref[..., cols].reshape(-1, 128)
        v2 = v_ref[..., cols].reshape(-1, 128)
        alphas = []
        pvs = []
        for half in range(2):
            h = pair * 2 + half
            qh = jnp.where(low if half == 0 else jnp.logical_not(low), q2, jnp.zeros_like(q2))
            s = lax.dot_general(
                qh, k2, (((1,), (1,)), ((), ())), preferred_element_type=jnp.float32
            )
            if valid is not None:
                s = jnp.where(valid, s, masked_score)
            m_prev = m_sc[h]
            m_new = jnp.maximum(m_prev, jnp.max(s, axis=1, keepdims=True))
            alpha = jnp.exp(m_prev - m_new)
            p = jnp.exp(s - m_new[:, 0:1])
            l_sc[h] = alpha * l_sc[h] + jnp.sum(p, axis=1, keepdims=True)
            m_sc[h] = m_new
            pvs.append(jnp.dot(p.astype(jnp.bfloat16), v2, preferred_element_type=jnp.float32))
            alphas.append(alpha)
        alpha2 = jnp.where(low, alphas[0], alphas[1])
        acc_sc[:, cols] = alpha2 * acc_sc[:, cols] + jnp.where(low, pvs[0], pvs[1])


def _local_kernel(sref, q_ref, k_ref, v_ref, m_out, l_out, acc_out, m_sc, l_sc, acc_sc, *, n_short, nk):
    i = pl.program_id(0)
    j = pl.program_id(1)
    short_len = sref[0]

    @pl.when(j == 0)
    def _():
        m_sc[...] = jnp.full(m_sc.shape, masked_score, jnp.float32)
        l_sc[...] = jnp.zeros(l_sc.shape, jnp.float32)
        acc_sc[...] = jnp.zeros(acc_sc.shape, jnp.float32)

    is_short = j < n_short
    c = j - n_short
    first_row = i * TQ
    full = jnp.where(is_short, (j + 1) * TK <= short_len, c * TK + TK - 1 <= first_row)
    some = jnp.where(is_short, j * TK < short_len, c * TK <= first_row + TQ - 1)

    @pl.when(full)
    def _():
        _attend_block(q_ref, k_ref, v_ref, m_sc, l_sc, acc_sc, None)

    @pl.when(jnp.logical_and(some, jnp.logical_not(full)))
    def _():
        rows = lax.broadcasted_iota(jnp.int32, (TQ, TK), 0) + first_row
        keys = lax.broadcasted_iota(jnp.int32, (TQ, TK), 1)
        bound = jnp.where(is_short, short_len - j * TK, rows - c * TK + 1)
        valid = keys < bound
        _attend_block(q_ref, k_ref, v_ref, m_sc, l_sc, acc_sc, valid)

    @pl.when(j == nk - 1)
    def _():
        m_out[...] = m_sc[...]
        l_out[...] = l_sc[...]
        acc_out[...] = acc_sc[...]


def _long_kernel(sref, q_ref, k_ref, v_ref, m_in, l_in, acc_in, *rest, nk, finalize):
    j = pl.program_id(1)
    if finalize:
        o_ref, m_sc, l_sc, acc_sc = rest
    else:
        m_out, l_out, acc_out, m_sc, l_sc, acc_sc = rest

    @pl.when(j == 0)
    def _():
        m_sc[...] = m_in[...]
        l_sc[...] = l_in[...]
        acc_sc[...] = acc_in[...]

    @pl.when(sref[1] > 0)
    def _():
        _attend_block(q_ref, k_ref, v_ref, m_sc, l_sc, acc_sc, None)

    @pl.when(j == nk - 1)
    def _():
        if finalize:
            width = o_ref.shape[1]
            col = lax.broadcasted_iota(jnp.int32, (TQ, 128), 1)
            for pair in range(width // 128):
                cols = slice(pair * 128, (pair + 1) * 128)
                total = jnp.where(col < HEAD_DIM, l_sc[2 * pair], l_sc[2 * pair + 1])
                o_ref[:, cols] = (acc_sc[:, cols] / total).astype(o_ref.dtype)
        else:
            m_out[...] = m_sc[...]
            l_out[...] = l_sc[...]
            acc_out[...] = acc_sc[...]


def _cost(span, keys, width):
    heads = width // HEAD_DIM
    return pl.CostEstimate(
        flops=8 * span * keys * width,
        transcendentals=span * keys * heads,
        bytes_accessed=2 * keys * width * 2 * (span // TQ) + 16 * span * width,
    )


def local_attention(scalars, q, kv, n_short):
    span, width = q.shape
    heads = width // HEAD_DIM
    nq = span // TQ
    nk = kv.shape[0] // TK

    def kv_block(i, j, s):
        last_short = (s[0] - 1) // TK
        last_new = (i * TQ + TQ - 1) // TK
        return jnp.where(
            j < n_short, jnp.minimum(j, last_short), n_short + jnp.minimum(j - n_short, last_new)
        )

    stat_spec = pl.BlockSpec((heads, TQ, 128), lambda i, j, s: (0, i, 0))
    grid_spec = pltpu.PrefetchScalarGridSpec(
        num_scalar_prefetch=1,
        grid=(nq, nk),
        in_specs=[
            pl.BlockSpec((TQ, width), lambda i, j, s: (i, 0)),
            pl.BlockSpec((TK, width), lambda i, j, s: (kv_block(i, j, s), 0)),
            pl.BlockSpec((TK, width), lambda i, j, s: (kv_block(i, j, s), 1)),
        ],
        out_specs=[stat_spec, stat_spec, pl.BlockSpec((TQ, width), lambda i, j, s: (i, 0))],
        scratch_shapes=[
            pltpu.VMEM((heads, TQ, 128), jnp.float32),
            pltpu.VMEM((heads, TQ, 128), jnp.float32),
            pltpu.VMEM((TQ, width), jnp.float32),
        ],
    )
    return pl.pallas_call(
        functools.partial(_local_kernel, n_short=n_short, nk=nk),
        grid_spec=grid_spec,
        out_shape=[
            jax.ShapeDtypeStruct((heads, span, 128), jnp.float32),
            jax.ShapeDtypeStruct((heads, span, 128), jnp.float32),
            jax.ShapeDtypeStruct((span, width), jnp.float32),
        ],
        compiler_params=pltpu.CompilerParams(dimension_semantics=("arbitrary", "arbitrary")),
        cost_estimate=_cost(span, kv.shape[0], width),
    )(scalars, q, kv, kv)


def long_attention(scalars, q, kv, m, l, acc, finalize):
    span, width = q.shape
    heads = width // HEAD_DIM
    nq = span // TQ
    group = -(-TK // kv.shape[2])
    nk = kv.shape[0] // group
    stat_spec = pl.BlockSpec((heads, TQ, 128), lambda i, j, s: (0, i, 0))
    row_spec = pl.BlockSpec((TQ, width), lambda i, j, s: (i, 0))
    kv_shape = (group, None, kv.shape[2], width)
    if finalize:
        out_specs = row_spec
        out_shape = jax.ShapeDtypeStruct((span, width), jnp.bfloat16)
    else:
        out_specs = [stat_spec, stat_spec, row_spec]
        out_shape = [
            jax.ShapeDtypeStruct((heads, span, 128), jnp.float32),
            jax.ShapeDtypeStruct((heads, span, 128), jnp.float32),
            jax.ShapeDtypeStruct((span, width), jnp.float32),
        ]
    grid_spec = pltpu.PrefetchScalarGridSpec(
        num_scalar_prefetch=1,
        grid=(nq, nk),
        in_specs=[
            row_spec,
            pl.BlockSpec(kv_shape, lambda i, j, s: (j * s[1], 0, 0, 0)),
            pl.BlockSpec(kv_shape, lambda i, j, s: (j * s[1], 1, 0, 0)),
            stat_spec,
            stat_spec,
            row_spec,
        ],
        out_specs=out_specs,
        scratch_shapes=[
            pltpu.VMEM((heads, TQ, 128), jnp.float32),
            pltpu.VMEM((heads, TQ, 128), jnp.float32),
            pltpu.VMEM((TQ, width), jnp.float32),
        ],
    )
    return pl.pallas_call(
        functools.partial(_long_kernel, nk=nk, finalize=finalize),
        grid_spec=grid_spec,
        out_shape=out_shape,
        compiler_params=pltpu.CompilerParams(dimension_semantics=("arbitrary", "arbitrary")),
        cost_estimate=_cost(span, kv.shape[0] * kv.shape[2], width),
    )(scalars, q, kv, kv, m, l, acc)


def solution(mesh):
    n_req = mesh.shape["req"]

    def body(
        hidden_in,
        short_cache,
        long_cache,
        short_len,
        long_owner,
        w_qkv,
        b_qkv,
        w_out,
        b_out,
        w_in,
        b_in,
        w_down,
        b_down,
        norm_gain,
        norm_offset,
    ):
        n_long = long_cache.shape[0]
        long_ids = jnp.arange(n_long, dtype=jnp.int32)

        def which_long(request):
            owned = long_owner == request
            return jnp.sum(jnp.where(owned, long_ids, 0)), jnp.any(owned)

        me = lax.axis_index("req")
        my_long, has_long = which_long(me)
        requests = jnp.arange(n_req, dtype=jnp.int32)
        pick = long_owner[None, :] == requests[:, None]
        dest_long = jnp.sum(jnp.where(pick, long_ids[None, :], 0), axis=1)
        chosen = dest_long[:, None, None, None, None] == long_ids[None, :, None, None, None]
        split = long_cache.shape[1] * 3 // 4

        def send_buffer(lo, hi):
            by_kind = jnp.swapaxes(long_cache[:, lo:hi], 1, 2)[None]
            return jnp.max(jnp.where(chosen, by_kind, jnp.finfo(long_cache.dtype).min), axis=1)

        first_part = lax.all_to_all(send_buffer(0, split), "req", 0, 0, tiled=True)

        n_tp = mesh.shape["tp"]

        def tp_gather(x):
            me_tp = lax.axis_index("tp")
            out = jnp.zeros((n_tp,) + x.shape, x.dtype)
            out = lax.dynamic_update_index_in_dim(out, x, me_tp, 0)
            for shift in range(1, n_tp):
                got = lax.ppermute(x, "tp", [(k, (k + shift) % n_tp) for k in range(n_tp)])
                out = lax.dynamic_update_index_in_dim(out, got, (me_tp + n_tp - shift) % n_tp, 0)
            return out.reshape((-1,) + x.shape[1:])

        w_out_full = tp_gather(w_out)

        local_rows = hidden_in[0]
        factors = jnp.array([0.125, 1.0, 1.0], jnp.float32)[None, :, None]
        rows_all = tp_gather(local_rows)
        mixed = jnp.einsum(
            "nd,cdk->nck",
            rows_all,
            w_qkv,
            preferred_element_type=jnp.float32,
        )
        projected = ((mixed + b_qkv[None]) * factors).astype(jnp.bfloat16)
        span_len = projected.shape[0]
        queries = projected[:, 0]
        new_kv = projected[None, :, 1:3]
        short_rows = short_cache[0]
        cache_len = short_rows.shape[0]
        local_kv = jnp.concatenate(
            [short_rows.reshape(cache_len, -1), projected[:, 1:3].reshape(span_len, -1)], axis=0
        )
        scalars = jnp.stack([short_len[0], has_long.astype(jnp.int32)])
        m, l, acc = local_attention(scalars, queries, local_kv, cache_len // TK)
        rest, m = lax.optimization_barrier((send_buffer(split, long_cache.shape[1]), m))
        second_part = lax.all_to_all(rest, "req", 0, 0, tiled=True)
        m, l, acc = long_attention(scalars, queries, first_part, m, l, acc, False)
        context = long_attention(scalars, queries, second_part, m, l, acc, True)

        n_y = n_tp // 2
        block = span_len // n_tp
        core = lax.axis_index("tp") % 2
        chip = lax.axis_index("tp") // 2
        by_core = jnp.swapaxes(context.reshape(n_y, 2, block, context.shape[1]), 0, 1)
        outgoing_ctx = jnp.broadcast_to(by_core[None], (n_y,) + by_core.shape).reshape(
            (n_tp, n_y, block, context.shape[1])
        )
        got = lax.all_to_all(outgoing_ctx, "tp", 0, 0, tiled=True)
        class_ctx = jnp.transpose(got, (1, 2, 0, 3)).reshape(n_y * block, -1)
        class_rows = lax.dynamic_index_in_dim(
            rows_all.reshape(n_y, 2, block, rows_all.shape[1]), core, 1, keepdims=False
        ).reshape(n_y * block, -1)
        attended = jnp.dot(class_ctx, w_out_full, preferred_element_type=jnp.float32) + b_out
        class_normed = layer_norm(
            class_rows.astype(jnp.float32) + attended, norm_gain[0], norm_offset[0]
        ).astype(jnp.bfloat16).reshape(n_y, block, -1)
        normed = lax.dynamic_index_in_dim(class_normed, chip, 0, keepdims=False)
        sibling = [(k, k ^ 1) for k in range(n_tp)]
        halves_in = (w_in, lax.ppermute(w_in, "tp", sibling))
        halves_b = (b_in, lax.ppermute(b_in, "tp", sibling))
        halves_down = (w_down, lax.ppermute(w_down, "tp", sibling))

        def ffn_part(rows):
            total = None
            for w_a, b_a, w_b in zip(halves_in, halves_b, halves_down):
                units = jax.nn.gelu(
                    jnp.dot(rows, w_a, preferred_element_type=jnp.float32) + b_a,
                    approximate=False,
                ).astype(jnp.bfloat16)
                part = jnp.dot(units, w_b, preferred_element_type=jnp.float32)
                total = part if total is None else total + part
            return total

        own_rows = normed
        returned = []
        for step in range(1, n_y):
            ahead = [(k, (k + 2 * step) % n_tp) for k in range(n_tp)]
            behind = [(b, a) for a, b in ahead]
            peer_rows = lax.dynamic_index_in_dim(
                class_normed, (chip + n_y - step) % n_y, 0, keepdims=False
            )
            peer_part = ffn_part(peer_rows)
            own_rows, peer_part = lax.optimization_barrier((own_rows, peer_part))
            returned.append(lax.ppermute(peer_part.astype(jnp.bfloat16), "tp", behind))
        mixed = ffn_part(own_rows)
        mixed, returned = lax.optimization_barrier((mixed, returned))
        for part in returned:
            mixed = mixed + part.astype(jnp.float32)
        mixed = mixed + b_down
        hidden_out = layer_norm(
            normed.astype(jnp.float32) + mixed, norm_gain[1], norm_offset[1]
        ).astype(jnp.bfloat16)
        return (hidden_out[None], new_kv)

    return jax.shard_map(
        body,
        mesh=mesh,
        in_specs=(
            P("req", "tp", None),
            P("req", None, None, "tp"),
            P(None, "req", None, "tp"),
            P("req"),
            P(),
            P(None, None, "tp"),
            P(None, "tp"),
            P("tp", None),
            P(),
            P(None, "tp"),
            P("tp"),
            P("tp", None),
            P(),
            P(),
            P(),
        ),
        out_specs=(P("req", "tp", None), P("req", None, None, "tp")),
        check_vma=False,
    )
```

```python
import functools

import jax
import jax.numpy as jnp
from jax import lax
from jax.experimental import pallas as pl
from jax.experimental.pallas import tpu as pltpu
from jax.sharding import PartitionSpec as P

HEAD_DIM = 64
masked_score = -1e30
TQ = 512
TK = 512


def layer_norm(rows_in, gain, shift):
    center = rows_in - jnp.mean(rows_in, axis=-1, keepdims=True)
    spread = jnp.mean(center * center, axis=-1, keepdims=True)
    return center * lax.rsqrt(spread + 1e-05) * gain + shift


def _attend_block(q_ref, k_ref, v_ref, m_sc, l_sc, acc_sc, valid):
    width = q_ref.shape[1]
    col = lax.broadcasted_iota(jnp.int32, (q_ref.shape[0], 128), 1)
    low = col < HEAD_DIM
    for pair in range(width // 128):
        cols = slice(pair * 128, (pair + 1) * 128)
        q2 = q_ref[:, cols]
        k2 = k_ref[..., cols].reshape(-1, 128)
        v2 = v_ref[..., cols].reshape(-1, 128)
        alphas = []
        pvs = []
        for half in range(2):
            h = pair * 2 + half
            qh = jnp.where(low if half == 0 else jnp.logical_not(low), q2, jnp.zeros_like(q2))
            s = lax.dot_general(
                qh, k2, (((1,), (1,)), ((), ())), preferred_element_type=jnp.float32
            )
            if valid is not None:
                s = jnp.where(valid, s, masked_score)
            m_prev = m_sc[h]
            m_new = jnp.maximum(m_prev, jnp.max(s, axis=1, keepdims=True))
            alpha = jnp.exp(m_prev - m_new)
            p = jnp.exp(s - m_new[:, 0:1])
            l_sc[h] = alpha * l_sc[h] + jnp.sum(p, axis=1, keepdims=True)
            m_sc[h] = m_new
            pvs.append(jnp.dot(p.astype(jnp.bfloat16), v2, preferred_element_type=jnp.float32))
            alphas.append(alpha)
        alpha2 = jnp.where(low, alphas[0], alphas[1])
        acc_sc[:, cols] = alpha2 * acc_sc[:, cols] + jnp.where(low, pvs[0], pvs[1])


def _local_kernel(sref, q_ref, k_ref, v_ref, m_out, l_out, acc_out, m_sc, l_sc, acc_sc, *, n_short, nk):
    i = pl.program_id(0)
    j = pl.program_id(1)
    short_len = sref[0]

    @pl.when(j == 0)
    def _():
        m_sc[...] = jnp.full(m_sc.shape, masked_score, jnp.float32)
        l_sc[...] = jnp.zeros(l_sc.shape, jnp.float32)
        acc_sc[...] = jnp.zeros(acc_sc.shape, jnp.float32)

    is_short = j < n_short
    c = j - n_short
    first_row = i * TQ
    full = jnp.where(is_short, (j + 1) * TK <= short_len, c * TK + TK - 1 <= first_row)
    some = jnp.where(is_short, j * TK < short_len, c * TK <= first_row + TQ - 1)

    @pl.when(full)
    def _():
        _attend_block(q_ref, k_ref, v_ref, m_sc, l_sc, acc_sc, None)

    @pl.when(jnp.logical_and(some, jnp.logical_not(full)))
    def _():
        rows = lax.broadcasted_iota(jnp.int32, (TQ, TK), 0) + first_row
        keys = lax.broadcasted_iota(jnp.int32, (TQ, TK), 1)
        bound = jnp.where(is_short, short_len - j * TK, rows - c * TK + 1)
        valid = keys < bound
        _attend_block(q_ref, k_ref, v_ref, m_sc, l_sc, acc_sc, valid)

    @pl.when(j == nk - 1)
    def _():
        m_out[...] = m_sc[...]
        l_out[...] = l_sc[...]
        acc_out[...] = acc_sc[...]


def _long_kernel(sref, q_ref, k_ref, v_ref, m_in, l_in, acc_in, *rest, nk, finalize):
    j = pl.program_id(1)
    if finalize:
        o_ref, m_sc, l_sc, acc_sc = rest
    else:
        m_out, l_out, acc_out, m_sc, l_sc, acc_sc = rest

    @pl.when(j == 0)
    def _():
        m_sc[...] = m_in[...]
        l_sc[...] = l_in[...]
        acc_sc[...] = acc_in[...]

    @pl.when(sref[1] > 0)
    def _():
        _attend_block(q_ref, k_ref, v_ref, m_sc, l_sc, acc_sc, None)

    @pl.when(j == nk - 1)
    def _():
        if finalize:
            width = o_ref.shape[1]
            col = lax.broadcasted_iota(jnp.int32, (TQ, 128), 1)
            for pair in range(width // 128):
                cols = slice(pair * 128, (pair + 1) * 128)
                total = jnp.where(col < HEAD_DIM, l_sc[2 * pair], l_sc[2 * pair + 1])
                o_ref[:, cols] = (acc_sc[:, cols] / total).astype(o_ref.dtype)
        else:
            m_out[...] = m_sc[...]
            l_out[...] = l_sc[...]
            acc_out[...] = acc_sc[...]


def _cost(span, keys, width):
    heads = width // HEAD_DIM
    return pl.CostEstimate(
        flops=8 * span * keys * width,
        transcendentals=span * keys * heads,
        bytes_accessed=2 * keys * width * 2 * (span // TQ) + 16 * span * width,
    )


def local_attention(scalars, q, kv, n_short):
    span, width = q.shape
    heads = width // HEAD_DIM
    nq = span // TQ
    nk = kv.shape[0] // TK

    def kv_block(i, j, s):
        last_short = (s[0] - 1) // TK
        last_new = (i * TQ + TQ - 1) // TK
        return jnp.where(
            j < n_short, jnp.minimum(j, last_short), n_short + jnp.minimum(j - n_short, last_new)
        )

    stat_spec = pl.BlockSpec((heads, TQ, 128), lambda i, j, s: (0, i, 0))
    grid_spec = pltpu.PrefetchScalarGridSpec(
        num_scalar_prefetch=1,
        grid=(nq, nk),
        in_specs=[
            pl.BlockSpec((TQ, width), lambda i, j, s: (i, 0)),
            pl.BlockSpec((TK, width), lambda i, j, s: (kv_block(i, j, s), 0)),
            pl.BlockSpec((TK, width), lambda i, j, s: (kv_block(i, j, s), 1)),
        ],
        out_specs=[stat_spec, stat_spec, pl.BlockSpec((TQ, width), lambda i, j, s: (i, 0))],
        scratch_shapes=[
            pltpu.VMEM((heads, TQ, 128), jnp.float32),
            pltpu.VMEM((heads, TQ, 128), jnp.float32),
            pltpu.VMEM((TQ, width), jnp.float32),
        ],
    )
    return pl.pallas_call(
        functools.partial(_local_kernel, n_short=n_short, nk=nk),
        grid_spec=grid_spec,
        out_shape=[
            jax.ShapeDtypeStruct((heads, span, 128), jnp.float32),
            jax.ShapeDtypeStruct((heads, span, 128), jnp.float32),
            jax.ShapeDtypeStruct((span, width), jnp.float32),
        ],
        compiler_params=pltpu.CompilerParams(dimension_semantics=("arbitrary", "arbitrary")),
        cost_estimate=_cost(span, kv.shape[0], width),
    )(scalars, q, kv, kv)


def long_attention(scalars, q, kv, m, l, acc, finalize):
    span, width = q.shape
    heads = width // HEAD_DIM
    nq = span // TQ
    group = -(-TK // kv.shape[2])
    nk = kv.shape[0] // group
    stat_spec = pl.BlockSpec((heads, TQ, 128), lambda i, j, s: (0, i, 0))
    row_spec = pl.BlockSpec((TQ, width), lambda i, j, s: (i, 0))
    kv_shape = (group, None, kv.shape[2], width)
    if finalize:
        out_specs = row_spec
        out_shape = jax.ShapeDtypeStruct((span, width), jnp.bfloat16)
    else:
        out_specs = [stat_spec, stat_spec, row_spec]
        out_shape = [
            jax.ShapeDtypeStruct((heads, span, 128), jnp.float32),
            jax.ShapeDtypeStruct((heads, span, 128), jnp.float32),
            jax.ShapeDtypeStruct((span, width), jnp.float32),
        ]
    grid_spec = pltpu.PrefetchScalarGridSpec(
        num_scalar_prefetch=1,
        grid=(nq, nk),
        in_specs=[
            row_spec,
            pl.BlockSpec(kv_shape, lambda i, j, s: (j * s[1], 0, 0, 0)),
            pl.BlockSpec(kv_shape, lambda i, j, s: (j * s[1], 1, 0, 0)),
            stat_spec,
            stat_spec,
            row_spec,
        ],
        out_specs=out_specs,
        scratch_shapes=[
            pltpu.VMEM((heads, TQ, 128), jnp.float32),
            pltpu.VMEM((heads, TQ, 128), jnp.float32),
            pltpu.VMEM((TQ, width), jnp.float32),
        ],
    )
    return pl.pallas_call(
        functools.partial(_long_kernel, nk=nk, finalize=finalize),
        grid_spec=grid_spec,
        out_shape=out_shape,
        compiler_params=pltpu.CompilerParams(dimension_semantics=("arbitrary", "arbitrary")),
        cost_estimate=_cost(span, kv.shape[0] * kv.shape[2], width),
    )(scalars, q, kv, kv, m, l, acc)


def solution(mesh):
    n_req = mesh.shape["req"]

    def body(
        hidden_in,
        short_cache,
        long_cache,
        short_len,
        long_owner,
        w_qkv,
        b_qkv,
        w_out,
        b_out,
        w_in,
        b_in,
        w_down,
        b_down,
        norm_gain,
        norm_offset,
    ):
        n_long = long_cache.shape[0]
        long_ids = jnp.arange(n_long, dtype=jnp.int32)

        def which_long(request):
            owned = long_owner == request
            return jnp.sum(jnp.where(owned, long_ids, 0)), jnp.any(owned)

        me = lax.axis_index("req")
        my_long, has_long = which_long(me)
        requests = jnp.arange(n_req, dtype=jnp.int32)
        pick = long_owner[None, :] == requests[:, None]
        dest_long = jnp.sum(jnp.where(pick, long_ids[None, :], 0), axis=1)
        chosen = dest_long[:, None, None, None, None] == long_ids[None, :, None, None, None]
        split = long_cache.shape[1] * 3 // 4

        def send_buffer(lo, hi):
            by_kind = jnp.swapaxes(long_cache[:, lo:hi], 1, 2)[None]
            return jnp.max(jnp.where(chosen, by_kind, jnp.finfo(long_cache.dtype).min), axis=1)

        first_part = lax.all_to_all(send_buffer(0, split), "req", 0, 0, tiled=True)

        n_tp = mesh.shape["tp"]

        def tp_gather(x):
            me_tp = lax.axis_index("tp")
            out = jnp.zeros((n_tp,) + x.shape, x.dtype)
            out = lax.dynamic_update_index_in_dim(out, x, me_tp, 0)
            for shift in range(1, n_tp):
                got = lax.ppermute(x, "tp", [(k, (k + shift) % n_tp) for k in range(n_tp)])
                out = lax.dynamic_update_index_in_dim(out, got, (me_tp + n_tp - shift) % n_tp, 0)
            return out


        local_rows = hidden_in[0]
        factors = jnp.array([0.125, 1.0, 1.0], jnp.float32)[None, :, None]
        both = tp_gather(jnp.stack([local_rows, w_out]))
        rows_all = both[:, 0].reshape(-1, local_rows.shape[1])
        w_out_full = both[:, 1].reshape(-1, w_out.shape[1])
        mixed = jnp.einsum(
            "nd,cdk->nck",
            rows_all,
            w_qkv,
            preferred_element_type=jnp.float32,
        )
        projected = ((mixed + b_qkv[None]) * factors).astype(jnp.bfloat16)
        span_len = projected.shape[0]
        queries = projected[:, 0]
        new_kv = projected[None, :, 1:3]
        short_rows = short_cache[0]
        cache_len = short_rows.shape[0]
        local_kv = jnp.concatenate(
            [short_rows.reshape(cache_len, -1), projected[:, 1:3].reshape(span_len, -1)], axis=0
        )
        scalars = jnp.stack([short_len[0], has_long.astype(jnp.int32)])
        m, l, acc = local_attention(scalars, queries, local_kv, cache_len // TK)
        rest, m = lax.optimization_barrier((send_buffer(split, long_cache.shape[1]), m))
        second_part = lax.all_to_all(rest, "req", 0, 0, tiled=True)
        m, l, acc = long_attention(scalars, queries, first_part, m, l, acc, False)
        context = long_attention(scalars, queries, second_part, m, l, acc, True)

        n_y = n_tp // 2
        block = span_len // n_tp
        core = lax.axis_index("tp") % 2
        chip = lax.axis_index("tp") // 2
        by_core = jnp.swapaxes(context.reshape(n_y, 2, block, context.shape[1]), 0, 1)
        outgoing_ctx = jnp.broadcast_to(by_core[None], (n_y,) + by_core.shape).reshape(
            (n_tp, n_y, block, context.shape[1])
        )
        got = lax.all_to_all(outgoing_ctx, "tp", 0, 0, tiled=True)
        class_ctx = jnp.transpose(got, (1, 2, 0, 3)).reshape(n_y * block, -1)
        class_rows = lax.dynamic_index_in_dim(
            rows_all.reshape(n_y, 2, block, rows_all.shape[1]), core, 1, keepdims=False
        ).reshape(n_y * block, -1)
        attended = jnp.dot(class_ctx, w_out_full, preferred_element_type=jnp.float32) + b_out
        class_normed = layer_norm(
            class_rows.astype(jnp.float32) + attended, norm_gain[0], norm_offset[0]
        ).astype(jnp.bfloat16).reshape(n_y, block, -1)
        normed = lax.dynamic_index_in_dim(class_normed, chip, 0, keepdims=False)
        sibling = [(k, k ^ 1) for k in range(n_tp)]
        halves_in = (w_in, lax.ppermute(w_in, "tp", sibling))
        halves_b = (b_in, lax.ppermute(b_in, "tp", sibling))
        halves_down = (w_down, lax.ppermute(w_down, "tp", sibling))

        def ffn_part(rows):
            total = None
            for w_a, b_a, w_b in zip(halves_in, halves_b, halves_down):
                units = jax.nn.gelu(
                    jnp.dot(rows, w_a, preferred_element_type=jnp.float32) + b_a,
                    approximate=False,
                ).astype(jnp.bfloat16)
                part = jnp.dot(units, w_b, preferred_element_type=jnp.float32)
                total = part if total is None else total + part
            return total

        own_rows = normed
        returned = []
        for step in range(1, n_y):
            ahead = [(k, (k + 2 * step) % n_tp) for k in range(n_tp)]
            behind = [(b, a) for a, b in ahead]
            peer_rows = lax.dynamic_index_in_dim(
                class_normed, (chip + n_y - step) % n_y, 0, keepdims=False
            )
            peer_part = ffn_part(peer_rows)
            own_rows, peer_part = lax.optimization_barrier((own_rows, peer_part))
            returned.append(lax.ppermute(peer_part.astype(jnp.bfloat16), "tp", behind))
        mixed = ffn_part(own_rows)
        mixed, returned = lax.optimization_barrier((mixed, returned))
        for part in returned:
            mixed = mixed + part.astype(jnp.float32)
        mixed = mixed + b_down
        hidden_out = layer_norm(
            normed.astype(jnp.float32) + mixed, norm_gain[1], norm_offset[1]
        ).astype(jnp.bfloat16)
        return (hidden_out[None], new_kv)

    return jax.shard_map(
        body,
        mesh=mesh,
        in_specs=(
            P("req", "tp", None),
            P("req", None, None, "tp"),
            P(None, "req", None, "tp"),
            P("req"),
            P(),
            P(None, None, "tp"),
            P(None, "tp"),
            P("tp", None),
            P(),
            P(None, "tp"),
            P("tp"),
            P("tp", None),
            P(),
            P(),
            P(),
        ),
        out_specs=(P("req", "tp", None), P("req", None, None, "tp")),
        check_vma=False,
    )
```

```python
import functools

import jax
import jax.numpy as jnp
from jax import lax
from jax.experimental import pallas as pl
from jax.experimental.pallas import tpu as pltpu
from jax.sharding import PartitionSpec as P

HEAD_DIM = 64
masked_score = -1e30
TQ = 512
TK = 512


def layer_norm(rows_in, gain, shift):
    center = rows_in - jnp.mean(rows_in, axis=-1, keepdims=True)
    spread = jnp.mean(center * center, axis=-1, keepdims=True)
    return center * lax.rsqrt(spread + 1e-05) * gain + shift


def _attend_block(q_ref, k_ref, v_ref, m_sc, l_sc, acc_sc, valid):
    width = q_ref.shape[1]
    col = lax.broadcasted_iota(jnp.int32, (q_ref.shape[0], 128), 1)
    low = col < HEAD_DIM
    for pair in range(width // 128):
        cols = slice(pair * 128, (pair + 1) * 128)
        q2 = q_ref[:, cols]
        k2 = k_ref[..., cols].reshape(-1, 128)
        v2 = v_ref[..., cols].reshape(-1, 128)
        alphas = []
        pvs = []
        for half in range(2):
            h = pair * 2 + half
            qh = jnp.where(low if half == 0 else jnp.logical_not(low), q2, jnp.zeros_like(q2))
            s = lax.dot_general(
                qh, k2, (((1,), (1,)), ((), ())), preferred_element_type=jnp.float32
            )
            if valid is not None:
                s = jnp.where(valid, s, masked_score)
            m_prev = m_sc[h]
            m_new = jnp.maximum(m_prev, jnp.max(s, axis=1, keepdims=True))
            alpha = jnp.exp(m_prev - m_new)
            p = jnp.exp(s - m_new[:, 0:1])
            l_sc[h] = alpha * l_sc[h] + jnp.sum(p, axis=1, keepdims=True)
            m_sc[h] = m_new
            pvs.append(jnp.dot(p.astype(jnp.bfloat16), v2, preferred_element_type=jnp.float32))
            alphas.append(alpha)
        alpha2 = jnp.where(low, alphas[0], alphas[1])
        acc_sc[:, cols] = alpha2 * acc_sc[:, cols] + jnp.where(low, pvs[0], pvs[1])


def _local_kernel(sref, q_ref, k_ref, v_ref, m_out, l_out, acc_out, m_sc, l_sc, acc_sc, *, n_short, nk):
    i = pl.program_id(0)
    j = pl.program_id(1)
    short_len = sref[0]

    @pl.when(j == 0)
    def _():
        m_sc[...] = jnp.full(m_sc.shape, masked_score, jnp.float32)
        l_sc[...] = jnp.zeros(l_sc.shape, jnp.float32)
        acc_sc[...] = jnp.zeros(acc_sc.shape, jnp.float32)

    is_short = j < n_short
    c = j - n_short
    first_row = i * TQ
    full = jnp.where(is_short, (j + 1) * TK <= short_len, c * TK + TK - 1 <= first_row)
    some = jnp.where(is_short, j * TK < short_len, c * TK <= first_row + TQ - 1)

    @pl.when(full)
    def _():
        _attend_block(q_ref, k_ref, v_ref, m_sc, l_sc, acc_sc, None)

    @pl.when(jnp.logical_and(some, jnp.logical_not(full)))
    def _():
        rows = lax.broadcasted_iota(jnp.int32, (TQ, TK), 0) + first_row
        keys = lax.broadcasted_iota(jnp.int32, (TQ, TK), 1)
        bound = jnp.where(is_short, short_len - j * TK, rows - c * TK + 1)
        valid = keys < bound
        _attend_block(q_ref, k_ref, v_ref, m_sc, l_sc, acc_sc, valid)

    @pl.when(j == nk - 1)
    def _():
        m_out[...] = m_sc[...]
        l_out[...] = l_sc[...]
        acc_out[...] = acc_sc[...]


def _long_kernel(sref, q_ref, k_ref, v_ref, m_in, l_in, acc_in, *rest, nk, finalize):
    j = pl.program_id(1)
    if finalize:
        o_ref, m_sc, l_sc, acc_sc = rest
    else:
        m_out, l_out, acc_out, m_sc, l_sc, acc_sc = rest

    @pl.when(j == 0)
    def _():
        m_sc[...] = m_in[...]
        l_sc[...] = l_in[...]
        acc_sc[...] = acc_in[...]

    @pl.when(sref[1] > 0)
    def _():
        _attend_block(q_ref, k_ref, v_ref, m_sc, l_sc, acc_sc, None)

    @pl.when(j == nk - 1)
    def _():
        if finalize:
            width = o_ref.shape[1]
            col = lax.broadcasted_iota(jnp.int32, (TQ, 128), 1)
            for pair in range(width // 128):
                cols = slice(pair * 128, (pair + 1) * 128)
                total = jnp.where(col < HEAD_DIM, l_sc[2 * pair], l_sc[2 * pair + 1])
                o_ref[:, cols] = (acc_sc[:, cols] / total).astype(o_ref.dtype)
        else:
            m_out[...] = m_sc[...]
            l_out[...] = l_sc[...]
            acc_out[...] = acc_sc[...]


def _cost(span, keys, width):
    heads = width // HEAD_DIM
    return pl.CostEstimate(
        flops=8 * span * keys * width,
        transcendentals=span * keys * heads,
        bytes_accessed=2 * keys * width * 2 * (span // TQ) + 16 * span * width,
    )


def local_attention(scalars, q, kv, n_short):
    span, width = q.shape
    heads = width // HEAD_DIM
    nq = span // TQ
    nk = kv.shape[0] // TK

    def kv_block(i, j, s):
        last_short = (s[0] - 1) // TK
        last_new = (i * TQ + TQ - 1) // TK
        return jnp.where(
            j < n_short, jnp.minimum(j, last_short), n_short + jnp.minimum(j - n_short, last_new)
        )

    stat_spec = pl.BlockSpec((heads, TQ, 128), lambda i, j, s: (0, i, 0))
    grid_spec = pltpu.PrefetchScalarGridSpec(
        num_scalar_prefetch=1,
        grid=(nq, nk),
        in_specs=[
            pl.BlockSpec((TQ, width), lambda i, j, s: (i, 0)),
            pl.BlockSpec((TK, width), lambda i, j, s: (kv_block(i, j, s), 0)),
            pl.BlockSpec((TK, width), lambda i, j, s: (kv_block(i, j, s), 1)),
        ],
        out_specs=[stat_spec, stat_spec, pl.BlockSpec((TQ, width), lambda i, j, s: (i, 0))],
        scratch_shapes=[
            pltpu.VMEM((heads, TQ, 128), jnp.float32),
            pltpu.VMEM((heads, TQ, 128), jnp.float32),
            pltpu.VMEM((TQ, width), jnp.float32),
        ],
    )
    return pl.pallas_call(
        functools.partial(_local_kernel, n_short=n_short, nk=nk),
        grid_spec=grid_spec,
        out_shape=[
            jax.ShapeDtypeStruct((heads, span, 128), jnp.float32),
            jax.ShapeDtypeStruct((heads, span, 128), jnp.float32),
            jax.ShapeDtypeStruct((span, width), jnp.float32),
        ],
        compiler_params=pltpu.CompilerParams(dimension_semantics=("arbitrary", "arbitrary")),
        cost_estimate=_cost(span, kv.shape[0], width),
    )(scalars, q, kv, kv)


def long_attention(scalars, q, kv, m, l, acc, finalize):
    span, width = q.shape
    heads = width // HEAD_DIM
    nq = span // TQ
    group = max(g for g in range(1, kv.shape[0] + 1) if kv.shape[0] % g == 0 and g * kv.shape[2] <= 2 * TK)
    nk = kv.shape[0] // group
    stat_spec = pl.BlockSpec((heads, TQ, 128), lambda i, j, s: (0, i, 0))
    row_spec = pl.BlockSpec((TQ, width), lambda i, j, s: (i, 0))
    kv_shape = (group, None, kv.shape[2], width)
    if finalize:
        out_specs = row_spec
        out_shape = jax.ShapeDtypeStruct((span, width), jnp.bfloat16)
    else:
        out_specs = [stat_spec, stat_spec, row_spec]
        out_shape = [
            jax.ShapeDtypeStruct((heads, span, 128), jnp.float32),
            jax.ShapeDtypeStruct((heads, span, 128), jnp.float32),
            jax.ShapeDtypeStruct((span, width), jnp.float32),
        ]
    grid_spec = pltpu.PrefetchScalarGridSpec(
        num_scalar_prefetch=1,
        grid=(nq, nk),
        in_specs=[
            row_spec,
            pl.BlockSpec(kv_shape, lambda i, j, s: (j * s[1], 0, 0, 0)),
            pl.BlockSpec(kv_shape, lambda i, j, s: (j * s[1], 1, 0, 0)),
            stat_spec,
            stat_spec,
            row_spec,
        ],
        out_specs=out_specs,
        scratch_shapes=[
            pltpu.VMEM((heads, TQ, 128), jnp.float32),
            pltpu.VMEM((heads, TQ, 128), jnp.float32),
            pltpu.VMEM((TQ, width), jnp.float32),
        ],
    )
    return pl.pallas_call(
        functools.partial(_long_kernel, nk=nk, finalize=finalize),
        grid_spec=grid_spec,
        out_shape=out_shape,
        compiler_params=pltpu.CompilerParams(dimension_semantics=("arbitrary", "arbitrary")),
        cost_estimate=_cost(span, kv.shape[0] * kv.shape[2], width),
    )(scalars, q, kv, kv, m, l, acc)


def solution(mesh):
    n_req = mesh.shape["req"]

    def body(
        hidden_in,
        short_cache,
        long_cache,
        short_len,
        long_owner,
        w_qkv,
        b_qkv,
        w_out,
        b_out,
        w_in,
        b_in,
        w_down,
        b_down,
        norm_gain,
        norm_offset,
    ):
        n_long = long_cache.shape[0]
        long_ids = jnp.arange(n_long, dtype=jnp.int32)

        def which_long(request):
            owned = long_owner == request
            return jnp.sum(jnp.where(owned, long_ids, 0)), jnp.any(owned)

        me = lax.axis_index("req")
        my_long, has_long = which_long(me)
        requests = jnp.arange(n_req, dtype=jnp.int32)
        pick = long_owner[None, :] == requests[:, None]
        dest_long = jnp.sum(jnp.where(pick, long_ids[None, :], 0), axis=1)
        chosen = dest_long[:, None, None, None, None] == long_ids[None, :, None, None, None]
        split = long_cache.shape[1] * 3 // 4

        def send_buffer(lo, hi):
            by_kind = jnp.swapaxes(long_cache[:, lo:hi], 1, 2)[None]
            return jnp.max(jnp.where(chosen, by_kind, jnp.finfo(long_cache.dtype).min), axis=1)

        first_part = lax.all_to_all(send_buffer(0, split), "req", 0, 0, tiled=True)

        n_tp = mesh.shape["tp"]

        def tp_gather(x):
            me_tp = lax.axis_index("tp")
            out = jnp.zeros((n_tp,) + x.shape, x.dtype)
            out = lax.dynamic_update_index_in_dim(out, x, me_tp, 0)
            for shift in range(1, n_tp):
                got = lax.ppermute(x, "tp", [(k, (k + shift) % n_tp) for k in range(n_tp)])
                out = lax.dynamic_update_index_in_dim(out, got, (me_tp + n_tp - shift) % n_tp, 0)
            return out.reshape((-1,) + x.shape[1:])

        w_out_full = tp_gather(w_out)

        local_rows = hidden_in[0]
        factors = jnp.array([0.125, 1.0, 1.0], jnp.float32)[None, :, None]
        rows_all = tp_gather(local_rows)
        mixed = jnp.einsum(
            "nd,cdk->nck",
            rows_all,
            w_qkv,
            preferred_element_type=jnp.float32,
        )
        projected = ((mixed + b_qkv[None]) * factors).astype(jnp.bfloat16)
        span_len = projected.shape[0]
        queries = projected[:, 0]
        new_kv = projected[None, :, 1:3]
        short_rows = short_cache[0]
        cache_len = short_rows.shape[0]
        local_kv = jnp.concatenate(
            [short_rows.reshape(cache_len, -1), projected[:, 1:3].reshape(span_len, -1)], axis=0
        )
        scalars = jnp.stack([short_len[0], has_long.astype(jnp.int32)])
        m, l, acc = local_attention(scalars, queries, local_kv, cache_len // TK)
        rest, m = lax.optimization_barrier((send_buffer(split, long_cache.shape[1]), m))
        second_part = lax.all_to_all(rest, "req", 0, 0, tiled=True)
        m, l, acc = long_attention(scalars, queries, first_part, m, l, acc, False)
        context = long_attention(scalars, queries, second_part, m, l, acc, True)

        n_y = n_tp // 2
        block = span_len // n_tp
        core = lax.axis_index("tp") % 2
        chip = lax.axis_index("tp") // 2
        by_core = jnp.swapaxes(context.reshape(n_y, 2, block, context.shape[1]), 0, 1)
        outgoing_ctx = jnp.broadcast_to(by_core[None], (n_y,) + by_core.shape).reshape(
            (n_tp, n_y, block, context.shape[1])
        )
        got = lax.all_to_all(outgoing_ctx, "tp", 0, 0, tiled=True)
        class_ctx = jnp.transpose(got, (1, 2, 0, 3)).reshape(n_y * block, -1)
        class_rows = lax.dynamic_index_in_dim(
            rows_all.reshape(n_y, 2, block, rows_all.shape[1]), core, 1, keepdims=False
        ).reshape(n_y * block, -1)
        attended = jnp.dot(class_ctx, w_out_full, preferred_element_type=jnp.float32) + b_out
        class_normed = layer_norm(
            class_rows.astype(jnp.float32) + attended, norm_gain[0], norm_offset[0]
        ).astype(jnp.bfloat16).reshape(n_y, block, -1)
        normed = lax.dynamic_index_in_dim(class_normed, chip, 0, keepdims=False)
        sibling = [(k, k ^ 1) for k in range(n_tp)]
        halves_in = (w_in, lax.ppermute(w_in, "tp", sibling))
        halves_b = (b_in, lax.ppermute(b_in, "tp", sibling))
        halves_down = (w_down, lax.ppermute(w_down, "tp", sibling))

        def ffn_part(rows):
            total = None
            for w_a, b_a, w_b in zip(halves_in, halves_b, halves_down):
                units = jax.nn.gelu(
                    jnp.dot(rows, w_a, preferred_element_type=jnp.float32) + b_a,
                    approximate=False,
                ).astype(jnp.bfloat16)
                part = jnp.dot(units, w_b, preferred_element_type=jnp.float32)
                total = part if total is None else total + part
            return total

        own_rows = normed
        returned = []
        for step in range(1, n_y):
            ahead = [(k, (k + 2 * step) % n_tp) for k in range(n_tp)]
            behind = [(b, a) for a, b in ahead]
            peer_rows = lax.dynamic_index_in_dim(
                class_normed, (chip + n_y - step) % n_y, 0, keepdims=False
            )
            peer_part = ffn_part(peer_rows)
            own_rows, peer_part = lax.optimization_barrier((own_rows, peer_part))
            returned.append(lax.ppermute(peer_part.astype(jnp.bfloat16), "tp", behind))
        mixed = ffn_part(own_rows)
        mixed, returned = lax.optimization_barrier((mixed, returned))
        for part in returned:
            mixed = mixed + part.astype(jnp.float32)
        mixed = mixed + b_down
        hidden_out = layer_norm(
            normed.astype(jnp.float32) + mixed, norm_gain[1], norm_offset[1]
        ).astype(jnp.bfloat16)
        return (hidden_out[None], new_kv)

    return jax.shard_map(
        body,
        mesh=mesh,
        in_specs=(
            P("req", "tp", None),
            P("req", None, None, "tp"),
            P(None, "req", None, "tp"),
            P("req"),
            P(),
            P(None, None, "tp"),
            P(None, "tp"),
            P("tp", None),
            P(),
            P(None, "tp"),
            P("tp"),
            P("tp", None),
            P(),
            P(),
            P(),
        ),
        out_specs=(P("req", "tp", None), P("req", None, None, "tp")),
        check_vma=False,
    )
```

```python
import functools

import jax
import jax.numpy as jnp
from jax import lax
from jax.experimental import pallas as pl
from jax.experimental.pallas import tpu as pltpu
from jax.sharding import PartitionSpec as P

HEAD_DIM = 64
masked_score = -1e30
TQ = 512
TK = 512


def layer_norm(rows_in, gain, shift):
    center = rows_in - jnp.mean(rows_in, axis=-1, keepdims=True)
    spread = jnp.mean(center * center, axis=-1, keepdims=True)
    return center * lax.rsqrt(spread + 1e-05) * gain + shift


def _attend_block(q_ref, k_ref, v_ref, m_sc, l_sc, acc_sc, valid):
    width = q_ref.shape[1]
    col = lax.broadcasted_iota(jnp.int32, (q_ref.shape[0], 128), 1)
    low = col < HEAD_DIM
    for pair in range(width // 128):
        cols = slice(pair * 128, (pair + 1) * 128)
        q2 = q_ref[:, cols]
        k2 = k_ref[..., cols].reshape(-1, 128)
        v2 = v_ref[..., cols].reshape(-1, 128)
        alphas = []
        pvs = []
        for half in range(2):
            h = pair * 2 + half
            qh = jnp.where(low if half == 0 else jnp.logical_not(low), q2, jnp.zeros_like(q2))
            s = lax.dot_general(
                qh, k2, (((1,), (1,)), ((), ())), preferred_element_type=jnp.float32
            )
            if valid is not None:
                s = jnp.where(valid, s, masked_score)
            m_prev = m_sc[h]
            m_new = jnp.maximum(m_prev, jnp.max(s, axis=1, keepdims=True))
            alpha = jnp.exp(m_prev - m_new)
            p = jnp.exp(s - m_new[:, 0:1])
            l_sc[h] = alpha * l_sc[h] + jnp.sum(p, axis=1, keepdims=True)
            m_sc[h] = m_new
            pvs.append(jnp.dot(p.astype(jnp.bfloat16), v2, preferred_element_type=jnp.float32))
            alphas.append(alpha)
        alpha2 = jnp.where(low, alphas[0], alphas[1])
        acc_sc[:, cols] = alpha2 * acc_sc[:, cols] + jnp.where(low, pvs[0], pvs[1])


def _local_kernel(sref, q_ref, k_ref, v_ref, m_out, l_out, acc_out, m_sc, l_sc, acc_sc, *, n_short, nk):
    i = pl.program_id(0)
    j = pl.program_id(1)
    short_len = sref[0]

    @pl.when(j == 0)
    def _():
        m_sc[...] = jnp.full(m_sc.shape, masked_score, jnp.float32)
        l_sc[...] = jnp.zeros(l_sc.shape, jnp.float32)
        acc_sc[...] = jnp.zeros(acc_sc.shape, jnp.float32)

    is_short = j < n_short
    c = j - n_short
    first_row = i * TQ
    full = jnp.where(is_short, (j + 1) * TK <= short_len, c * TK + TK - 1 <= first_row)
    some = jnp.where(is_short, j * TK < short_len, c * TK <= first_row + TQ - 1)

    @pl.when(full)
    def _():
        _attend_block(q_ref, k_ref, v_ref, m_sc, l_sc, acc_sc, None)

    @pl.when(jnp.logical_and(some, jnp.logical_not(full)))
    def _():
        rows = lax.broadcasted_iota(jnp.int32, (TQ, TK), 0) + first_row
        keys = lax.broadcasted_iota(jnp.int32, (TQ, TK), 1)
        bound = jnp.where(is_short, short_len - j * TK, rows - c * TK + 1)
        valid = keys < bound
        _attend_block(q_ref, k_ref, v_ref, m_sc, l_sc, acc_sc, valid)

    @pl.when(j == nk - 1)
    def _():
        m_out[...] = m_sc[...]
        l_out[...] = l_sc[...]
        acc_out[...] = acc_sc[...]


def _long_kernel(sref, q_ref, k_ref, v_ref, m_in, l_in, acc_in, *rest, nk, finalize):
    j = pl.program_id(1)
    if finalize:
        o_ref, m_sc, l_sc, acc_sc = rest
    else:
        m_out, l_out, acc_out, m_sc, l_sc, acc_sc = rest

    @pl.when(j == 0)
    def _():
        m_sc[...] = m_in[...]
        l_sc[...] = l_in[...]
        acc_sc[...] = acc_in[...]

    @pl.when(sref[1] > 0)
    def _():
        _attend_block(q_ref, k_ref, v_ref, m_sc, l_sc, acc_sc, None)

    @pl.when(j == nk - 1)
    def _():
        if finalize:
            width = o_ref.shape[1]
            col = lax.broadcasted_iota(jnp.int32, (o_ref.shape[0], 128), 1)
            for pair in range(width // 128):
                cols = slice(pair * 128, (pair + 1) * 128)
                total = jnp.where(col < HEAD_DIM, l_sc[2 * pair], l_sc[2 * pair + 1])
                o_ref[:, cols] = (acc_sc[:, cols] / total).astype(o_ref.dtype)
        else:
            m_out[...] = m_sc[...]
            l_out[...] = l_sc[...]
            acc_out[...] = acc_sc[...]


def _cost(span, keys, width):
    heads = width // HEAD_DIM
    return pl.CostEstimate(
        flops=8 * span * keys * width,
        transcendentals=span * keys * heads,
        bytes_accessed=2 * keys * width * 2 * (span // TQ) + 16 * span * width,
    )


def local_attention(scalars, q, kv, n_short):
    span, width = q.shape
    heads = width // HEAD_DIM
    nq = span // TQ
    nk = kv.shape[0] // TK

    def kv_block(i, j, s):
        last_short = (s[0] - 1) // TK
        last_new = (i * TQ + TQ - 1) // TK
        return jnp.where(
            j < n_short, jnp.minimum(j, last_short), n_short + jnp.minimum(j - n_short, last_new)
        )

    stat_spec = pl.BlockSpec((heads, TQ, 128), lambda i, j, s: (0, i, 0))
    grid_spec = pltpu.PrefetchScalarGridSpec(
        num_scalar_prefetch=1,
        grid=(nq, nk),
        in_specs=[
            pl.BlockSpec((TQ, width), lambda i, j, s: (i, 0)),
            pl.BlockSpec((TK, width), lambda i, j, s: (kv_block(i, j, s), 0)),
            pl.BlockSpec((TK, width), lambda i, j, s: (kv_block(i, j, s), 1)),
        ],
        out_specs=[stat_spec, stat_spec, pl.BlockSpec((TQ, width), lambda i, j, s: (i, 0))],
        scratch_shapes=[
            pltpu.VMEM((heads, TQ, 128), jnp.float32),
            pltpu.VMEM((heads, TQ, 128), jnp.float32),
            pltpu.VMEM((TQ, width), jnp.float32),
        ],
    )
    return pl.pallas_call(
        functools.partial(_local_kernel, n_short=n_short, nk=nk),
        grid_spec=grid_spec,
        out_shape=[
            jax.ShapeDtypeStruct((heads, span, 128), jnp.float32),
            jax.ShapeDtypeStruct((heads, span, 128), jnp.float32),
            jax.ShapeDtypeStruct((span, width), jnp.float32),
        ],
        compiler_params=pltpu.CompilerParams(dimension_semantics=("arbitrary", "arbitrary")),
        cost_estimate=_cost(span, kv.shape[0], width),
    )(scalars, q, kv, kv)


def long_attention(scalars, q, kv, m, l, acc, finalize):
    span, width = q.shape
    heads = width // HEAD_DIM
    tq = span
    nq = span // tq
    group = max(g for g in range(1, kv.shape[0] + 1) if kv.shape[0] % g == 0 and g * kv.shape[2] <= 2 * TK)
    nk = kv.shape[0] // group
    stat_spec = pl.BlockSpec((heads, tq, 128), lambda i, j, s: (0, i, 0))
    row_spec = pl.BlockSpec((tq, width), lambda i, j, s: (i, 0))
    kv_shape = (group, None, kv.shape[2], width)
    if finalize:
        out_specs = row_spec
        out_shape = jax.ShapeDtypeStruct((span, width), jnp.bfloat16)
    else:
        out_specs = [stat_spec, stat_spec, row_spec]
        out_shape = [
            jax.ShapeDtypeStruct((heads, span, 128), jnp.float32),
            jax.ShapeDtypeStruct((heads, span, 128), jnp.float32),
            jax.ShapeDtypeStruct((span, width), jnp.float32),
        ]
    grid_spec = pltpu.PrefetchScalarGridSpec(
        num_scalar_prefetch=1,
        grid=(nq, nk),
        in_specs=[
            row_spec,
            pl.BlockSpec(kv_shape, lambda i, j, s: (j * s[1], 0, 0, 0)),
            pl.BlockSpec(kv_shape, lambda i, j, s: (j * s[1], 1, 0, 0)),
            stat_spec,
            stat_spec,
            row_spec,
        ],
        out_specs=out_specs,
        scratch_shapes=[
            pltpu.VMEM((heads, tq, 128), jnp.float32),
            pltpu.VMEM((heads, tq, 128), jnp.float32),
            pltpu.VMEM((tq, width), jnp.float32),
        ],
    )
    return pl.pallas_call(
        functools.partial(_long_kernel, nk=nk, finalize=finalize),
        grid_spec=grid_spec,
        out_shape=out_shape,
        compiler_params=pltpu.CompilerParams(dimension_semantics=("arbitrary", "arbitrary")),
        cost_estimate=_cost(span, kv.shape[0] * kv.shape[2], width),
    )(scalars, q, kv, kv, m, l, acc)


def solution(mesh):
    n_req = mesh.shape["req"]

    def body(
        hidden_in,
        short_cache,
        long_cache,
        short_len,
        long_owner,
        w_qkv,
        b_qkv,
        w_out,
        b_out,
        w_in,
        b_in,
        w_down,
        b_down,
        norm_gain,
        norm_offset,
    ):
        n_long = long_cache.shape[0]
        long_ids = jnp.arange(n_long, dtype=jnp.int32)

        def which_long(request):
            owned = long_owner == request
            return jnp.sum(jnp.where(owned, long_ids, 0)), jnp.any(owned)

        me = lax.axis_index("req")
        my_long, has_long = which_long(me)
        requests = jnp.arange(n_req, dtype=jnp.int32)
        pick = long_owner[None, :] == requests[:, None]
        dest_long = jnp.sum(jnp.where(pick, long_ids[None, :], 0), axis=1)
        chosen = dest_long[:, None, None, None, None] == long_ids[None, :, None, None, None]
        split = long_cache.shape[1] * 3 // 4

        def send_buffer(lo, hi):
            by_kind = jnp.swapaxes(long_cache[:, lo:hi], 1, 2)[None]
            return jnp.max(jnp.where(chosen, by_kind, jnp.finfo(long_cache.dtype).min), axis=1)

        first_part = lax.all_to_all(send_buffer(0, split), "req", 0, 0, tiled=True)

        n_tp = mesh.shape["tp"]

        def tp_gather(x):
            me_tp = lax.axis_index("tp")
            out = jnp.zeros((n_tp,) + x.shape, x.dtype)
            out = lax.dynamic_update_index_in_dim(out, x, me_tp, 0)
            for shift in range(1, n_tp):
                got = lax.ppermute(x, "tp", [(k, (k + shift) % n_tp) for k in range(n_tp)])
                out = lax.dynamic_update_index_in_dim(out, got, (me_tp + n_tp - shift) % n_tp, 0)
            return out.reshape((-1,) + x.shape[1:])

        w_out_full = tp_gather(w_out)

        local_rows = hidden_in[0]
        factors = jnp.array([0.125, 1.0, 1.0], jnp.float32)[None, :, None]
        rows_all = tp_gather(local_rows)
        mixed = jnp.einsum(
            "nd,cdk->nck",
            rows_all,
            w_qkv,
            preferred_element_type=jnp.float32,
        )
        projected = ((mixed + b_qkv[None]) * factors).astype(jnp.bfloat16)
        span_len = projected.shape[0]
        queries = projected[:, 0]
        new_kv = projected[None, :, 1:3]
        short_rows = short_cache[0]
        cache_len = short_rows.shape[0]
        local_kv = jnp.concatenate(
            [short_rows.reshape(cache_len, -1), projected[:, 1:3].reshape(span_len, -1)], axis=0
        )
        scalars = jnp.stack([short_len[0], has_long.astype(jnp.int32)])
        m, l, acc = local_attention(scalars, queries, local_kv, cache_len // TK)
        rest, m = lax.optimization_barrier((send_buffer(split, long_cache.shape[1]), m))
        second_part = lax.all_to_all(rest, "req", 0, 0, tiled=True)
        m, l, acc = long_attention(scalars, queries, first_part, m, l, acc, False)
        context = long_attention(scalars, queries, second_part, m, l, acc, True)

        n_y = n_tp // 2
        block = span_len // n_tp
        core = lax.axis_index("tp") % 2
        chip = lax.axis_index("tp") // 2
        by_core = jnp.swapaxes(context.reshape(n_y, 2, block, context.shape[1]), 0, 1)
        outgoing_ctx = jnp.broadcast_to(by_core[None], (n_y,) + by_core.shape).reshape(
            (n_tp, n_y, block, context.shape[1])
        )
        got = lax.all_to_all(outgoing_ctx, "tp", 0, 0, tiled=True)
        class_ctx = jnp.transpose(got, (1, 2, 0, 3)).reshape(n_y * block, -1)
        class_rows = lax.dynamic_index_in_dim(
            rows_all.reshape(n_y, 2, block, rows_all.shape[1]), core, 1, keepdims=False
        ).reshape(n_y * block, -1)
        attended = jnp.dot(class_ctx, w_out_full, preferred_element_type=jnp.float32) + b_out
        class_normed = layer_norm(
            class_rows.astype(jnp.float32) + attended, norm_gain[0], norm_offset[0]
        ).astype(jnp.bfloat16).reshape(n_y, block, -1)
        normed = lax.dynamic_index_in_dim(class_normed, chip, 0, keepdims=False)
        sibling = [(k, k ^ 1) for k in range(n_tp)]
        halves_in = (w_in, lax.ppermute(w_in, "tp", sibling))
        halves_b = (b_in, lax.ppermute(b_in, "tp", sibling))
        halves_down = (w_down, lax.ppermute(w_down, "tp", sibling))

        def ffn_part(rows):
            total = None
            for w_a, b_a, w_b in zip(halves_in, halves_b, halves_down):
                units = jax.nn.gelu(
                    jnp.dot(rows, w_a, preferred_element_type=jnp.float32) + b_a,
                    approximate=False,
                ).astype(jnp.bfloat16)
                part = jnp.dot(units, w_b, preferred_element_type=jnp.float32)
                total = part if total is None else total + part
            return total

        own_rows = normed
        returned = []
        for step in range(1, n_y):
            ahead = [(k, (k + 2 * step) % n_tp) for k in range(n_tp)]
            behind = [(b, a) for a, b in ahead]
            peer_rows = lax.dynamic_index_in_dim(
                class_normed, (chip + n_y - step) % n_y, 0, keepdims=False
            )
            peer_part = ffn_part(peer_rows)
            own_rows, peer_part = lax.optimization_barrier((own_rows, peer_part))
            returned.append(lax.ppermute(peer_part.astype(jnp.bfloat16), "tp", behind))
        mixed = ffn_part(own_rows)
        mixed, returned = lax.optimization_barrier((mixed, returned))
        for part in returned:
            mixed = mixed + part.astype(jnp.float32)
        mixed = mixed + b_down
        hidden_out = layer_norm(
            normed.astype(jnp.float32) + mixed, norm_gain[1], norm_offset[1]
        ).astype(jnp.bfloat16)
        return (hidden_out[None], new_kv)

    return jax.shard_map(
        body,
        mesh=mesh,
        in_specs=(
            P("req", "tp", None),
            P("req", None, None, "tp"),
            P(None, "req", None, "tp"),
            P("req"),
            P(),
            P(None, None, "tp"),
            P(None, "tp"),
            P("tp", None),
            P(),
            P(None, "tp"),
            P("tp"),
            P("tp", None),
            P(),
            P(),
            P(),
        ),
        out_specs=(P("req", "tp", None), P("req", None, None, "tp")),
        check_vma=False,
    )
```

```python
import functools

import jax
import jax.numpy as jnp
from jax import lax
from jax.experimental import pallas as pl
from jax.experimental.pallas import tpu as pltpu
from jax.sharding import PartitionSpec as P

HEAD_DIM = 64
masked_score = -1e30
TQ = 512
TK = 512


def layer_norm(rows_in, gain, shift):
    center = rows_in - jnp.mean(rows_in, axis=-1, keepdims=True)
    spread = jnp.mean(center * center, axis=-1, keepdims=True)
    return center * lax.rsqrt(spread + 1e-05) * gain + shift


def _attend_block(q_ref, k_ref, v_ref, m_sc, l_sc, acc_sc, valid):
    width = q_ref.shape[1]
    col = lax.broadcasted_iota(jnp.int32, (q_ref.shape[0], 128), 1)
    low = col < HEAD_DIM
    for pair in range(width // 128):
        cols = slice(pair * 128, (pair + 1) * 128)
        q2 = q_ref[:, cols]
        k2 = k_ref[..., cols].reshape(-1, 128)
        v2 = v_ref[..., cols].reshape(-1, 128)
        alphas = []
        pvs = []
        for half in range(2):
            h = pair * 2 + half
            qh = jnp.where(low if half == 0 else jnp.logical_not(low), q2, jnp.zeros_like(q2))
            s = lax.dot_general(
                qh, k2, (((1,), (1,)), ((), ())), preferred_element_type=jnp.float32
            )
            if valid is not None:
                s = jnp.where(valid, s, masked_score)
            m_prev = m_sc[h]
            m_new = jnp.maximum(m_prev, jnp.max(s, axis=1, keepdims=True))
            alpha = jnp.exp(m_prev - m_new)
            p = jnp.exp(s - m_new[:, 0:1])
            l_sc[h] = alpha * l_sc[h] + jnp.sum(p, axis=1, keepdims=True)
            m_sc[h] = m_new
            pvs.append(jnp.dot(p.astype(jnp.bfloat16), v2, preferred_element_type=jnp.float32))
            alphas.append(alpha)
        alpha2 = jnp.where(low, alphas[0], alphas[1])
        acc_sc[:, cols] = alpha2 * acc_sc[:, cols] + jnp.where(low, pvs[0], pvs[1])


def _local_kernel(sref, q_ref, k_ref, v_ref, m_out, l_out, acc_out, m_sc, l_sc, acc_sc, *, n_short, nk):
    i = pl.program_id(0)
    j = pl.program_id(1)
    short_len = sref[0]

    @pl.when(j == 0)
    def _():
        m_sc[...] = jnp.full(m_sc.shape, masked_score, jnp.float32)
        l_sc[...] = jnp.zeros(l_sc.shape, jnp.float32)
        acc_sc[...] = jnp.zeros(acc_sc.shape, jnp.float32)

    is_short = j < n_short
    c = j - n_short
    first_row = i * TQ
    full = jnp.where(is_short, (j + 1) * TK <= short_len, c * TK + TK - 1 <= first_row)
    some = jnp.where(is_short, j * TK < short_len, c * TK <= first_row + TQ - 1)

    @pl.when(full)
    def _():
        _attend_block(q_ref, k_ref, v_ref, m_sc, l_sc, acc_sc, None)

    @pl.when(jnp.logical_and(some, jnp.logical_not(full)))
    def _():
        rows = lax.broadcasted_iota(jnp.int32, (TQ, TK), 0) + first_row
        keys = lax.broadcasted_iota(jnp.int32, (TQ, TK), 1)
        bound = jnp.where(is_short, short_len - j * TK, rows - c * TK + 1)
        valid = keys < bound
        _attend_block(q_ref, k_ref, v_ref, m_sc, l_sc, acc_sc, valid)

    @pl.when(j == nk - 1)
    def _():
        m_out[...] = m_sc[...]
        l_out[...] = l_sc[...]
        acc_out[...] = acc_sc[...]


def _long_kernel(sref, q_ref, k_ref, v_ref, m_in, l_in, acc_in, *rest, nk, finalize):
    j = pl.program_id(1)
    if finalize:
        o_ref, m_sc, l_sc, acc_sc = rest
    else:
        m_out, l_out, acc_out, m_sc, l_sc, acc_sc = rest

    @pl.when(j == 0)
    def _():
        m_sc[...] = m_in[...]
        l_sc[...] = l_in[...]
        acc_sc[...] = acc_in[...]

    @pl.when(sref[1] > 0)
    def _():
        _attend_block(q_ref, k_ref, v_ref, m_sc, l_sc, acc_sc, None)

    @pl.when(j == nk - 1)
    def _():
        if finalize:
            width = o_ref.shape[1]
            col = lax.broadcasted_iota(jnp.int32, (TQ, 128), 1)
            for pair in range(width // 128):
                cols = slice(pair * 128, (pair + 1) * 128)
                total = jnp.where(col < HEAD_DIM, l_sc[2 * pair], l_sc[2 * pair + 1])
                o_ref[:, cols] = (acc_sc[:, cols] / total).astype(o_ref.dtype)
        else:
            m_out[...] = m_sc[...]
            l_out[...] = l_sc[...]
            acc_out[...] = acc_sc[...]


def _cost(span, keys, width):
    heads = width // HEAD_DIM
    return pl.CostEstimate(
        flops=8 * span * keys * width,
        transcendentals=span * keys * heads,
        bytes_accessed=2 * keys * width * 2 * (span // TQ) + 16 * span * width,
    )


def local_attention(scalars, q, kv, n_short):
    span, width = q.shape
    heads = width // HEAD_DIM
    nq = span // TQ
    nk = kv.shape[0] // TK

    def kv_block(i, j, s):
        last_short = (s[0] - 1) // TK
        last_new = (i * TQ + TQ - 1) // TK
        return jnp.where(
            j < n_short, jnp.minimum(j, last_short), n_short + jnp.minimum(j - n_short, last_new)
        )

    stat_spec = pl.BlockSpec((heads, TQ, 128), lambda i, j, s: (0, i, 0))
    grid_spec = pltpu.PrefetchScalarGridSpec(
        num_scalar_prefetch=1,
        grid=(nq, nk),
        in_specs=[
            pl.BlockSpec((TQ, width), lambda i, j, s: (i, 0)),
            pl.BlockSpec((TK, width), lambda i, j, s: (kv_block(i, j, s), 0)),
            pl.BlockSpec((TK, width), lambda i, j, s: (kv_block(i, j, s), 1)),
        ],
        out_specs=[stat_spec, stat_spec, pl.BlockSpec((TQ, width), lambda i, j, s: (i, 0))],
        scratch_shapes=[
            pltpu.VMEM((heads, TQ, 128), jnp.float32),
            pltpu.VMEM((heads, TQ, 128), jnp.float32),
            pltpu.VMEM((TQ, width), jnp.float32),
        ],
    )
    return pl.pallas_call(
        functools.partial(_local_kernel, n_short=n_short, nk=nk),
        grid_spec=grid_spec,
        out_shape=[
            jax.ShapeDtypeStruct((heads, span, 128), jnp.float32),
            jax.ShapeDtypeStruct((heads, span, 128), jnp.float32),
            jax.ShapeDtypeStruct((span, width), jnp.float32),
        ],
        compiler_params=pltpu.CompilerParams(dimension_semantics=("arbitrary", "arbitrary")),
        cost_estimate=_cost(span, kv.shape[0], width),
    )(scalars, q, kv, kv)


def long_attention(scalars, q, kv, m, l, acc, finalize):
    span, width = q.shape
    heads = width // HEAD_DIM
    nq = span // TQ
    group = max(g for g in range(1, kv.shape[0] + 1) if kv.shape[0] % g == 0 and g * kv.shape[2] <= 2 * TK)
    nk = kv.shape[0] // group
    stat_spec = pl.BlockSpec((heads, TQ, 128), lambda i, j, s: (0, i, 0))
    row_spec = pl.BlockSpec((TQ, width), lambda i, j, s: (i, 0))
    kv_shape = (group, None, kv.shape[2], width)
    if finalize:
        out_specs = row_spec
        out_shape = jax.ShapeDtypeStruct((span, width), jnp.bfloat16)
    else:
        out_specs = [stat_spec, stat_spec, row_spec]
        out_shape = [
            jax.ShapeDtypeStruct((heads, span, 128), jnp.float32),
            jax.ShapeDtypeStruct((heads, span, 128), jnp.float32),
            jax.ShapeDtypeStruct((span, width), jnp.float32),
        ]
    grid_spec = pltpu.PrefetchScalarGridSpec(
        num_scalar_prefetch=1,
        grid=(nq, nk),
        in_specs=[
            row_spec,
            pl.BlockSpec(kv_shape, lambda i, j, s: (j * s[1], 0, 0, 0)),
            pl.BlockSpec(kv_shape, lambda i, j, s: (j * s[1], 1, 0, 0)),
            stat_spec,
            stat_spec,
            row_spec,
        ],
        out_specs=out_specs,
        scratch_shapes=[
            pltpu.VMEM((heads, TQ, 128), jnp.float32),
            pltpu.VMEM((heads, TQ, 128), jnp.float32),
            pltpu.VMEM((TQ, width), jnp.float32),
        ],
    )
    return pl.pallas_call(
        functools.partial(_long_kernel, nk=nk, finalize=finalize),
        grid_spec=grid_spec,
        out_shape=out_shape,
        compiler_params=pltpu.CompilerParams(dimension_semantics=("arbitrary", "arbitrary")),
        cost_estimate=_cost(span, kv.shape[0] * kv.shape[2], width),
    )(scalars, q, kv, kv, m, l, acc)


def solution(mesh):
    n_req = mesh.shape["req"]

    def body(
        hidden_in,
        short_cache,
        long_cache,
        short_len,
        long_owner,
        w_qkv,
        b_qkv,
        w_out,
        b_out,
        w_in,
        b_in,
        w_down,
        b_down,
        norm_gain,
        norm_offset,
    ):
        n_long = long_cache.shape[0]
        long_ids = jnp.arange(n_long, dtype=jnp.int32)

        def which_long(request):
            owned = long_owner == request
            return jnp.sum(jnp.where(owned, long_ids, 0)), jnp.any(owned)

        me = lax.axis_index("req")
        my_long, has_long = which_long(me)
        requests = jnp.arange(n_req, dtype=jnp.int32)
        pick = long_owner[None, :] == requests[:, None]
        dest_long = jnp.sum(jnp.where(pick, long_ids[None, :], 0), axis=1)
        chosen = dest_long[:, None, None, None, None] == long_ids[None, :, None, None, None]
        split = long_cache.shape[1] * 3 // 4

        def send_buffer(lo, hi):
            by_kind = jnp.swapaxes(long_cache[:, lo:hi], 1, 2)[None]
            return jnp.max(jnp.where(chosen, by_kind, jnp.finfo(long_cache.dtype).min), axis=1)

        first_part = lax.all_to_all(send_buffer(0, split), "req", 0, 0, tiled=True)

        n_tp = mesh.shape["tp"]

        def tp_gather(x):
            me_tp = lax.axis_index("tp")
            out = jnp.zeros((n_tp,) + x.shape, x.dtype)
            out = lax.dynamic_update_index_in_dim(out, x, me_tp, 0)
            for shift in range(1, n_tp):
                got = lax.ppermute(x, "tp", [(k, (k + shift) % n_tp) for k in range(n_tp)])
                out = lax.dynamic_update_index_in_dim(out, got, (me_tp + n_tp - shift) % n_tp, 0)
            return out.reshape((-1,) + x.shape[1:])


        local_rows = hidden_in[0]
        factors = jnp.array([0.125, 1.0, 1.0], jnp.float32)[None, :, None]
        rows_all = tp_gather(local_rows)
        mixed = jnp.einsum(
            "nd,cdk->nck",
            rows_all,
            w_qkv,
            preferred_element_type=jnp.float32,
        )
        projected = ((mixed + b_qkv[None]) * factors).astype(jnp.bfloat16)
        span_len = projected.shape[0]
        queries = projected[:, 0]
        new_kv = projected[None, :, 1:3]
        short_rows = short_cache[0]
        cache_len = short_rows.shape[0]
        local_kv = jnp.concatenate(
            [short_rows.reshape(cache_len, -1), projected[:, 1:3].reshape(span_len, -1)], axis=0
        )
        scalars = jnp.stack([short_len[0], has_long.astype(jnp.int32)])
        m, l, acc = local_attention(scalars, queries, local_kv, cache_len // TK)
        rest, m = lax.optimization_barrier((send_buffer(split, long_cache.shape[1]), m))
        second_part = lax.all_to_all(rest, "req", 0, 0, tiled=True)
        m, l, acc = long_attention(scalars, queries, first_part, m, l, acc, False)
        context = long_attention(scalars, queries, second_part, m, l, acc, True)
        w_out_now, context = lax.optimization_barrier((w_out, context))
        w_out_full = tp_gather(w_out_now)

        n_y = n_tp // 2
        block = span_len // n_tp
        core = lax.axis_index("tp") % 2
        chip = lax.axis_index("tp") // 2
        by_core = jnp.swapaxes(context.reshape(n_y, 2, block, context.shape[1]), 0, 1)
        outgoing_ctx = jnp.broadcast_to(by_core[None], (n_y,) + by_core.shape).reshape(
            (n_tp, n_y, block, context.shape[1])
        )
        got = lax.all_to_all(outgoing_ctx, "tp", 0, 0, tiled=True)
        class_ctx = jnp.transpose(got, (1, 2, 0, 3)).reshape(n_y * block, -1)
        class_rows = lax.dynamic_index_in_dim(
            rows_all.reshape(n_y, 2, block, rows_all.shape[1]), core, 1, keepdims=False
        ).reshape(n_y * block, -1)
        attended = jnp.dot(class_ctx, w_out_full, preferred_element_type=jnp.float32) + b_out
        class_normed = layer_norm(
            class_rows.astype(jnp.float32) + attended, norm_gain[0], norm_offset[0]
        ).astype(jnp.bfloat16).reshape(n_y, block, -1)
        normed = lax.dynamic_index_in_dim(class_normed, chip, 0, keepdims=False)
        sibling = [(k, k ^ 1) for k in range(n_tp)]
        halves_in = (w_in, lax.ppermute(w_in, "tp", sibling))
        halves_b = (b_in, lax.ppermute(b_in, "tp", sibling))
        halves_down = (w_down, lax.ppermute(w_down, "tp", sibling))

        def ffn_part(rows):
            total = None
            for w_a, b_a, w_b in zip(halves_in, halves_b, halves_down):
                units = jax.nn.gelu(
                    jnp.dot(rows, w_a, preferred_element_type=jnp.float32) + b_a,
                    approximate=False,
                ).astype(jnp.bfloat16)
                part = jnp.dot(units, w_b, preferred_element_type=jnp.float32)
                total = part if total is None else total + part
            return total

        own_rows = normed
        returned = []
        for step in range(1, n_y):
            ahead = [(k, (k + 2 * step) % n_tp) for k in range(n_tp)]
            behind = [(b, a) for a, b in ahead]
            peer_rows = lax.dynamic_index_in_dim(
                class_normed, (chip + n_y - step) % n_y, 0, keepdims=False
            )
            peer_part = ffn_part(peer_rows)
            own_rows, peer_part = lax.optimization_barrier((own_rows, peer_part))
            returned.append(lax.ppermute(peer_part.astype(jnp.bfloat16), "tp", behind))
        mixed = ffn_part(own_rows)
        mixed, returned = lax.optimization_barrier((mixed, returned))
        for part in returned:
            mixed = mixed + part.astype(jnp.float32)
        mixed = mixed + b_down
        hidden_out = layer_norm(
            normed.astype(jnp.float32) + mixed, norm_gain[1], norm_offset[1]
        ).astype(jnp.bfloat16)
        return (hidden_out[None], new_kv)

    return jax.shard_map(
        body,
        mesh=mesh,
        in_specs=(
            P("req", "tp", None),
            P("req", None, None, "tp"),
            P(None, "req", None, "tp"),
            P("req"),
            P(),
            P(None, None, "tp"),
            P(None, "tp"),
            P("tp", None),
            P(),
            P(None, "tp"),
            P("tp"),
            P("tp", None),
            P(),
            P(),
            P(),
        ),
        out_specs=(P("req", "tp", None), P("req", None, None, "tp")),
        check_vma=False,
    )
```
